32 devices in a mesh: gx: 4 (over x, core), gy: 4 (over z), gz: 2 (over y).
Axes of the slice: x: 2, y: 2, z: 4, core: 2. Of those that a mesh axis runs over, the one named last changes fastest.
Arguments:
- adjoint: float32 [5, 128, 64, 256], P(None, 'gx', 'gy', 'gz'), may hold values from -6 to 6
- stencil_weights: float32 [3, 2, 3, 5, 128, 64, 256], P(None, None, None, None, 'gx', 'gy', 'gz'), as said below
- flux_plus: float32 [3, 5, 5], replicated, may hold values from -1.5 to 1.5
- flux_minus: float32 [3, 5, 5], replicated, may hold values from -1.5 to 1.5
- wall_row: int32 [512], P(('gx', 'gy', 'gz')), may hold values from 0 to 511
- wall_panel: int32 [512, 128], P(('gx', 'gy', 'gz')), may hold values from 0 to 1023
- wall_coef: float32 [5, 512, 128], P(None, ('gx', 'gy', 'gz')), may hold values from -1.2 to 1.2
- wall_count: int32 [32], P(('gx', 'gy', 'gz')), may hold values from 1 to 16, 256 in all
- panel_owner: int32 [1024], replicated, may hold values from 0 to 31, as said below
Outputs:
- section_adjoint: float32 [5, 128, 64, 256], P(None, 'gx', 'gy', 'gz')
- panel_sens: float32 [1024], P(('gx', 'gy', 'gz'))
The draws below stay inside these ranges and needn't reach their ends.
Inputs may be any that keep to these rules, and one draw needn't show every extreme that they name: `stencil_weights`: Positive; the three candidate weights of one direction, side, field and cell sum to one up to rounding. `panel_owner`: each device index owns exactly 32 panels.
All inputs are finite; a program needn't handle non-finite values. No bound on the sum of `wall_count` on one device may be relied on, other than what follows from the above.
Results may differ from the reference program's by a relative error of at most 0.00012.
Values sent between devices are 32-bit elements; how exact they have to be, the bound alone decides.
No kernel may reach another device: no remote copies, remote signals or barrier semaphores. Data moves between devices by JAX's collectives and lax.ppermute only.
A program may use at most 128 MiB of HBM per device.

```python
import math
import jax
import jax.numpy as jnp
import numpy as np
from jax import lax

FIELDS = 5
CX = 32
CY = 16
CZ = 128
WR_DEV = 16
PANEL_DEV = 32
NX = 128
NY = 64
NZ = 256
WALLS = 512
PANELS = 1024
N_GY = 4
N_GZ = 2
DEVICES = 32


def draw_stencil_weights(key, part):
    shape = (3, 2, 3, FIELDS, NX, NY, NZ)
    raw = jnp.exp(jax.random.uniform(key, shape, jnp.float32, -3.0, 0.0))
    return raw / jnp.sum(raw, axis=2, keepdims=True)


def draw_wall_panel(key, part):
    return jax.random.randint(jax.random.fold_in(key, 12), (WALLS, CZ), 0, PANELS).astype(jnp.int32)


def draw_panel_owner(key, part):
    return (jax.random.permutation(jax.random.fold_in(key, 21), PANELS) // PANEL_DEV).astype(jnp.int32)


def with_ends(array, own_key, low, largest):
    place = [jax.random.randint(jax.random.fold_in(own_key, axis), (), 0, length) for axis, length in enumerate(array.shape)]
    main_axis = array.shape.index(max(array.shape))
    neighbour = place[:main_axis] + [(place[main_axis] + 1) % array.shape[main_axis]] + place[main_axis + 1:]
    return array.at[tuple(place)].set(low).at[tuple(neighbour)].set(largest)


def steps_of(rng, dims, cuts, smallest, largest):
    factor_of = 1.0
    for position, parts in cuts:
        draws = jax.random.uniform(jax.random.fold_in(jax.random.fold_in(rng, 6), position), (parts,), jnp.float32, smallest / len(cuts), largest / len(cuts))
        factor_of = factor_of * jnp.repeat(jnp.exp(draws), dims[position] // parts).reshape((-1,) + (1,) * (len(dims) - 1 - position))
    return factor_of


def length_profile(count, total, limit, skew):
    weights = [(1 << 20) // math.isqrt(grade ** skew) + 1 for grade in range(2, count + 1)]
    rest, given = total - limit - (count - 1), [1] * (count - 1)
    while rest > 0:
        movable = [i for i in range(count - 1) if given[i] < limit]
        mass, remaining = sum([weights[i] for i in movable]), rest
        for i in movable:
            addition = min(limit - given[i], max(1, remaining * weights[i] // mass), rest)
            given[i] = given[i] + addition
            rest = rest - addition
    return np.array([limit] + given)


def uneven_parts(own_key, count, total, reach, slope):
    if count == 2:
        one = jax.random.randint(own_key, (), max(1, total - reach), min(reach, total - 1) + 1)
        return jnp.stack([one, total - one])
    tallies = jnp.asarray(length_profile(count, total, reach, slope), jnp.int32)
    twos = (count - 1) // 2
    donor, receiver = tallies[1:1 + 2 * twos:2], tallies[2:2 + 2 * twos:2]
    room = jnp.minimum(donor - 1, reach - receiver)
    passed = jax.random.randint(jax.random.fold_in(own_key, 1), (twos,), 0, 1 << 20) % (room + 1)
    tallies = tallies.at[1:1 + 2 * twos:2].set(donor - passed).at[2:2 + 2 * twos:2].set(receiver + passed)
    return tallies[jax.random.permutation(jax.random.fold_in(own_key, 2), count)]


def normal_values(own_key, shape, width, reach, pieces=(), held_as=jnp.bfloat16):
    array = width * jax.random.normal(own_key, shape, jnp.float32)
    if pieces:
        array = array * steps_of(own_key, shape, pieces, -0.22, 0.18)
    return jnp.clip(array, -reach, reach).astype(held_as)


def setup_inputs(seed: int = 0) -> dict:
    keys = jax.random.split(jax.random.key(seed), 10)
    return {
        "adjoint": normal_values(keys[0], (FIELDS, NX, NY, NZ), 1.0, 6.0, ((1, 4), (2, 4), (3, 2)), jnp.float32),
        "stencil_weights": draw_stencil_weights(jax.random.fold_in(keys[9], 71), 0),
        "flux_plus": normal_values(keys[2], (3, FIELDS, FIELDS), 0.3, 1.5, (), jnp.float32),
        "flux_minus": normal_values(keys[3], (3, FIELDS, FIELDS), 0.3, 1.5, (), jnp.float32),
        "wall_row": with_ends(jax.random.randint(keys[4], (WALLS,), 0, CX * CY), jax.random.fold_in(keys[4], 1), 0, (CX * CY) - 1).astype(jnp.int32),
        "wall_panel": draw_wall_panel(jax.random.fold_in(keys[9], 71), 0),
        "wall_coef": normal_values(keys[6], (FIELDS, WALLS, CZ), 0.2, 1.2, ((1, 32),), jnp.float32),
        "wall_count": uneven_parts(keys[7], DEVICES, WR_DEV * DEVICES // 2, WR_DEV, 2).astype(jnp.int32),
        "panel_owner": draw_panel_owner(jax.random.fold_in(keys[9], 71), 0),
    }


step_ratio = 0.4
section_weight = 0.25
left_table = ((1.0 / 3.0, -7.0 / 6.0, 11.0 / 6.0, 0.0, 0.0, 0.0), (0.0, -1.0 / 6.0, 5.0 / 6.0, 1.0 / 3.0, 0.0, 0.0), (0.0, 0.0, 1.0 / 3.0, 5.0 / 6.0, -1.0 / 6.0, 0.0))
right_table = ((0.0, 0.0, 0.0, 11.0 / 6.0, -7.0 / 6.0, 1.0 / 3.0), (0.0, 0.0, 1.0 / 3.0, 5.0 / 6.0, -1.0 / 6.0, 0.0), (0.0, -1.0 / 6.0, 5.0 / 6.0, 1.0 / 3.0, 0.0, 0.0))


def combine_weights(weight_set, table, offset):
    result = None
    for stencil in range(3):
        factor = table[stencil][offset]
        if factor != 0.0:
            piece = weight_set[stencil] * factor
            result = piece if result is None else result + piece
    return result


def face_terms(adjoint_now, adjoint_next, weights_dir, plus_matrix, minus_matrix):
    face_grad = (adjoint_next - adjoint_now) * step_ratio
    plus_part = jnp.einsum("gf,gxyz->fxyz", plus_matrix, face_grad, precision=lax.Precision.HIGHEST)
    minus_part = jnp.einsum("gf,gxyz->fxyz", minus_matrix, face_grad, precision=lax.Precision.HIGHEST)
    offset_terms = []
    for offset in range(6):
        left_coef = combine_weights(weights_dir[0], left_table, offset)
        right_coef = combine_weights(weights_dir[1], right_table, offset)
        term = None
        if left_coef is not None:
            term = plus_part * left_coef
        if right_coef is not None:
            side = minus_part * right_coef
            term = side if term is None else term + side
        offset_terms.append(term)
    return offset_terms


def reference(adjoint, stencil_weights, flux_plus, flux_minus, wall_row, wall_panel, wall_coef, wall_count, panel_owner):
    total = jnp.zeros(adjoint.shape, jnp.float32)
    for direction in range(3):
        spatial_axis = direction + 1
        following = jnp.roll(adjoint, -1, spatial_axis)
        offset_terms = face_terms(adjoint, following, stencil_weights[direction], flux_plus[direction], flux_minus[direction])
        for offset in range(6):
            total = total + jnp.roll(offset_terms[offset], offset - 2, spatial_axis)
    section_adjoint = section_weight * (adjoint + total)
    row_ids = jnp.arange(WALLS, dtype=jnp.int32)
    device = row_ids // WR_DEV
    live = ((row_ids % WR_DEV) < wall_count[device]).astype(jnp.float32)
    x_index = (device // (N_GY * N_GZ)) * CX + wall_row // CY
    y_index = ((device // N_GZ) % N_GY) * CY + wall_row % CY
    z_index = (device % N_GZ)[:, None] * CZ + jnp.arange(CZ, dtype=jnp.int32)[None, :]
    gathered = section_adjoint[:, x_index[:, None], y_index[:, None], z_index]
    wall_terms = jnp.sum(gathered * wall_coef, axis=0) * live[:, None]
    panel_totals = jax.ops.segment_sum(wall_terms.reshape(-1), wall_panel.reshape(-1), num_segments=PANELS)
    order = jnp.argsort(panel_owner, stable=True)
    return section_adjoint, panel_totals[order]
```

```python
import jax
import jax.numpy as jnp
from jax import lax
from jax.experimental import pallas as pl
from jax.experimental.pallas import tpu as pltpu
from jax.sharding import PartitionSpec as P

AXES = ("gx", "gy", "gz")
STEP = 0.4
SECTION = 0.25
XC = 4
F32 = jnp.float32
HI = lax.Precision.HIGHEST
VMEM = pl.BlockSpec(memory_space=pltpu.VMEM)
SMEM = pl.BlockSpec(memory_space=pltpu.SMEM)


def shift_from(x, axis, by):
    n = lax.axis_size(axis)
    return lax.ppermute(x, axis, [(i, (i + by) % n) for i in range(n)])


def iotas(ny, nz):
    return (
        lax.broadcasted_iota(jnp.int32, (ny, nz), 0),
        lax.broadcasted_iota(jnp.int32, (ny, nz), 1),
    )


def fronts_kernel(adj_ref, xf_ref, yf_ref, zf_ref):
    nf, nx, ny, nz = adj_ref.shape
    row, lane = iotas(ny, nz)
    for f in range(nf):
        xf_ref[f] = adj_ref[f, 0]
        zacc = jnp.zeros((ny, nz), F32)
        for x in range(nx):
            s = adj_ref[f, x]
            yf_ref[f, pl.ds(x, 1), :] = s[0:1, :]
            zacc = zacc + pltpu.roll(jnp.where(lane == 0, s, 0.0), x, 1)
        zf_ref[f] = zacc


def offset_terms(plus, minus, w):
    p0, p1, p2 = plus * w(0, 0), plus * w(0, 1), plus * w(0, 2)
    m0, m1, m2 = minus * w(1, 0), minus * w(1, 1), minus * w(1, 2)
    a = p1 + m2
    b = p2 + m1
    return [
        p0 * (1.0 / 3.0),
        p0 * (-7.0 / 6.0) + a * (-1.0 / 6.0),
        p0 * (11.0 / 6.0) + a * (5.0 / 6.0) + b * (1.0 / 3.0),
        a * (1.0 / 3.0) + b * (5.0 / 6.0) + m0 * (11.0 / 6.0),
        b * (-1.0 / 6.0) + m0 * (-7.0 / 6.0),
        m0 * (1.0 / 3.0),
    ]


def split_wrap(terms, idx, n, axis):
    inner = terms[2]
    wrap = None
    for o in (0, 1, 3, 4, 5):
        s = o - 2
        r = pltpu.roll(terms[o], s % n, axis)
        valid = (idx >= s) if s > 0 else (idx < n + s)
        inner = inner + jnp.where(valid, r, 0.0)
        piece = jnp.where(valid, 0.0, r)
        wrap = piece if wrap is None else wrap + piece
    return inner, wrap


def stencil_kernel(fp_ref, fm_ref, adj_ref, xf_ref, yf_ref, zf_ref, w_ref,
                   sec_ref, xl_ref, xr_ref, yl_ref, yr_ref, zl_ref, zr_ref, acc_ref):
    nf, nx, ny, nz = adj_ref.shape
    i = pl.program_id(0)
    row, lane = iotas(ny, nz)

    @pl.when(i == 0)
    def _():
        acc_ref[...] = jnp.zeros_like(acc_ref)
        zl_ref[...] = jnp.zeros_like(zl_ref)
        zr_ref[...] = jnp.zeros_like(zr_ref)

    def flux(d, diff):
        plus, minus = [], []
        for f in range(nf):
            p = m = None
            for g in range(nf):
                k = (d * nf + g) * nf + f
                tp = diff[g] * fp_ref[k]
                tm = diff[g] * fm_ref[k]
                p = tp if p is None else p + tp
                m = tm if m is None else m + tm
            plus.append(p)
            minus.append(m)
        return plus, minus

    yr_parts = {}
    yl_parts = {}
    for xl in range(XC):
        x = i * XC + xl
        a = [adj_ref[f, x] for f in range(nf)]
        last = x == nx - 1
        nxt = jnp.minimum(x + 1, nx - 1)
        an_x = [jnp.where(last, xf_ref[f], adj_ref[f, nxt]) for f in range(nf)]
        an_y = [
            jnp.where(row == ny - 1, yf_ref[f, pl.ds(x, 1), :], pltpu.roll(a[f], ny - 1, 0))
            for f in range(nf)
        ]
        zshift = nz - 1 - x
        an_z = [
            jnp.where(lane == nz - 1, pltpu.roll(zf_ref[f], zshift, 1), pltpu.roll(a[f], nz - 1, 1))
            for f in range(nf)
        ]
        fx = flux(0, [an_x[g] - a[g] for g in range(nf)])
        fy = flux(1, [an_y[g] - a[g] for g in range(nf)])
        fz = flux(2, [an_z[g] - a[g] for g in range(nf)])
        for f in range(nf):
            sx = offset_terms(fx[0][f], fx[1][f], lambda s, k: w_ref[0, s, k, f, xl])
            sy = offset_terms(fy[0][f], fy[1][f], lambda s, k: w_ref[1, s, k, f, xl])
            sz = offset_terms(fz[0][f], fz[1][f], lambda s, k: w_ref[2, s, k, f, xl])
            iy, wy = split_wrap(sy, row, ny, 0)
            iz, wz = split_wrap(sz, lane, nz, 1)
            for o in range(6):
                val = sx[o] if o != 2 else sx[2] + iy + iz
                acc_ref[f, x + o] = acc_ref[f, x + o] + val
            rear = pltpu.roll(jnp.where(row < 3, wy, 0.0), 4 * (xl % 2), 0)[0:8]
            lead = pltpu.roll(jnp.where(row >= ny - 2, wy, 0.0), 2 + 2 * (xl % 4), 0)[0:8]
            kr = (f, xl // 2)
            kl = (f, xl // 4)
            yr_parts[kr] = rear if kr not in yr_parts else yr_parts[kr] + rear
            yl_parts[kl] = lead if kl not in yl_parts else yl_parts[kl] + lead
            zr_ref[f] = zr_ref[f] + pltpu.roll(jnp.where(lane < 3, wz, 0.0), 4 * x, 1)
            zl_ref[f] = zl_ref[f] + pltpu.roll(jnp.where(lane >= nz - 2, wz, 0.0), 2 + 4 * x, 1)
    for (f, t), v in yr_parts.items():
        yr_ref[f, t] = v
    for (f, t), v in yl_parts.items():
        yl_ref[f, t] = v

    @pl.when(i == pl.num_programs(0) - 1)
    def _():
        def body(x, c):
            for f in range(nf):
                sec_ref[f, x] = SECTION * (adj_ref[f, x] + acc_ref[f, x + 2])
            return c

        lax.fori_loop(0, nx, body, 0)
        for f in range(nf):
            xl_ref[f] = acc_ref[f, 0:2]
            xr_ref[f] = acc_ref[f, nx + 2:nx + 5]


def fix_kernel(row_ref, cnt_ref, sec_ref, axl_ref, axr_ref, ayl_ref, ayr_ref, azl_ref, azr_ref,
               coef_ref, out_ref, wt_ref):
    nf, nx, ny, nz = sec_ref.shape
    row, lane = iotas(ny, nz)
    pad = jnp.zeros((ny - 8, nz), F32)
    for x in range(nx):
        for f in range(nf):
            ty = jnp.concatenate([ayr_ref[f, x // 2], pad], 0)
            add = jnp.where(row < 3, pltpu.roll(ty, (ny - 4 * (x % 2)) % ny, 0), 0.0)
            ty = jnp.concatenate([ayl_ref[f, x // 4], pad], 0)
            add = add + jnp.where(row >= ny - 2, pltpu.roll(ty, (ny - 2 - 2 * (x % 4)) % ny, 0), 0.0)
            add = add + jnp.where(lane < 3, pltpu.roll(azr_ref[f], (nz - 4 * x) % nz, 1), 0.0)
            add = add + jnp.where(lane >= nz - 2, pltpu.roll(azl_ref[f], (nz - 2 - 4 * x) % nz, 1), 0.0)
            if x < 3:
                add = add + axr_ref[f, x]
            if x >= nx - 2:
                add = add + axl_ref[f, x - (nx - 2)]
            out_ref[f, x] = sec_ref[f, x] + SECTION * add
    live_n = cnt_ref[0]
    for r in range(wt_ref.shape[0]):
        idx = row_ref[r]
        lx = idx // ny
        ly = idx % ny
        val = None
        for f in range(nf):
            v = out_ref[f, lx, pl.ds(ly, 1), :] * coef_ref[f, pl.ds(r, 1), :]
            val = v if val is None else val + v
        wt_ref[pl.ds(r, 1), :] = val * jnp.where(r < live_n, 1.0, 0.0).astype(F32)


def on_device(ndev, adjoint, stencil_weights, flux_plus, flux_minus, wall_row, wall_panel, wall_coef,
              wall_count, panel_owner):
    nf, nx, ny, nz = adjoint.shape
    assert nx % XC == 0 and XC % 4 == 0 and ny == 16 and nx * 4 <= nz
    xf, yf, zf = pl.pallas_call(
        fronts_kernel,
        out_shape=(
            jax.ShapeDtypeStruct((nf, ny, nz), F32),
            jax.ShapeDtypeStruct((nf, nx, nz), F32),
            jax.ShapeDtypeStruct((nf, ny, nz), F32),
        ),
        in_specs=[VMEM],
        out_specs=(VMEM, VMEM, VMEM),
    )(adjoint)
    xf = shift_from(xf, "gx", -1)
    yf = shift_from(yf, "gy", -1)
    zf = shift_from(zf, "gz", -1)
    fp = (STEP * flux_plus).reshape(-1)
    fm = (STEP * flux_minus).reshape(-1)
    const4 = lambda i: (0, 0, 0, 0)
    const3 = lambda i: (0, 0, 0)
    sec, xl, xr, yl, yr, zl, zr = pl.pallas_call(
        stencil_kernel,
        grid=(nx // XC,),
        out_shape=(
            jax.ShapeDtypeStruct((nf, nx, ny, nz), F32),
            jax.ShapeDtypeStruct((nf, 2, ny, nz), F32),
            jax.ShapeDtypeStruct((nf, 3, ny, nz), F32),
            jax.ShapeDtypeStruct((nf, nx // 4, 8, nz), F32),
            jax.ShapeDtypeStruct((nf, nx // 2, 8, nz), F32),
            jax.ShapeDtypeStruct((nf, ny, nz), F32),
            jax.ShapeDtypeStruct((nf, ny, nz), F32),
        ),
        in_specs=[
            SMEM,
            SMEM,
            pl.BlockSpec((nf, nx, ny, nz), const4),
            pl.BlockSpec((nf, ny, nz), const3),
            pl.BlockSpec((nf, nx, nz), const3),
            pl.BlockSpec((nf, ny, nz), const3),
            pl.BlockSpec((3, 2, 3, nf, XC, ny, nz), lambda i: (0, 0, 0, 0, i, 0, 0)),
        ],
        out_specs=(
            pl.BlockSpec((nf, nx, ny, nz), const4),
            pl.BlockSpec((nf, 2, ny, nz), const4),
            pl.BlockSpec((nf, 3, ny, nz), const4),
            pl.BlockSpec((nf, XC // 4, 8, nz), lambda i: (0, i, 0, 0)),
            pl.BlockSpec((nf, XC // 2, 8, nz), lambda i: (0, i, 0, 0)),
            pl.BlockSpec((nf, ny, nz), const3),
            pl.BlockSpec((nf, ny, nz), const3),
        ),
        scratch_shapes=[pltpu.VMEM((nf, nx + 5, ny, nz), F32)],
        compiler_params=pltpu.CompilerParams(dimension_semantics=("arbitrary",)),
    )(fp, fm, adjoint, xf, yf, zf, stencil_weights)
    axl = shift_from(xl, "gx", -1)
    axr = shift_from(xr, "gx", 1)
    ayl = shift_from(yl, "gy", -1)
    ayr = shift_from(yr, "gy", 1)
    azl = shift_from(zl, "gz", -1)
    azr = shift_from(zr, "gz", 1)
    nr = wall_row.shape[0]
    section, wt = pl.pallas_call(
        fix_kernel,
        out_shape=(
            jax.ShapeDtypeStruct((nf, nx, ny, nz), F32),
            jax.ShapeDtypeStruct((nr, nz), F32),
        ),
        in_specs=[SMEM, SMEM] + [VMEM] * 8,
        out_specs=(VMEM, VMEM),
        input_output_aliases={2: 0},
    )(wall_row, wall_count, sec, axl, axr, ayl, ayr, azl, azr, wall_coef)

    npan = panel_owner.shape[0]
    per = npan // ndev
    nb = 32
    na = npan // nb
    pa = wall_panel // nb
    pb = wall_panel % nb
    oh_a = (pa[..., None] == jnp.arange(na, dtype=jnp.int32)).astype(F32) * wt[..., None]
    oh_b = (pb[..., None] == jnp.arange(nb, dtype=jnp.int32)).astype(F32)
    tp = jnp.einsum("rza,rzb->ab", oh_a, oh_b, precision=HI).reshape(npan)
    own_oh = (panel_owner[:, None] == jnp.arange(ndev, dtype=jnp.int32)).astype(F32)
    rank = jnp.sum(jnp.cumsum(own_oh, axis=0) * own_oh, axis=1) - 1.0
    rank_oh = (rank[:, None] == jnp.arange(per, dtype=F32)).astype(F32)
    t = jnp.einsum("po,pk->ok", own_oh * tp[:, None], rank_oh, precision=HI)
    got = lax.all_to_all(t, AXES, 0, 0, tiled=True)
    return section, jnp.sum(got, axis=0)


def solution(mesh):
    ndev = mesh.size
    placed = (
        P(None, "gx", "gy", "gz"),
        P(None, None, None, None, "gx", "gy", "gz"),
        P(),
        P(),
        P(AXES),
        P(AXES, None),
        P(None, AXES, None),
        P(AXES),
        P(),
    )
    return jax.shard_map(
        lambda *args: on_device(ndev, *args),
        mesh=mesh,
        in_specs=placed,
        out_specs=(P(None, "gx", "gy", "gz"), P(AXES)),
        check_vma=False,
    )
```

```python
import jax
import jax.numpy as jnp
from jax import lax
from jax.experimental import pallas as pl
from jax.experimental.pallas import tpu as pltpu
from jax.sharding import PartitionSpec as P

AXES = ("gx", "gy", "gz")
STEP = 0.4
SECTION = 0.25
XC = 4
F32 = jnp.float32
HI = lax.Precision.HIGHEST
VMEM = pl.BlockSpec(memory_space=pltpu.VMEM)
SMEM = pl.BlockSpec(memory_space=pltpu.SMEM)


def shift_from(x, axis, by):
    n = lax.axis_size(axis)
    return lax.ppermute(x, axis, [(i, (i + by) % n) for i in range(n)])


def iotas(ny, nz):
    return (
        lax.broadcasted_iota(jnp.int32, (ny, nz), 0),
        lax.broadcasted_iota(jnp.int32, (ny, nz), 1),
    )


def fronts_kernel(adj_ref, xf_ref, yf_ref, zf_ref):
    nf, nx, ny, nz = adj_ref.shape
    row, lane = iotas(ny, nz)
    for f in range(nf):
        xf_ref[f] = adj_ref[f, 0]
        zacc = jnp.zeros((ny, nz), F32)
        for x in range(nx):
            s = adj_ref[f, x]
            yf_ref[f, pl.ds(x, 1), :] = s[0:1, :]
            zacc = zacc + pltpu.roll(jnp.where(lane == 0, s, 0.0), x, 1)
        zf_ref[f] = zacc


def offset_terms(plus, minus, w):
    p0, p1, p2 = plus * w(0, 0), plus * w(0, 1), plus * w(0, 2)
    m0, m1, m2 = minus * w(1, 0), minus * w(1, 1), minus * w(1, 2)
    a = p1 + m2
    b = p2 + m1
    return [
        p0 * (1.0 / 3.0),
        p0 * (-7.0 / 6.0) + a * (-1.0 / 6.0),
        p0 * (11.0 / 6.0) + a * (5.0 / 6.0) + b * (1.0 / 3.0),
        a * (1.0 / 3.0) + b * (5.0 / 6.0) + m0 * (11.0 / 6.0),
        b * (-1.0 / 6.0) + m0 * (-7.0 / 6.0),
        m0 * (1.0 / 3.0),
    ]


def split_wrap(terms, idx, n, axis):
    inner = terms[2]
    wrap = None
    for o in (0, 1, 3, 4, 5):
        s = o - 2
        r = pltpu.roll(terms[o], s % n, axis)
        valid = (idx >= s) if s > 0 else (idx < n + s)
        inner = inner + jnp.where(valid, r, 0.0)
        piece = jnp.where(valid, 0.0, r)
        wrap = piece if wrap is None else wrap + piece
    return inner, wrap


def stencil_kernel(fp_ref, fm_ref, adj_ref, xf_ref, yf_ref, zf_ref, w_ref,
                   sec_ref, xl_ref, xr_ref, yl_ref, yr_ref, zl_ref, zr_ref, acc_ref):
    nf, nx, ny, nz = adj_ref.shape
    i = pl.program_id(0)
    row, lane = iotas(ny, nz)

    @pl.when(i == 0)
    def _():
        acc_ref[...] = jnp.zeros_like(acc_ref)
        zl_ref[...] = jnp.zeros_like(zl_ref)
        zr_ref[...] = jnp.zeros_like(zr_ref)

    def flux(d, diff):
        plus, minus = [], []
        for f in range(nf):
            p = m = None
            for g in range(nf):
                tp = diff[g] * (STEP * fp_ref[d, g, f])
                tm = diff[g] * (STEP * fm_ref[d, g, f])
                p = tp if p is None else p + tp
                m = tm if m is None else m + tm
            plus.append(p)
            minus.append(m)
        return plus, minus

    yr_parts = {}
    yl_parts = {}
    for xl in range(XC):
        x = i * XC + xl
        a = [adj_ref[f, x] for f in range(nf)]
        last = x == nx - 1
        nxt = jnp.minimum(x + 1, nx - 1)
        an_x = [jnp.where(last, xf_ref[f], adj_ref[f, nxt]) for f in range(nf)]
        an_y = [
            jnp.where(row == ny - 1, yf_ref[f, pl.ds(x, 1), :], pltpu.roll(a[f], ny - 1, 0))
            for f in range(nf)
        ]
        zshift = nz - 1 - x
        an_z = [
            jnp.where(lane == nz - 1, pltpu.roll(zf_ref[f], zshift, 1), pltpu.roll(a[f], nz - 1, 1))
            for f in range(nf)
        ]
        fx = flux(0, [an_x[g] - a[g] for g in range(nf)])
        fy = flux(1, [an_y[g] - a[g] for g in range(nf)])
        fz = flux(2, [an_z[g] - a[g] for g in range(nf)])
        for f in range(nf):
            sx = offset_terms(fx[0][f], fx[1][f], lambda s, k: w_ref[0, s, k, f, xl])
            sy = offset_terms(fy[0][f], fy[1][f], lambda s, k: w_ref[1, s, k, f, xl])
            sz = offset_terms(fz[0][f], fz[1][f], lambda s, k: w_ref[2, s, k, f, xl])
            iy, wy = split_wrap(sy, row, ny, 0)
            iz, wz = split_wrap(sz, lane, nz, 1)
            for o in range(6):
                val = sx[o] if o != 2 else sx[2] + iy + iz
                acc_ref[f, x + o] = acc_ref[f, x + o] + val
            rear = pltpu.roll(jnp.where(row < 3, wy, 0.0), 4 * (xl % 2), 0)[0:8]
            lead = pltpu.roll(jnp.where(row >= ny - 2, wy, 0.0), 2 + 2 * (xl % 4), 0)[0:8]
            kr = (f, xl // 2)
            kl = (f, xl // 4)
            yr_parts[kr] = rear if kr not in yr_parts else yr_parts[kr] + rear
            yl_parts[kl] = lead if kl not in yl_parts else yl_parts[kl] + lead
            zr_ref[f] = zr_ref[f] + pltpu.roll(jnp.where(lane < 3, wz, 0.0), 4 * x, 1)
            zl_ref[f] = zl_ref[f] + pltpu.roll(jnp.where(lane >= nz - 2, wz, 0.0), 2 + 4 * x, 1)
    for (f, t), v in yr_parts.items():
        yr_ref[f, t] = v
    for (f, t), v in yl_parts.items():
        yl_ref[f, t] = v

    @pl.when(i == pl.num_programs(0) - 1)
    def _():
        def body(x, c):
            for f in range(nf):
                sec_ref[f, x] = SECTION * (adj_ref[f, x] + acc_ref[f, x + 2])
            return c

        lax.fori_loop(0, nx, body, 0)
        for f in range(nf):
            xl_ref[f] = acc_ref[f, 0:2]
            xr_ref[f] = acc_ref[f, nx + 2:nx + 5]


def fix_kernel(row_ref, cnt_ref, sec_ref, axl_ref, axr_ref, ayl_ref, ayr_ref, azl_ref, azr_ref,
               coef_ref, out_ref, wt_ref):
    nf, nx, ny, nz = sec_ref.shape
    row, lane = iotas(ny, nz)
    pad = jnp.zeros((ny - 8, nz), F32)
    for x in range(nx):
        for f in range(nf):
            ty = jnp.concatenate([ayr_ref[f, x // 2], pad], 0)
            add = jnp.where(row < 3, pltpu.roll(ty, (ny - 4 * (x % 2)) % ny, 0), 0.0)
            ty = jnp.concatenate([ayl_ref[f, x // 4], pad], 0)
            add = add + jnp.where(row >= ny - 2, pltpu.roll(ty, (ny - 2 - 2 * (x % 4)) % ny, 0), 0.0)
            add = add + jnp.where(lane < 3, pltpu.roll(azr_ref[f], (nz - 4 * x) % nz, 1), 0.0)
            add = add + jnp.where(lane >= nz - 2, pltpu.roll(azl_ref[f], (nz - 2 - 4 * x) % nz, 1), 0.0)
            if x < 3:
                add = add + axr_ref[f, x]
            if x >= nx - 2:
                add = add + axl_ref[f, x - (nx - 2)]
            out_ref[f, x] = sec_ref[f, x] + SECTION * add
    live_n = cnt_ref[0]
    for r in range(wt_ref.shape[0]):
        idx = row_ref[r]
        lx = idx // ny
        ly = idx % ny
        val = None
        for f in range(nf):
            v = out_ref[f, lx, pl.ds(ly, 1), :] * coef_ref[f, pl.ds(r, 1), :]
            val = v if val is None else val + v
        wt_ref[pl.ds(r, 1), :] = val * jnp.where(r < live_n, 1.0, 0.0).astype(F32)


def on_device(ndev, adjoint, stencil_weights, flux_plus, flux_minus, wall_row, wall_panel, wall_coef,
              wall_count, panel_owner):
    nf, nx, ny, nz = adjoint.shape
    assert nx % XC == 0 and XC % 4 == 0 and ny == 16 and nx * 4 <= nz
    xf, yf, zf = pl.pallas_call(
        fronts_kernel,
        out_shape=(
            jax.ShapeDtypeStruct((nf, ny, nz), F32),
            jax.ShapeDtypeStruct((nf, nx, nz), F32),
            jax.ShapeDtypeStruct((nf, ny, nz), F32),
        ),
        in_specs=[VMEM],
        out_specs=(VMEM, VMEM, VMEM),
    )(adjoint)
    xf = shift_from(xf, "gx", -1)
    yf = shift_from(yf, "gy", -1)
    zf = shift_from(zf, "gz", -1)
    const4 = lambda i: (0, 0, 0, 0)
    const3 = lambda i: (0, 0, 0)
    sec, xl, xr, yl, yr, zl, zr = pl.pallas_call(
        stencil_kernel,
        grid=(nx // XC,),
        out_shape=(
            jax.ShapeDtypeStruct((nf, nx, ny, nz), F32),
            jax.ShapeDtypeStruct((nf, 2, ny, nz), F32),
            jax.ShapeDtypeStruct((nf, 3, ny, nz), F32),
            jax.ShapeDtypeStruct((nf, nx // 4, 8, nz), F32),
            jax.ShapeDtypeStruct((nf, nx // 2, 8, nz), F32),
            jax.ShapeDtypeStruct((nf, ny, nz), F32),
            jax.ShapeDtypeStruct((nf, ny, nz), F32),
        ),
        in_specs=[
            SMEM,
            SMEM,
            pl.BlockSpec((nf, nx, ny, nz), const4),
            pl.BlockSpec((nf, ny, nz), const3),
            pl.BlockSpec((nf, nx, nz), const3),
            pl.BlockSpec((nf, ny, nz), const3),
            pl.BlockSpec((3, 2, 3, nf, XC, ny, nz), lambda i: (0, 0, 0, 0, i, 0, 0)),
        ],
        out_specs=(
            pl.BlockSpec((nf, nx, ny, nz), const4),
            pl.BlockSpec((nf, 2, ny, nz), const4),
            pl.BlockSpec((nf, 3, ny, nz), const4),
            pl.BlockSpec((nf, XC // 4, 8, nz), lambda i: (0, i, 0, 0)),
            pl.BlockSpec((nf, XC // 2, 8, nz), lambda i: (0, i, 0, 0)),
            pl.BlockSpec((nf, ny, nz), const3),
            pl.BlockSpec((nf, ny, nz), const3),
        ),
        scratch_shapes=[pltpu.VMEM((nf, nx + 5, ny, nz), F32)],
        compiler_params=pltpu.CompilerParams(dimension_semantics=("arbitrary",)),
    )(flux_plus, flux_minus, adjoint, xf, yf, zf, stencil_weights)
    axl = shift_from(xl, "gx", -1)
    axr = shift_from(xr, "gx", 1)
    ayl = shift_from(yl, "gy", -1)
    ayr = shift_from(yr, "gy", 1)
    if lax.axis_size("gz") == 2:
        azl, azr = shift_from(jnp.stack([zl, zr]), "gz", 1)
    else:
        azl = shift_from(zl, "gz", -1)
        azr = shift_from(zr, "gz", 1)
    nr = wall_row.shape[0]
    section, wt = pl.pallas_call(
        fix_kernel,
        out_shape=(
            jax.ShapeDtypeStruct((nf, nx, ny, nz), F32),
            jax.ShapeDtypeStruct((nr, nz), F32),
        ),
        in_specs=[SMEM, SMEM] + [VMEM] * 8,
        out_specs=(VMEM, VMEM),
        input_output_aliases={2: 0},
    )(wall_row, wall_count, sec, axl, axr, ayl, ayr, azl, azr, wall_coef)

    npan = panel_owner.shape[0]
    per = npan // ndev
    nb = 32
    na = npan // nb
    pa = wall_panel // nb
    pb = wall_panel % nb
    oh_a = (pa[..., None] == jnp.arange(na, dtype=jnp.int32)).astype(F32) * wt[..., None]
    oh_b = (pb[..., None] == jnp.arange(nb, dtype=jnp.int32)).astype(F32)
    tp = jnp.einsum("rza,rzb->ab", oh_a, oh_b, precision=HI).reshape(npan)
    own_oh = (panel_owner[:, None] == jnp.arange(ndev, dtype=jnp.int32)).astype(F32)
    oh3 = own_oh.reshape(na, nb, ndev)
    below_b = (jnp.arange(nb)[None, :] < jnp.arange(nb)[:, None]).astype(F32)
    below_a = (jnp.arange(na)[None, :] < jnp.arange(na)[:, None]).astype(F32)
    inner = jnp.einsum("bc,acd->abd", below_b, oh3, precision=HI)
    before = jnp.einsum("ac,cd->ad", below_a, jnp.sum(oh3, axis=1), precision=HI)
    rank = jnp.sum((inner + before[:, None, :]) * oh3, axis=2).reshape(npan)
    rank_oh = (rank[:, None] == jnp.arange(per, dtype=F32)).astype(F32)
    t = jnp.einsum("po,pk->ok", own_oh * tp[:, None], rank_oh, precision=HI)
    got = lax.all_to_all(t, AXES, 0, 0, tiled=True)
    return section, jnp.sum(got, axis=0)


def solution(mesh):
    ndev = mesh.size
    placed = (
        P(None, "gx", "gy", "gz"),
        P(None, None, None, None, "gx", "gy", "gz"),
        P(),
        P(),
        P(AXES),
        P(AXES, None),
        P(None, AXES, None),
        P(AXES),
        P(),
    )
    return jax.shard_map(
        lambda *args: on_device(ndev, *args),
        mesh=mesh,
        in_specs=placed,
        out_specs=(P(None, "gx", "gy", "gz"), P(AXES)),
        check_vma=False,
    )
```

```python
import jax
import jax.numpy as jnp
from jax import lax
from jax.experimental import pallas as pl
from jax.experimental.pallas import tpu as pltpu
from jax.sharding import PartitionSpec as P

AXES = ("gx", "gy", "gz")
STEP = 0.4
SECTION = 0.25
XC = 4
F32 = jnp.float32
HI = lax.Precision.HIGHEST
VMEM = pl.BlockSpec(memory_space=pltpu.VMEM)
SMEM = pl.BlockSpec(memory_space=pltpu.SMEM)


def shift_from(x, axis, by):
    n = lax.axis_size(axis)
    return lax.ppermute(x, axis, [(i, (i + by) % n) for i in range(n)])


def iotas(ny, nz):
    return (
        lax.broadcasted_iota(jnp.int32, (ny, nz), 0),
        lax.broadcasted_iota(jnp.int32, (ny, nz), 1),
    )


def fronts_kernel(adj_ref, xf_ref, yf_ref, zf_ref):
    nf, nx, ny, nz = adj_ref.shape
    row, lane = iotas(ny, nz)
    for f in range(nf):
        xf_ref[f] = adj_ref[f, 0]
        zacc = jnp.zeros((ny, nz), F32)
        for x in range(nx):
            s = adj_ref[f, x]
            yf_ref[f, pl.ds(x, 1), :] = s[0:1, :]
            zacc = zacc + pltpu.roll(jnp.where(lane == 0, s, 0.0), x, 1)
        zf_ref[f] = zacc


def offset_terms(plus, minus, w):
    p0, p1, p2 = plus * w(0, 0), plus * w(0, 1), plus * w(0, 2)
    m0, m1, m2 = minus * w(1, 0), minus * w(1, 1), minus * w(1, 2)
    a = p1 + m2
    b = p2 + m1
    return [
        p0 * (1.0 / 3.0),
        p0 * (-7.0 / 6.0) + a * (-1.0 / 6.0),
        p0 * (11.0 / 6.0) + a * (5.0 / 6.0) + b * (1.0 / 3.0),
        a * (1.0 / 3.0) + b * (5.0 / 6.0) + m0 * (11.0 / 6.0),
        b * (-1.0 / 6.0) + m0 * (-7.0 / 6.0),
        m0 * (1.0 / 3.0),
    ]


def rolled_sum(terms, n, axis):
    r = {o: pltpu.roll(terms[o], (o - 2) % n, axis) for o in (0, 1, 3, 4, 5)}
    tot = terms[2] + r[0] + r[1] + r[3] + r[4] + r[5]
    return r, tot


def split_rows(terms, row8, ny):
    r, tot = rolled_sum(terms, ny, 0)
    h = ny - 8
    wr = (jnp.where(row8 < 1, r[3][0:8], 0.0) + jnp.where(row8 < 2, r[4][0:8], 0.0)
          + jnp.where(row8 < 3, r[5][0:8], 0.0))
    wl = jnp.where(row8 >= 6, r[0][h:ny], 0.0) + jnp.where(row8 >= 7, r[1][h:ny], 0.0)
    inner = jnp.concatenate([tot[0:8] - wr, tot[8:h], tot[h:ny] - wl], 0) if h > 8 else \
        jnp.concatenate([tot[0:8] - wr, tot[h:ny] - wl], 0)
    return inner, wr, wl


def split_lanes(terms, lane, nz):
    r, tot = rolled_sum(terms, nz, 1)
    wr = jnp.where(lane < 1, r[3], 0.0) + jnp.where(lane < 2, r[4], 0.0) + jnp.where(lane < 3, r[5], 0.0)
    wl = jnp.where(lane >= nz - 2, r[0], 0.0) + jnp.where(lane >= nz - 1, r[1], 0.0)
    return tot - wr - wl, wr, wl


def stencil_kernel(fp_ref, fm_ref, adj_ref, xf_ref, yf_ref, zf_ref, w_ref,
                   sec_ref, xl_ref, xr_ref, yl_ref, yr_ref, zl_ref, zr_ref, acc_ref):
    nf, nx, ny, nz = adj_ref.shape
    i = pl.program_id(0)
    row, lane = iotas(ny, nz)
    row8 = lax.broadcasted_iota(jnp.int32, (8, nz), 0)

    @pl.when(i == 0)
    def _():
        acc_ref[...] = jnp.zeros_like(acc_ref)
        zl_ref[...] = jnp.zeros_like(zl_ref)
        zr_ref[...] = jnp.zeros_like(zr_ref)

    def flux(d, diff):
        plus, minus = [], []
        for f in range(nf):
            p = m = None
            for g in range(nf):
                tp = diff[g] * (STEP * fp_ref[d, g, f])
                tm = diff[g] * (STEP * fm_ref[d, g, f])
                p = tp if p is None else p + tp
                m = tm if m is None else m + tm
            plus.append(p)
            minus.append(m)
        return plus, minus

    yr_parts = {}
    yl_parts = {}
    for xl in range(XC):
        x = i * XC + xl
        a = [adj_ref[f, x] for f in range(nf)]
        last = x == nx - 1
        nxt = jnp.minimum(x + 1, nx - 1)
        an_x = [jnp.where(last, xf_ref[f], adj_ref[f, nxt]) for f in range(nf)]
        an_y = [
            jnp.where(row == ny - 1, yf_ref[f, pl.ds(x, 1), :], pltpu.roll(a[f], ny - 1, 0))
            for f in range(nf)
        ]
        zshift = nz - 1 - x
        an_z = [
            jnp.where(lane == nz - 1, pltpu.roll(zf_ref[f], zshift, 1), pltpu.roll(a[f], nz - 1, 1))
            for f in range(nf)
        ]
        fx = flux(0, [an_x[g] - a[g] for g in range(nf)])
        fy = flux(1, [an_y[g] - a[g] for g in range(nf)])
        fz = flux(2, [an_z[g] - a[g] for g in range(nf)])
        for f in range(nf):
            sx = offset_terms(fx[0][f], fx[1][f], lambda s, k: w_ref[0, s, k, f, xl])
            sy = offset_terms(fy[0][f], fy[1][f], lambda s, k: w_ref[1, s, k, f, xl])
            sz = offset_terms(fz[0][f], fz[1][f], lambda s, k: w_ref[2, s, k, f, xl])
            iy, wyr, wyl = split_rows(sy, row8, ny)
            iz, wzr, wzl = split_lanes(sz, lane, nz)
            for o in range(6):
                val = sx[o] if o != 2 else sx[2] + iy + iz
                acc_ref[f, x + o] = acc_ref[f, x + o] + val
            rear = pltpu.roll(wyr, 4 * (xl % 2), 0)
            lead = pltpu.roll(wyl, (2 + 2 * (xl % 4)) % 8, 0)
            kr = (f, xl // 2)
            kl = (f, xl // 4)
            yr_parts[kr] = rear if kr not in yr_parts else yr_parts[kr] + rear
            yl_parts[kl] = lead if kl not in yl_parts else yl_parts[kl] + lead
            zr_ref[f] = zr_ref[f] + pltpu.roll(wzr, 4 * x, 1)
            zl_ref[f] = zl_ref[f] + pltpu.roll(wzl, 2 + 4 * x, 1)
    for (f, t), v in yr_parts.items():
        yr_ref[f, t] = v
    for (f, t), v in yl_parts.items():
        yl_ref[f, t] = v

    @pl.when(i == pl.num_programs(0) - 1)
    def _():
        def body(x, c):
            for f in range(nf):
                sec_ref[f, x] = SECTION * (adj_ref[f, x] + acc_ref[f, x + 2])
            return c

        lax.fori_loop(0, nx, body, 0)
        for f in range(nf):
            xl_ref[f] = acc_ref[f, 0:2]
            xr_ref[f] = acc_ref[f, nx + 2:nx + 5]


def fix_kernel(row_ref, cnt_ref, sec_ref, axl_ref, axr_ref, ayl_ref, ayr_ref, azl_ref, azr_ref,
               coef_ref, out_ref, wt_ref):
    nf, nx, ny, nz = sec_ref.shape
    row, lane = iotas(ny, nz)
    pad = jnp.zeros((ny - 8, nz), F32)
    for x in range(nx):
        for f in range(nf):
            ty = jnp.concatenate([ayr_ref[f, x // 2], pad], 0)
            add = jnp.where(row < 3, pltpu.roll(ty, (ny - 4 * (x % 2)) % ny, 0), 0.0)
            ty = jnp.concatenate([ayl_ref[f, x // 4], pad], 0)
            add = add + jnp.where(row >= ny - 2, pltpu.roll(ty, (ny - 2 - 2 * (x % 4)) % ny, 0), 0.0)
            add = add + jnp.where(lane < 3, pltpu.roll(azr_ref[f], (nz - 4 * x) % nz, 1), 0.0)
            add = add + jnp.where(lane >= nz - 2, pltpu.roll(azl_ref[f], (nz - 2 - 4 * x) % nz, 1), 0.0)
            if x < 3:
                add = add + axr_ref[f, x]
            if x >= nx - 2:
                add = add + axl_ref[f, x - (nx - 2)]
            out_ref[f, x] = sec_ref[f, x] + SECTION * add
    live_n = cnt_ref[0]
    for r in range(wt_ref.shape[0]):
        idx = row_ref[r]
        lx = idx // ny
        ly = idx % ny
        val = None
        for f in range(nf):
            v = out_ref[f, lx, pl.ds(ly, 1), :] * coef_ref[f, pl.ds(r, 1), :]
            val = v if val is None else val + v
        wt_ref[pl.ds(r, 1), :] = val * jnp.where(r < live_n, 1.0, 0.0).astype(F32)


def on_device(ndev, adjoint, stencil_weights, flux_plus, flux_minus, wall_row, wall_panel, wall_coef,
              wall_count, panel_owner):
    nf, nx, ny, nz = adjoint.shape
    assert nx % XC == 0 and XC % 4 == 0 and ny == 16 and nx * 4 <= nz
    xf, yf, zf = pl.pallas_call(
        fronts_kernel,
        out_shape=(
            jax.ShapeDtypeStruct((nf, ny, nz), F32),
            jax.ShapeDtypeStruct((nf, nx, nz), F32),
            jax.ShapeDtypeStruct((nf, ny, nz), F32),
        ),
        in_specs=[VMEM],
        out_specs=(VMEM, VMEM, VMEM),
    )(adjoint)
    xf = shift_from(xf, "gx", -1)
    yf = shift_from(yf, "gy", -1)
    zf = shift_from(zf, "gz", -1)
    const4 = lambda i: (0, 0, 0, 0)
    const3 = lambda i: (0, 0, 0)
    sec, xl, xr, yl, yr, zl, zr = pl.pallas_call(
        stencil_kernel,
        grid=(nx // XC,),
        out_shape=(
            jax.ShapeDtypeStruct((nf, nx, ny, nz), F32),
            jax.ShapeDtypeStruct((nf, 2, ny, nz), F32),
            jax.ShapeDtypeStruct((nf, 3, ny, nz), F32),
            jax.ShapeDtypeStruct((nf, nx // 4, 8, nz), F32),
            jax.ShapeDtypeStruct((nf, nx // 2, 8, nz), F32),
            jax.ShapeDtypeStruct((nf, ny, nz), F32),
            jax.ShapeDtypeStruct((nf, ny, nz), F32),
        ),
        in_specs=[
            SMEM,
            SMEM,
            pl.BlockSpec((nf, nx, ny, nz), const4),
            pl.BlockSpec((nf, ny, nz), const3),
            pl.BlockSpec((nf, nx, nz), const3),
            pl.BlockSpec((nf, ny, nz), const3),
            pl.BlockSpec((3, 2, 3, nf, XC, ny, nz), lambda i: (0, 0, 0, 0, i, 0, 0)),
        ],
        out_specs=(
            pl.BlockSpec((nf, nx, ny, nz), const4),
            pl.BlockSpec((nf, 2, ny, nz), const4),
            pl.BlockSpec((nf, 3, ny, nz), const4),
            pl.BlockSpec((nf, XC // 4, 8, nz), lambda i: (0, i, 0, 0)),
            pl.BlockSpec((nf, XC // 2, 8, nz), lambda i: (0, i, 0, 0)),
            pl.BlockSpec((nf, ny, nz), const3),
            pl.BlockSpec((nf, ny, nz), const3),
        ),
        scratch_shapes=[pltpu.VMEM((nf, nx + 5, ny, nz), F32)],
        compiler_params=pltpu.CompilerParams(dimension_semantics=("arbitrary",)),
    )(flux_plus, flux_minus, adjoint, xf, yf, zf, stencil_weights)
    axl = shift_from(xl, "gx", -1)
    axr = shift_from(xr, "gx", 1)
    ayl = shift_from(yl, "gy", -1)
    ayr = shift_from(yr, "gy", 1)
    if lax.axis_size("gz") == 2:
        azl, azr = shift_from(jnp.stack([zl, zr]), "gz", 1)
    else:
        azl = shift_from(zl, "gz", -1)
        azr = shift_from(zr, "gz", 1)
    nr = wall_row.shape[0]
    section, wt = pl.pallas_call(
        fix_kernel,
        out_shape=(
            jax.ShapeDtypeStruct((nf, nx, ny, nz), F32),
            jax.ShapeDtypeStruct((nr, nz), F32),
        ),
        in_specs=[SMEM, SMEM] + [VMEM] * 8,
        out_specs=(VMEM, VMEM),
        input_output_aliases={2: 0},
    )(wall_row, wall_count, sec, axl, axr, ayl, ayr, azl, azr, wall_coef)

    npan = panel_owner.shape[0]
    per = npan // ndev
    nb = 32
    na = npan // nb
    pa = wall_panel // nb
    pb = wall_panel % nb
    oh_a = (pa[..., None] == jnp.arange(na, dtype=jnp.int32)).astype(F32) * wt[..., None]
    oh_b = (pb[..., None] == jnp.arange(nb, dtype=jnp.int32)).astype(F32)
    tp = jnp.einsum("rza,rzb->ab", oh_a, oh_b, precision=HI).reshape(npan)
    own_oh = (panel_owner[:, None] == jnp.arange(ndev, dtype=jnp.int32)).astype(F32)
    oh3 = own_oh.reshape(na, nb, ndev)
    below_b = (jnp.arange(nb)[None, :] < jnp.arange(nb)[:, None]).astype(F32)
    below_a = (jnp.arange(na)[None, :] < jnp.arange(na)[:, None]).astype(F32)
    inner = jnp.einsum("bc,acd->abd", below_b, oh3, precision=HI)
    before = jnp.einsum("ac,cd->ad", below_a, jnp.sum(oh3, axis=1), precision=HI)
    rank = jnp.sum((inner + before[:, None, :]) * oh3, axis=2).reshape(npan)
    rank_oh = (rank[:, None] == jnp.arange(per, dtype=F32)).astype(F32)
    t = jnp.einsum("po,pk->ok", own_oh * tp[:, None], rank_oh, precision=HI)
    got = lax.all_to_all(t, AXES, 0, 0, tiled=True)
    return section, jnp.sum(got, axis=0)


def solution(mesh):
    ndev = mesh.size
    placed = (
        P(None, "gx", "gy", "gz"),
        P(None, None, None, None, "gx", "gy", "gz"),
        P(),
        P(),
        P(AXES),
        P(AXES, None),
        P(None, AXES, None),
        P(AXES),
        P(),
    )
    return jax.shard_map(
        lambda *args: on_device(ndev, *args),
        mesh=mesh,
        in_specs=placed,
        out_specs=(P(None, "gx", "gy", "gz"), P(AXES)),
        check_vma=False,
    )
```

```python
import jax
import jax.numpy as jnp
from jax import lax
from jax.experimental import pallas as pl
from jax.experimental.pallas import tpu as pltpu
from jax.sharding import PartitionSpec as P

AXES = ("gx", "gy", "gz")
STEP = 0.4
SECTION = 0.25
XC = 4
F32 = jnp.float32
HI = lax.Precision.HIGHEST
VMEM = pl.BlockSpec(memory_space=pltpu.VMEM)
SMEM = pl.BlockSpec(memory_space=pltpu.SMEM)


def shift_from(x, axis, by):
    n = lax.axis_size(axis)
    return lax.ppermute(x, axis, [(i, (i + by) % n) for i in range(n)])


def iotas(ny, nz):
    return (
        lax.broadcasted_iota(jnp.int32, (ny, nz), 0),
        lax.broadcasted_iota(jnp.int32, (ny, nz), 1),
    )


def fronts_kernel(adj_ref, xf_ref, yf_ref, zf_ref):
    nf, nx, ny, nz = adj_ref.shape
    row, lane = iotas(ny, nz)
    for f in range(nf):
        xf_ref[f] = adj_ref[f, 0]
        zacc = jnp.zeros((ny, nz), F32)
        for x in range(nx):
            s = adj_ref[f, x]
            yf_ref[f, pl.ds(x, 1), :] = s[0:1, :]
            zacc = zacc + pltpu.roll(jnp.where(lane == 0, s, 0.0), x, 1)
        zf_ref[f] = zacc


def offset_terms(plus, minus, w):
    p0, p1, p2 = plus * w(0, 0), plus * w(0, 1), plus * w(0, 2)
    m0, m1, m2 = minus * w(1, 0), minus * w(1, 1), minus * w(1, 2)
    a = p1 + m2
    b = p2 + m1
    return [
        p0 * (1.0 / 3.0),
        p0 * (-7.0 / 6.0) + a * (-1.0 / 6.0),
        p0 * (11.0 / 6.0) + a * (5.0 / 6.0) + b * (1.0 / 3.0),
        a * (1.0 / 3.0) + b * (5.0 / 6.0) + m0 * (11.0 / 6.0),
        b * (-1.0 / 6.0) + m0 * (-7.0 / 6.0),
        m0 * (1.0 / 3.0),
    ]


def rolled_sum(terms, n, axis):
    r = {o: pltpu.roll(terms[o], (o - 2) % n, axis) for o in (0, 1, 3, 4, 5)}
    tot = terms[2] + r[0] + r[1] + r[3] + r[4] + r[5]
    return r, tot


def split_rows(terms, row8, ny):
    r, tot = rolled_sum(terms, ny, 0)
    h = ny - 8
    wr = (jnp.where(row8 < 1, r[3][0:8], 0.0) + jnp.where(row8 < 2, r[4][0:8], 0.0)
          + jnp.where(row8 < 3, r[5][0:8], 0.0))
    wl = jnp.where(row8 >= 6, r[0][h:ny], 0.0) + jnp.where(row8 >= 7, r[1][h:ny], 0.0)
    inner = jnp.concatenate([tot[0:8] - wr, tot[8:h], tot[h:ny] - wl], 0) if h > 8 else \
        jnp.concatenate([tot[0:8] - wr, tot[h:ny] - wl], 0)
    return inner, wr, wl


def split_lanes(terms, lane, nz):
    r, tot = rolled_sum(terms, nz, 1)
    wr = jnp.where(lane < 1, r[3], 0.0) + jnp.where(lane < 2, r[4], 0.0) + jnp.where(lane < 3, r[5], 0.0)
    wl = jnp.where(lane >= nz - 2, r[0], 0.0) + jnp.where(lane >= nz - 1, r[1], 0.0)
    return tot - wr - wl, wr, wl


def stencil_kernel(fp_ref, fm_ref, adj_ref, xf_ref, yf_ref, zf_ref, w_ref,
                   sec_ref, xl_ref, xr_ref, yl_ref, yr_ref, zl_ref, zr_ref, acc_ref):
    nf, nx, ny, nz = adj_ref.shape
    i = pl.program_id(0)
    row, lane = iotas(ny, nz)
    row8 = lax.broadcasted_iota(jnp.int32, (8, nz), 0)

    @pl.when(i == 0)
    def _():
        acc_ref[...] = jnp.zeros_like(acc_ref)
        zl_ref[...] = jnp.zeros_like(zl_ref)
        zr_ref[...] = jnp.zeros_like(zr_ref)

    def flux(d, diff):
        plus, minus = [], []
        for f in range(nf):
            p = m = None
            for g in range(nf):
                tp = diff[g] * (STEP * fp_ref[d, g, f])
                tm = diff[g] * (STEP * fm_ref[d, g, f])
                p = tp if p is None else p + tp
                m = tm if m is None else m + tm
            plus.append(p)
            minus.append(m)
        return plus, minus

    yr_parts = {}
    yl_parts = {}
    for xl in range(XC):
        x = i * XC + xl
        last = x == nx - 1
        nxt = jnp.minimum(x + 1, nx - 1)
        a = [adj_ref[f, x] for f in range(nf)]
        plus, minus = flux(0, [jnp.where(last, xf_ref[g], adj_ref[g, nxt]) - a[g] for g in range(nf)])
        for f in range(nf):
            sx = offset_terms(plus[f], minus[f], lambda s, k: w_ref[0, s, k, f, xl])
            for o in range(6):
                acc_ref[f, x + o] = acc_ref[f, x + o] + sx[o]
        a = [adj_ref[f, x] for f in range(nf)]
        plus, minus = flux(1, [
            jnp.where(row == ny - 1, yf_ref[g, pl.ds(x, 1), :], pltpu.roll(a[g], ny - 1, 0)) - a[g]
            for g in range(nf)
        ])
        for f in range(nf):
            sy = offset_terms(plus[f], minus[f], lambda s, k: w_ref[1, s, k, f, xl])
            iy, wyr, wyl = split_rows(sy, row8, ny)
            acc_ref[f, x + 2] = acc_ref[f, x + 2] + iy
            rear = pltpu.roll(wyr, 4 * (xl % 2), 0)
            lead = pltpu.roll(wyl, (2 + 2 * (xl % 4)) % 8, 0)
            kr = (f, xl // 2)
            kl = (f, xl // 4)
            yr_parts[kr] = rear if kr not in yr_parts else yr_parts[kr] + rear
            yl_parts[kl] = lead if kl not in yl_parts else yl_parts[kl] + lead
        a = [adj_ref[f, x] for f in range(nf)]
        zshift = nz - 1 - x
        plus, minus = flux(2, [
            jnp.where(lane == nz - 1, pltpu.roll(zf_ref[g], zshift, 1), pltpu.roll(a[g], nz - 1, 1)) - a[g]
            for g in range(nf)
        ])
        for f in range(nf):
            sz = offset_terms(plus[f], minus[f], lambda s, k: w_ref[2, s, k, f, xl])
            iz, wzr, wzl = split_lanes(sz, lane, nz)
            acc_ref[f, x + 2] = acc_ref[f, x + 2] + iz
            zr_ref[f] = zr_ref[f] + pltpu.roll(wzr, 4 * x, 1)
            zl_ref[f] = zl_ref[f] + pltpu.roll(wzl, 2 + 4 * x, 1)
    for (f, t), v in yr_parts.items():
        yr_ref[f, t] = v
    for (f, t), v in yl_parts.items():
        yl_ref[f, t] = v

    @pl.when(i == pl.num_programs(0) - 1)
    def _():
        def body(x, c):
            for f in range(nf):
                sec_ref[f, x] = SECTION * (adj_ref[f, x] + acc_ref[f, x + 2])
            return c

        lax.fori_loop(0, nx, body, 0)
        for f in range(nf):
            xl_ref[f] = acc_ref[f, 0:2]
            xr_ref[f] = acc_ref[f, nx + 2:nx + 5]


def fix_kernel(row_ref, cnt_ref, sec_ref, axl_ref, axr_ref, ayl_ref, ayr_ref, azl_ref, azr_ref,
               coef_ref, out_ref, wt_ref):
    nf, nx, ny, nz = sec_ref.shape
    row, lane = iotas(ny, nz)
    pad = jnp.zeros((ny - 8, nz), F32)
    for x in range(nx):
        for f in range(nf):
            ty = jnp.concatenate([ayr_ref[f, x // 2], pad], 0)
            add = jnp.where(row < 3, pltpu.roll(ty, (ny - 4 * (x % 2)) % ny, 0), 0.0)
            ty = jnp.concatenate([ayl_ref[f, x // 4], pad], 0)
            add = add + jnp.where(row >= ny - 2, pltpu.roll(ty, (ny - 2 - 2 * (x % 4)) % ny, 0), 0.0)
            add = add + jnp.where(lane < 3, pltpu.roll(azr_ref[f], (nz - 4 * x) % nz, 1), 0.0)
            add = add + jnp.where(lane >= nz - 2, pltpu.roll(azl_ref[f], (nz - 2 - 4 * x) % nz, 1), 0.0)
            if x < 3:
                add = add + axr_ref[f, x]
            if x >= nx - 2:
                add = add + axl_ref[f, x - (nx - 2)]
            out_ref[f, x] = sec_ref[f, x] + SECTION * add
    live_n = cnt_ref[0]
    for r in range(wt_ref.shape[0]):
        idx = row_ref[r]
        lx = idx // ny
        ly = idx % ny
        val = None
        for f in range(nf):
            v = out_ref[f, lx, pl.ds(ly, 1), :] * coef_ref[f, pl.ds(r, 1), :]
            val = v if val is None else val + v
        wt_ref[pl.ds(r, 1), :] = val * jnp.where(r < live_n, 1.0, 0.0).astype(F32)


def on_device(ndev, adjoint, stencil_weights, flux_plus, flux_minus, wall_row, wall_panel, wall_coef,
              wall_count, panel_owner):
    nf, nx, ny, nz = adjoint.shape
    assert nx % XC == 0 and XC % 4 == 0 and ny == 16 and nx * 4 <= nz
    xf, yf, zf = pl.pallas_call(
        fronts_kernel,
        out_shape=(
            jax.ShapeDtypeStruct((nf, ny, nz), F32),
            jax.ShapeDtypeStruct((nf, nx, nz), F32),
            jax.ShapeDtypeStruct((nf, ny, nz), F32),
        ),
        in_specs=[VMEM],
        out_specs=(VMEM, VMEM, VMEM),
    )(adjoint)
    xf = shift_from(xf, "gx", -1)
    yf = shift_from(yf, "gy", -1)
    zf = shift_from(zf, "gz", -1)
    const4 = lambda i: (0, 0, 0, 0)
    const3 = lambda i: (0, 0, 0)
    sec, xl, xr, yl, yr, zl, zr = pl.pallas_call(
        stencil_kernel,
        grid=(nx // XC,),
        out_shape=(
            jax.ShapeDtypeStruct((nf, nx, ny, nz), F32),
            jax.ShapeDtypeStruct((nf, 2, ny, nz), F32),
            jax.ShapeDtypeStruct((nf, 3, ny, nz), F32),
            jax.ShapeDtypeStruct((nf, nx // 4, 8, nz), F32),
            jax.ShapeDtypeStruct((nf, nx // 2, 8, nz), F32),
            jax.ShapeDtypeStruct((nf, ny, nz), F32),
            jax.ShapeDtypeStruct((nf, ny, nz), F32),
        ),
        in_specs=[
            SMEM,
            SMEM,
            pl.BlockSpec((nf, nx, ny, nz), const4),
            pl.BlockSpec((nf, ny, nz), const3),
            pl.BlockSpec((nf, nx, nz), const3),
            pl.BlockSpec((nf, ny, nz), const3),
            pl.BlockSpec((3, 2, 3, nf, XC, ny, nz), lambda i: (0, 0, 0, 0, i, 0, 0)),
        ],
        out_specs=(
            pl.BlockSpec((nf, nx, ny, nz), const4),
            pl.BlockSpec((nf, 2, ny, nz), const4),
            pl.BlockSpec((nf, 3, ny, nz), const4),
            pl.BlockSpec((nf, XC // 4, 8, nz), lambda i: (0, i, 0, 0)),
            pl.BlockSpec((nf, XC // 2, 8, nz), lambda i: (0, i, 0, 0)),
            pl.BlockSpec((nf, ny, nz), const3),
            pl.BlockSpec((nf, ny, nz), const3),
        ),
        scratch_shapes=[pltpu.VMEM((nf, nx + 5, ny, nz), F32)],
        compiler_params=pltpu.CompilerParams(dimension_semantics=("arbitrary",)),
    )(flux_plus, flux_minus, adjoint, xf, yf, zf, stencil_weights)
    axl = shift_from(xl, "gx", -1)
    axr = shift_from(xr, "gx", 1)
    ayl = shift_from(yl, "gy", -1)
    ayr = shift_from(yr, "gy", 1)
    if lax.axis_size("gz") == 2:
        azl, azr = shift_from(jnp.stack([zl, zr]), "gz", 1)
    else:
        azl = shift_from(zl, "gz", -1)
        azr = shift_from(zr, "gz", 1)
    nr = wall_row.shape[0]
    section, wt = pl.pallas_call(
        fix_kernel,
        out_shape=(
            jax.ShapeDtypeStruct((nf, nx, ny, nz), F32),
            jax.ShapeDtypeStruct((nr, nz), F32),
        ),
        in_specs=[SMEM, SMEM] + [VMEM] * 8,
        out_specs=(VMEM, VMEM),
        input_output_aliases={2: 0},
    )(wall_row, wall_count, sec, axl, axr, ayl, ayr, azl, azr, wall_coef)

    npan = panel_owner.shape[0]
    per = npan // ndev
    nb = 32
    na = npan // nb
    pa = wall_panel // nb
    pb = wall_panel % nb
    oh_a = (pa[..., None] == jnp.arange(na, dtype=jnp.int32)).astype(F32) * wt[..., None]
    oh_b = (pb[..., None] == jnp.arange(nb, dtype=jnp.int32)).astype(F32)
    tp = jnp.einsum("rza,rzb->ab", oh_a, oh_b, precision=HI).reshape(npan)
    own_oh = (panel_owner[:, None] == jnp.arange(ndev, dtype=jnp.int32)).astype(F32)
    oh3 = own_oh.reshape(na, nb, ndev)
    below_b = (jnp.arange(nb)[None, :] < jnp.arange(nb)[:, None]).astype(F32)
    below_a = (jnp.arange(na)[None, :] < jnp.arange(na)[:, None]).astype(F32)
    inner = jnp.einsum("bc,acd->abd", below_b, oh3, precision=HI)
    before = jnp.einsum("ac,cd->ad", below_a, jnp.sum(oh3, axis=1), precision=HI)
    rank = jnp.sum((inner + before[:, None, :]) * oh3, axis=2).reshape(npan)
    rank_oh = (rank[:, None] == jnp.arange(per, dtype=F32)).astype(F32)
    t = jnp.einsum("po,pk->ok", own_oh * tp[:, None], rank_oh, precision=HI)
    got = lax.all_to_all(t, AXES, 0, 0, tiled=True)
    return section, jnp.sum(got, axis=0)


def solution(mesh):
    ndev = mesh.size
    placed = (
        P(None, "gx", "gy", "gz"),
        P(None, None, None, None, "gx", "gy", "gz"),
        P(),
        P(),
        P(AXES),
        P(AXES, None),
        P(None, AXES, None),
        P(AXES),
        P(),
    )
    return jax.shard_map(
        lambda *args: on_device(ndev, *args),
        mesh=mesh,
        in_specs=placed,
        out_specs=(P(None, "gx", "gy", "gz"), P(AXES)),
        check_vma=False,
    )
```

```python
import jax
import jax.numpy as jnp
from jax import lax
from jax.experimental import pallas as pl
from jax.experimental.pallas import tpu as pltpu
from jax.sharding import PartitionSpec as P

AXES = ("gx", "gy", "gz")
STEP = 0.4
SECTION = 0.25
XC = 4
F32 = jnp.float32
HI = lax.Precision.HIGHEST
VMEM = pl.BlockSpec(memory_space=pltpu.VMEM)
SMEM = pl.BlockSpec(memory_space=pltpu.SMEM)


def shift_from(x, axis, by):
    n = lax.axis_size(axis)
    return lax.ppermute(x, axis, [(i, (i + by) % n) for i in range(n)])


def iotas(ny, nz):
    return (
        lax.broadcasted_iota(jnp.int32, (ny, nz), 0),
        lax.broadcasted_iota(jnp.int32, (ny, nz), 1),
    )


def fronts_kernel(adj_ref, xf_ref, yf_ref, zf_ref):
    nf, nx, ny, nz = adj_ref.shape
    row, lane = iotas(ny, nz)
    for f in range(nf):
        xf_ref[f] = adj_ref[f, 0]
        zacc = jnp.zeros((ny, nz), F32)
        for x in range(nx):
            s = adj_ref[f, x]
            yf_ref[f, pl.ds(x, 1), :] = s[0:1, :]
            zacc = zacc + pltpu.roll(jnp.where(lane == 0, s, 0.0), x, 1)
        zf_ref[f] = zacc


def offset_terms(plus, minus, w):
    p0, p1, p2 = plus * w(0, 0), plus * w(0, 1), plus * w(0, 2)
    m0, m1, m2 = minus * w(1, 0), minus * w(1, 1), minus * w(1, 2)
    a = p1 + m2
    b = p2 + m1
    return [
        p0 * (1.0 / 3.0),
        p0 * (-7.0 / 6.0) + a * (-1.0 / 6.0),
        p0 * (11.0 / 6.0) + a * (5.0 / 6.0) + b * (1.0 / 3.0),
        a * (1.0 / 3.0) + b * (5.0 / 6.0) + m0 * (11.0 / 6.0),
        b * (-1.0 / 6.0) + m0 * (-7.0 / 6.0),
        m0 * (1.0 / 3.0),
    ]


def rolled_sum(terms, n, axis):
    r = {o: pltpu.roll(terms[o], (o - 2) % n, axis) for o in (0, 1, 3, 4, 5)}
    tot = terms[2] + r[0] + r[1] + r[3] + r[4] + r[5]
    return r, tot


def split_rows(terms, row8, ny):
    r, tot = rolled_sum(terms, ny, 0)
    h = ny - 8
    wr = (jnp.where(row8 < 1, r[3][0:8], 0.0) + jnp.where(row8 < 2, r[4][0:8], 0.0)
          + jnp.where(row8 < 3, r[5][0:8], 0.0))
    wl = jnp.where(row8 >= 6, r[0][h:ny], 0.0) + jnp.where(row8 >= 7, r[1][h:ny], 0.0)
    inner = jnp.concatenate([tot[0:8] - wr, tot[8:h], tot[h:ny] - wl], 0) if h > 8 else \
        jnp.concatenate([tot[0:8] - wr, tot[h:ny] - wl], 0)
    return inner, wr, wl


def split_lanes(terms, lane, nz):
    r, tot = rolled_sum(terms, nz, 1)
    wr = jnp.where(lane < 1, r[3], 0.0) + jnp.where(lane < 2, r[4], 0.0) + jnp.where(lane < 3, r[5], 0.0)
    wl = jnp.where(lane >= nz - 2, r[0], 0.0) + jnp.where(lane >= nz - 1, r[1], 0.0)
    return tot - wr - wl, wr, wl


def stencil_kernel(fp_ref, fm_ref, adj_ref, xf_ref, yf_ref, zf_ref, w_ref,
                   sec_ref, xl_ref, xr_ref, yl_ref, yr_ref, zz_ref, acc_ref):
    nf, nx, ny, nz = adj_ref.shape
    i = pl.program_id(0)
    row, lane = iotas(ny, nz)
    row8 = lax.broadcasted_iota(jnp.int32, (8, nz), 0)

    @pl.when(i == 0)
    def _():
        acc_ref[...] = jnp.zeros_like(acc_ref)
        zz_ref[...] = jnp.zeros_like(zz_ref)

    def flux(d, diff):
        plus, minus = [], []
        for f in range(nf):
            p = m = None
            for g in range(nf):
                tp = diff[g] * (STEP * fp_ref[d, g, f])
                tm = diff[g] * (STEP * fm_ref[d, g, f])
                p = tp if p is None else p + tp
                m = tm if m is None else m + tm
            plus.append(p)
            minus.append(m)
        return plus, minus

    yr_parts = {}
    yl_parts = {}
    for xl in range(XC):
        x = i * XC + xl
        last = x == nx - 1
        nxt = jnp.minimum(x + 1, nx - 1)
        a = [adj_ref[f, x] for f in range(nf)]
        plus, minus = flux(0, [jnp.where(last, xf_ref[g], adj_ref[g, nxt]) - a[g] for g in range(nf)])
        for f in range(nf):
            sx = offset_terms(plus[f], minus[f], lambda s, k: w_ref[0, s, k, f, xl])
            for o in range(6):
                acc_ref[f, x + o] = acc_ref[f, x + o] + sx[o]
        a = [adj_ref[f, x] for f in range(nf)]
        plus, minus = flux(1, [
            jnp.where(row == ny - 1, yf_ref[g, pl.ds(x, 1), :], pltpu.roll(a[g], ny - 1, 0)) - a[g]
            for g in range(nf)
        ])
        for f in range(nf):
            sy = offset_terms(plus[f], minus[f], lambda s, k: w_ref[1, s, k, f, xl])
            iy, wyr, wyl = split_rows(sy, row8, ny)
            acc_ref[f, x + 2] = acc_ref[f, x + 2] + iy
            rear = pltpu.roll(wyr, 4 * (xl % 2), 0)
            lead = pltpu.roll(wyl, (2 + 2 * (xl % 4)) % 8, 0)
            kr = (f, xl // 2)
            kl = (f, xl // 4)
            yr_parts[kr] = rear if kr not in yr_parts else yr_parts[kr] + rear
            yl_parts[kl] = lead if kl not in yl_parts else yl_parts[kl] + lead
        a = [adj_ref[f, x] for f in range(nf)]
        zshift = nz - 1 - x
        plus, minus = flux(2, [
            jnp.where(lane == nz - 1, pltpu.roll(zf_ref[g], zshift, 1), pltpu.roll(a[g], nz - 1, 1)) - a[g]
            for g in range(nf)
        ])
        for f in range(nf):
            sz = offset_terms(plus[f], minus[f], lambda s, k: w_ref[2, s, k, f, xl])
            iz, wzr, wzl = split_lanes(sz, lane, nz)
            acc_ref[f, x + 2] = acc_ref[f, x + 2] + iz
            zz_ref[0, f] = zz_ref[0, f] + pltpu.roll(wzl, 2 + 4 * x, 1)
            zz_ref[1, f] = zz_ref[1, f] + pltpu.roll(wzr, 4 * x, 1)
    for (f, t), v in yr_parts.items():
        yr_ref[f, t] = v
    for (f, t), v in yl_parts.items():
        yl_ref[f, t] = v

    @pl.when(i == pl.num_programs(0) - 1)
    def _():
        def body(x, c):
            for f in range(nf):
                sec_ref[f, x] = SECTION * (adj_ref[f, x] + acc_ref[f, x + 2])
            return c

        lax.fori_loop(0, nx, body, 0)
        for f in range(nf):
            xl_ref[f] = acc_ref[f, 0:2]
            xr_ref[f] = acc_ref[f, nx + 2:nx + 5]


def fix_kernel(row_ref, cnt_ref, sec_ref, axl_ref, axr_ref, ayl_ref, ayr_ref, az_ref,
               coef_ref, out_ref, wt_ref):
    nf, nx, ny, nz = sec_ref.shape
    row, lane = iotas(ny, nz)
    pad = jnp.zeros((ny - 8, nz), F32)
    for x in range(nx):
        for f in range(nf):
            ty = jnp.concatenate([ayr_ref[f, x // 2], pad], 0)
            add = jnp.where(row < 3, pltpu.roll(ty, (ny - 4 * (x % 2)) % ny, 0), 0.0)
            ty = jnp.concatenate([ayl_ref[f, x // 4], pad], 0)
            add = add + jnp.where(row >= ny - 2, pltpu.roll(ty, (ny - 2 - 2 * (x % 4)) % ny, 0), 0.0)
            add = add + jnp.where(lane < 3, pltpu.roll(az_ref[1, f], (nz - 4 * x) % nz, 1), 0.0)
            add = add + jnp.where(lane >= nz - 2, pltpu.roll(az_ref[0, f], (nz - 2 - 4 * x) % nz, 1), 0.0)
            if x < 3:
                add = add + axr_ref[f, x]
            if x >= nx - 2:
                add = add + axl_ref[f, x - (nx - 2)]
            out_ref[f, x] = sec_ref[f, x] + SECTION * add
    live_n = cnt_ref[0]
    for r in range(wt_ref.shape[0]):
        idx = row_ref[r]
        lx = idx // ny
        ly = idx % ny
        val = None
        for f in range(nf):
            v = out_ref[f, lx, pl.ds(ly, 1), :] * coef_ref[f, pl.ds(r, 1), :]
            val = v if val is None else val + v
        wt_ref[pl.ds(r, 1), :] = val * jnp.where(r < live_n, 1.0, 0.0).astype(F32)


def on_device(ndev, adjoint, stencil_weights, flux_plus, flux_minus, wall_row, wall_panel, wall_coef,
              wall_count, panel_owner):
    nf, nx, ny, nz = adjoint.shape
    assert nx % XC == 0 and XC % 4 == 0 and ny == 16 and nx * 4 <= nz
    xf, yf, zf = pl.pallas_call(
        fronts_kernel,
        out_shape=(
            jax.ShapeDtypeStruct((nf, ny, nz), F32),
            jax.ShapeDtypeStruct((nf, nx, nz), F32),
            jax.ShapeDtypeStruct((nf, ny, nz), F32),
        ),
        in_specs=[VMEM],
        out_specs=(VMEM, VMEM, VMEM),
    )(adjoint)
    xf = shift_from(xf, "gx", -1)
    yf = shift_from(yf, "gy", -1)
    zf = shift_from(zf, "gz", -1)
    const4 = lambda i: (0, 0, 0, 0)
    const3 = lambda i: (0, 0, 0)
    sec, xl, xr, yl, yr, zz = pl.pallas_call(
        stencil_kernel,
        grid=(nx // XC,),
        out_shape=(
            jax.ShapeDtypeStruct((nf, nx, ny, nz), F32),
            jax.ShapeDtypeStruct((nf, 2, ny, nz), F32),
            jax.ShapeDtypeStruct((nf, 3, ny, nz), F32),
            jax.ShapeDtypeStruct((nf, nx // 4, 8, nz), F32),
            jax.ShapeDtypeStruct((nf, nx // 2, 8, nz), F32),
            jax.ShapeDtypeStruct((2, nf, ny, nz), F32),
        ),
        in_specs=[
            SMEM,
            SMEM,
            pl.BlockSpec((nf, nx, ny, nz), const4),
            pl.BlockSpec((nf, ny, nz), const3),
            pl.BlockSpec((nf, nx, nz), const3),
            pl.BlockSpec((nf, ny, nz), const3),
            pl.BlockSpec((3, 2, 3, nf, XC, ny, nz), lambda i: (0, 0, 0, 0, i, 0, 0)),
        ],
        out_specs=(
            pl.BlockSpec((nf, nx, ny, nz), const4),
            pl.BlockSpec((nf, 2, ny, nz), const4),
            pl.BlockSpec((nf, 3, ny, nz), const4),
            pl.BlockSpec((nf, XC // 4, 8, nz), lambda i: (0, i, 0, 0)),
            pl.BlockSpec((nf, XC // 2, 8, nz), lambda i: (0, i, 0, 0)),
            pl.BlockSpec((2, nf, ny, nz), const4),
        ),
        scratch_shapes=[pltpu.VMEM((nf, nx + 5, ny, nz), F32)],
        compiler_params=pltpu.CompilerParams(dimension_semantics=("arbitrary",)),
    )(flux_plus, flux_minus, adjoint, xf, yf, zf, stencil_weights)
    axl = shift_from(xl, "gx", -1)
    axr = shift_from(xr, "gx", 1)
    ayl = shift_from(yl, "gy", -1)
    ayr = shift_from(yr, "gy", 1)
    if lax.axis_size("gz") == 2:
        az = shift_from(zz, "gz", 1)
    else:
        az = jnp.stack([shift_from(zz[0], "gz", -1), shift_from(zz[1], "gz", 1)])
    nr = wall_row.shape[0]
    section, wt = pl.pallas_call(
        fix_kernel,
        out_shape=(
            jax.ShapeDtypeStruct((nf, nx, ny, nz), F32),
            jax.ShapeDtypeStruct((nr, nz), F32),
        ),
        in_specs=[SMEM, SMEM] + [VMEM] * 7,
        out_specs=(VMEM, VMEM),
        input_output_aliases={2: 0},
    )(wall_row, wall_count, sec, axl, axr, ayl, ayr, az, wall_coef)

    npan = panel_owner.shape[0]
    per = npan // ndev
    nb = 32
    na = npan // nb
    pa = wall_panel // nb
    pb = wall_panel % nb
    oh_a = (pa[..., None] == jnp.arange(na, dtype=jnp.int32)).astype(F32) * wt[..., None]
    oh_b = (pb[..., None] == jnp.arange(nb, dtype=jnp.int32)).astype(F32)
    tp = jnp.einsum("rza,rzb->ab", oh_a, oh_b, precision=HI).reshape(npan)
    own_oh = (panel_owner[:, None] == jnp.arange(ndev, dtype=jnp.int32)).astype(F32)
    oh3 = own_oh.reshape(na, nb, ndev)
    below_b = (jnp.arange(nb)[None, :] < jnp.arange(nb)[:, None]).astype(F32)
    below_a = (jnp.arange(na)[None, :] < jnp.arange(na)[:, None]).astype(F32)
    inner = jnp.einsum("bc,acd->abd", below_b, oh3, precision=HI)
    before = jnp.einsum("ac,cd->ad", below_a, jnp.sum(oh3, axis=1), precision=HI)
    rank = jnp.sum((inner + before[:, None, :]) * oh3, axis=2).reshape(npan)
    rank_oh = (rank[:, None] == jnp.arange(per, dtype=F32)).astype(F32)
    t = jnp.einsum("po,pk->ok", own_oh * tp[:, None], rank_oh, precision=HI)
    got = lax.all_to_all(t, AXES, 0, 0, tiled=True)
    return section, jnp.sum(got, axis=0)


def solution(mesh):
    ndev = mesh.size
    placed = (
        P(None, "gx", "gy", "gz"),
        P(None, None, None, None, "gx", "gy", "gz"),
        P(),
        P(),
        P(AXES),
        P(AXES, None),
        P(None, AXES, None),
        P(AXES),
        P(),
    )
    return jax.shard_map(
        lambda *args: on_device(ndev, *args),
        mesh=mesh,
        in_specs=placed,
        out_specs=(P(None, "gx", "gy", "gz"), P(AXES)),
        check_vma=False,
    )
```

```python
import jax
import jax.numpy as jnp
from jax import lax
from jax.experimental import pallas as pl
from jax.experimental.pallas import tpu as pltpu
from jax.sharding import PartitionSpec as P

AXES = ("gx", "gy", "gz")
STEP = 0.4
SECTION = 0.25
XC = 4
F32 = jnp.float32
HI = lax.Precision.HIGHEST
VMEM = pl.BlockSpec(memory_space=pltpu.VMEM)
SMEM = pl.BlockSpec(memory_space=pltpu.SMEM)


def shift_from(x, axis, by):
    n = lax.axis_size(axis)
    return lax.ppermute(x, axis, [(i, (i + by) % n) for i in range(n)])


def iotas(ny, nz):
    return (
        lax.broadcasted_iota(jnp.int32, (ny, nz), 0),
        lax.broadcasted_iota(jnp.int32, (ny, nz), 1),
    )


def fronts_kernel(adj_ref, xf_ref, yf_ref, zf_ref):
    nf, nx, ny, nz = adj_ref.shape
    row, lane = iotas(ny, nz)
    for f in range(nf):
        xf_ref[f] = adj_ref[f, 0]
        zacc = jnp.zeros((ny, nz), F32)
        for x in range(nx):
            s = adj_ref[f, x]
            yf_ref[f, pl.ds(x, 1), :] = s[0:1, :]
            zacc = zacc + pltpu.roll(jnp.where(lane == 0, s, 0.0), x, 1)
        zf_ref[f] = zacc


def offset_terms(plus, minus, w):
    p0, p1, p2 = plus * w(0, 0), plus * w(0, 1), plus * w(0, 2)
    m0, m1, m2 = minus * w(1, 0), minus * w(1, 1), minus * w(1, 2)
    a = p1 + m2
    b = p2 + m1
    return [
        p0 * (1.0 / 3.0),
        p0 * (-7.0 / 6.0) + a * (-1.0 / 6.0),
        p0 * (11.0 / 6.0) + a * (5.0 / 6.0) + b * (1.0 / 3.0),
        a * (1.0 / 3.0) + b * (5.0 / 6.0) + m0 * (11.0 / 6.0),
        b * (-1.0 / 6.0) + m0 * (-7.0 / 6.0),
        m0 * (1.0 / 3.0),
    ]


def rolled_sum(terms, n, axis):
    r = {o: pltpu.roll(terms[o], (o - 2) % n, axis) for o in (0, 1, 3, 4, 5)}
    tot = terms[2] + r[0] + r[1] + r[3] + r[4] + r[5]
    return r, tot


def split_rows(terms, row8, ny):
    r, tot = rolled_sum(terms, ny, 0)
    h = ny - 8
    wr = (jnp.where(row8 < 1, r[3][0:8], 0.0) + jnp.where(row8 < 2, r[4][0:8], 0.0)
          + jnp.where(row8 < 3, r[5][0:8], 0.0))
    wl = jnp.where(row8 >= 6, r[0][h:ny], 0.0) + jnp.where(row8 >= 7, r[1][h:ny], 0.0)
    inner = jnp.concatenate([tot[0:8] - wr, tot[8:h], tot[h:ny] - wl], 0) if h > 8 else \
        jnp.concatenate([tot[0:8] - wr, tot[h:ny] - wl], 0)
    return inner, wr, wl


def split_lanes(terms, lane, nz):
    r, tot = rolled_sum(terms, nz, 1)
    wr = jnp.where(lane < 1, r[3], 0.0) + jnp.where(lane < 2, r[4], 0.0) + jnp.where(lane < 3, r[5], 0.0)
    wl = jnp.where(lane >= nz - 2, r[0], 0.0) + jnp.where(lane >= nz - 1, r[1], 0.0)
    return tot - wr - wl, wr, wl


def stencil_kernel(fp_ref, fm_ref, adj_ref, xf_ref, yf_ref, zf_ref, w_ref,
                   sec_ref, xl_ref, xr_ref, yl_ref, yr_ref, zz_ref, acc_ref):
    nf, nx, ny, nz = adj_ref.shape
    i = pl.program_id(0)
    row, lane = iotas(ny, nz)
    row8 = lax.broadcasted_iota(jnp.int32, (8, nz), 0)

    @pl.when(i == 0)
    def _():
        acc_ref[...] = jnp.zeros_like(acc_ref)
        zz_ref[...] = jnp.zeros_like(zz_ref)

    def flux(d, diff):
        plus, minus = [], []
        for f in range(nf):
            p = m = None
            for g in range(nf):
                tp = diff[g] * (STEP * fp_ref[d, g, f])
                tm = diff[g] * (STEP * fm_ref[d, g, f])
                p = tp if p is None else p + tp
                m = tm if m is None else m + tm
            plus.append(p)
            minus.append(m)
        return plus, minus

    yr_parts = {}
    yl_parts = {}
    for xl in range(XC):
        x = i * XC + xl
        last = x == nx - 1
        nxt = jnp.minimum(x + 1, nx - 1)
        a = [adj_ref[f, x] for f in range(nf)]
        plus, minus = flux(0, [jnp.where(last, xf_ref[g], adj_ref[g, nxt]) - a[g] for g in range(nf)])
        for f in range(nf):
            sx = offset_terms(plus[f], minus[f], lambda s, k: w_ref[0, s, k, f, xl])
            for o in range(6):
                acc_ref[f, x + o] = acc_ref[f, x + o] + sx[o]
        a = [adj_ref[f, x] for f in range(nf)]
        plus, minus = flux(1, [
            jnp.where(row == ny - 1, yf_ref[g, pl.ds(x, 1), :], pltpu.roll(a[g], ny - 1, 0)) - a[g]
            for g in range(nf)
        ])
        for f in range(nf):
            sy = offset_terms(plus[f], minus[f], lambda s, k: w_ref[1, s, k, f, xl])
            iy, wyr, wyl = split_rows(sy, row8, ny)
            acc_ref[f, x + 2] = acc_ref[f, x + 2] + iy
            rear = pltpu.roll(wyr, 4 * (xl % 2), 0)
            lead = pltpu.roll(wyl, (2 + 2 * (xl % 4)) % 8, 0)
            kr = (f, xl // 2)
            kl = (f, xl // 4)
            yr_parts[kr] = rear if kr not in yr_parts else yr_parts[kr] + rear
            yl_parts[kl] = lead if kl not in yl_parts else yl_parts[kl] + lead
        a = [adj_ref[f, x] for f in range(nf)]
        zshift = nz - 1 - x
        plus, minus = flux(2, [
            jnp.where(lane == nz - 1, pltpu.roll(zf_ref[g], zshift, 1), pltpu.roll(a[g], nz - 1, 1)) - a[g]
            for g in range(nf)
        ])
        for f in range(nf):
            sz = offset_terms(plus[f], minus[f], lambda s, k: w_ref[2, s, k, f, xl])
            iz, wzr, wzl = split_lanes(sz, lane, nz)
            acc_ref[f, x + 2] = acc_ref[f, x + 2] + iz
            zz_ref[0, f] = zz_ref[0, f] + pltpu.roll(wzl, 2 + 4 * x, 1)
            zz_ref[1, f] = zz_ref[1, f] + pltpu.roll(wzr, 4 * x, 1)
    for (f, t), v in yr_parts.items():
        yr_ref[f, t] = v
    for (f, t), v in yl_parts.items():
        yl_ref[f, t] = v

    @pl.when(i == pl.num_programs(0) - 1)
    def _():
        def body(x, c):
            for f in range(nf):
                sec_ref[f, x] = SECTION * (adj_ref[f, x] + acc_ref[f, x + 2])
            return c

        lax.fori_loop(0, nx, body, 0)
        for f in range(nf):
            xl_ref[f] = acc_ref[f, 0:2]
            xr_ref[f] = acc_ref[f, nx + 2:nx + 5]


def fix_kernel(row_ref, cnt_ref, sec_ref, axl_ref, axr_ref, ayl_ref, ayr_ref, az_ref,
               coef_ref, out_ref, wt_ref):
    nf, nx, ny, nz = sec_ref.shape
    row, lane = iotas(ny, nz)
    pad = jnp.zeros((ny - 8, nz), F32)
    for x in range(nx):
        for f in range(nf):
            ty = jnp.concatenate([ayr_ref[f, x // 2], pad], 0)
            add = jnp.where(row < 3, pltpu.roll(ty, (ny - 4 * (x % 2)) % ny, 0), 0.0)
            ty = jnp.concatenate([ayl_ref[f, x // 4], pad], 0)
            add = add + jnp.where(row >= ny - 2, pltpu.roll(ty, (ny - 2 - 2 * (x % 4)) % ny, 0), 0.0)
            add = add + jnp.where(lane < 3, pltpu.roll(az_ref[1, f], (nz - 4 * x) % nz, 1), 0.0)
            add = add + jnp.where(lane >= nz - 2, pltpu.roll(az_ref[0, f], (nz - 2 - 4 * x) % nz, 1), 0.0)
            if x < 3:
                add = add + axr_ref[f, x]
            if x >= nx - 2:
                add = add + axl_ref[f, x - (nx - 2)]
            out_ref[f, x] = sec_ref[f, x] + SECTION * add
    live_n = cnt_ref[0]
    for r in range(wt_ref.shape[0]):
        idx = row_ref[r]
        lx = idx // ny
        ly = idx % ny
        val = None
        for f in range(nf):
            v = out_ref[f, lx, pl.ds(ly, 1), :] * coef_ref[f, pl.ds(r, 1), :]
            val = v if val is None else val + v
        wt_ref[pl.ds(r, 1), :] = val * jnp.where(r < live_n, 1.0, 0.0).astype(F32)


def on_device(ndev, adjoint, stencil_weights, flux_plus, flux_minus, wall_row, wall_panel, wall_coef,
              wall_count, panel_owner):
    nf, nx, ny, nz = adjoint.shape
    assert nx % XC == 0 and XC % 4 == 0 and ny == 16 and nx * 4 <= nz
    xf, yf, zf = pl.pallas_call(
        fronts_kernel,
        out_shape=(
            jax.ShapeDtypeStruct((nf, ny, nz), F32),
            jax.ShapeDtypeStruct((nf, nx, nz), F32),
            jax.ShapeDtypeStruct((nf, ny, nz), F32),
        ),
        in_specs=[VMEM],
        out_specs=(VMEM, VMEM, VMEM),
    )(adjoint)
    xf = shift_from(xf, "gx", -1)
    yf = shift_from(yf, "gy", -1)
    zf = shift_from(zf, "gz", -1)
    const4 = lambda i: (0, 0, 0, 0)
    const3 = lambda i: (0, 0, 0)
    sec, xl, xr, yl, yr, zz = pl.pallas_call(
        stencil_kernel,
        grid=(nx // XC,),
        out_shape=(
            jax.ShapeDtypeStruct((nf, nx, ny, nz), F32),
            jax.ShapeDtypeStruct((nf, 2, ny, nz), F32),
            jax.ShapeDtypeStruct((nf, 3, ny, nz), F32),
            jax.ShapeDtypeStruct((nf, nx // 4, 8, nz), F32),
            jax.ShapeDtypeStruct((nf, nx // 2, 8, nz), F32),
            jax.ShapeDtypeStruct((2, nf, ny, nz), F32),
        ),
        in_specs=[
            SMEM,
            SMEM,
            pl.BlockSpec((nf, nx, ny, nz), const4),
            pl.BlockSpec((nf, ny, nz), const3),
            pl.BlockSpec((nf, nx, nz), const3),
            pl.BlockSpec((nf, ny, nz), const3),
            pl.BlockSpec((3, 2, 3, nf, XC, ny, nz), lambda i: (0, 0, 0, 0, i, 0, 0)),
        ],
        out_specs=(
            pl.BlockSpec((nf, nx, ny, nz), const4),
            pl.BlockSpec((nf, 2, ny, nz), const4),
            pl.BlockSpec((nf, 3, ny, nz), const4),
            pl.BlockSpec((nf, XC // 4, 8, nz), lambda i: (0, i, 0, 0)),
            pl.BlockSpec((nf, XC // 2, 8, nz), lambda i: (0, i, 0, 0)),
            pl.BlockSpec((2, nf, ny, nz), const4),
        ),
        scratch_shapes=[pltpu.VMEM((nf, nx + 5, ny, nz), F32)],
        compiler_params=pltpu.CompilerParams(dimension_semantics=("arbitrary",)),
    )(flux_plus, flux_minus, adjoint, xf, yf, zf, stencil_weights)
    axl = shift_from(xl, "gx", -1)
    axr = shift_from(xr, "gx", 1)
    ayl = shift_from(yl, "gy", -1)
    ayr = shift_from(yr, "gy", 1)
    if lax.axis_size("gz") == 2:
        az = shift_from(zz, "gz", 1)
    else:
        az = jnp.stack([shift_from(zz[0], "gz", -1), shift_from(zz[1], "gz", 1)])
    nr = wall_row.shape[0]
    section, wt = pl.pallas_call(
        fix_kernel,
        out_shape=(
            jax.ShapeDtypeStruct((nf, nx, ny, nz), F32),
            jax.ShapeDtypeStruct((nr, nz), F32),
        ),
        in_specs=[SMEM, SMEM] + [VMEM] * 7,
        out_specs=(VMEM, VMEM),
        input_output_aliases={2: 0},
    )(wall_row, wall_count, sec, axl, axr, ayl, ayr, az, wall_coef)

    npan = panel_owner.shape[0]
    per = npan // ndev
    nb = 32
    na = npan // nb
    own_oh = (panel_owner[:, None] == jnp.arange(ndev, dtype=jnp.int32)).astype(F32)
    oh3 = own_oh.reshape(na, nb, ndev)
    below_b = (jnp.arange(nb)[None, :] < jnp.arange(nb)[:, None]).astype(F32)
    below_a = (jnp.arange(na)[None, :] < jnp.arange(na)[:, None]).astype(F32)
    inner = jnp.einsum("bc,acd->abd", below_b, oh3, precision=HI)
    before = jnp.einsum("ac,cd->ad", below_a, jnp.sum(oh3, axis=1), precision=HI)
    rank = jnp.sum((inner + before[:, None, :]) * oh3, axis=2)
    oh_a = (wall_panel[..., None] // nb == jnp.arange(na, dtype=jnp.int32)).astype(F32)
    oh_b = (wall_panel[..., None] % nb == jnp.arange(nb, dtype=jnp.int32)).astype(F32)

    def lookup(table):
        picked = jnp.einsum("rza,ab->rzb", oh_a, table, precision=HI) * oh_b
        return jnp.round(jnp.sum(picked, axis=2)).astype(jnp.int32)

    cell_own = lookup(panel_owner.reshape(na, nb).astype(F32))
    cell_rank = lookup(rank)
    oh_o = (cell_own[..., None] == jnp.arange(ndev, dtype=jnp.int32)).astype(F32)
    oh_k = (cell_rank[..., None] == jnp.arange(per, dtype=jnp.int32)).astype(F32)
    t = jnp.einsum("rzo,rzk->ok", oh_o * wt[..., None], oh_k, precision=HI)
    got = lax.all_to_all(t, AXES, 0, 0, tiled=True)
    return section, jnp.sum(got, axis=0)


def solution(mesh):
    ndev = mesh.size
    placed = (
        P(None, "gx", "gy", "gz"),
        P(None, None, None, None, "gx", "gy", "gz"),
        P(),
        P(),
        P(AXES),
        P(AXES, None),
        P(None, AXES, None),
        P(AXES),
        P(),
    )
    return jax.shard_map(
        lambda *args: on_device(ndev, *args),
        mesh=mesh,
        in_specs=placed,
        out_specs=(P(None, "gx", "gy", "gz"), P(AXES)),
        check_vma=False,
    )
```

```python
import jax
import jax.numpy as jnp
from jax import lax
from jax.experimental import pallas as pl
from jax.experimental.pallas import tpu as pltpu
from jax.sharding import PartitionSpec as P

AXES = ("gx", "gy", "gz")
STEP = 0.4
SECTION = 0.25
XC = 4
F32 = jnp.float32
HI = lax.Precision.HIGHEST
VMEM = pl.BlockSpec(memory_space=pltpu.VMEM)
SMEM = pl.BlockSpec(memory_space=pltpu.SMEM)
ANY = pl.BlockSpec(memory_space=pl.ANY)


def shift_from(x, axis, by):
    n = lax.axis_size(axis)
    return lax.ppermute(x, axis, [(i, (i + by) % n) for i in range(n)])


def iotas(ny, nz):
    return (
        lax.broadcasted_iota(jnp.int32, (ny, nz), 0),
        lax.broadcasted_iota(jnp.int32, (ny, nz), 1),
    )


def fronts_kernel(adj_ref, ysl_ref, xf_ref, zf_ref):
    del ysl_ref
    nf, nx, ny, nz = adj_ref.shape
    row, lane = iotas(ny, nz)
    for f in range(nf):
        xf_ref[f] = adj_ref[f, 0]
        zacc = jnp.zeros((ny, nz), F32)
        for x in range(nx):
            s = adj_ref[f, x]
            zacc = zacc + pltpu.roll(jnp.where(lane == 0, s, 0.0), x, 1)
        zf_ref[f] = zacc


def offset_terms(plus, minus, w):
    p0, p1, p2 = plus * w(0, 0), plus * w(0, 1), plus * w(0, 2)
    m0, m1, m2 = minus * w(1, 0), minus * w(1, 1), minus * w(1, 2)
    a = p1 + m2
    b = p2 + m1
    return [
        p0 * (1.0 / 3.0),
        p0 * (-7.0 / 6.0) + a * (-1.0 / 6.0),
        p0 * (11.0 / 6.0) + a * (5.0 / 6.0) + b * (1.0 / 3.0),
        a * (1.0 / 3.0) + b * (5.0 / 6.0) + m0 * (11.0 / 6.0),
        b * (-1.0 / 6.0) + m0 * (-7.0 / 6.0),
        m0 * (1.0 / 3.0),
    ]


def rolled_sum(terms, n, axis):
    r = {o: pltpu.roll(terms[o], (o - 2) % n, axis) for o in (0, 1, 3, 4, 5)}
    tot = terms[2] + r[0] + r[1] + r[3] + r[4] + r[5]
    return r, tot


def split_rows(terms, row8, ny):
    r, tot = rolled_sum(terms, ny, 0)
    h = ny - 8
    wr = (jnp.where(row8 < 1, r[3][0:8], 0.0) + jnp.where(row8 < 2, r[4][0:8], 0.0)
          + jnp.where(row8 < 3, r[5][0:8], 0.0))
    wl = jnp.where(row8 >= 6, r[0][h:ny], 0.0) + jnp.where(row8 >= 7, r[1][h:ny], 0.0)
    inner = jnp.concatenate([tot[0:8] - wr, tot[8:h], tot[h:ny] - wl], 0) if h > 8 else \
        jnp.concatenate([tot[0:8] - wr, tot[h:ny] - wl], 0)
    return inner, wr, wl


def split_lanes(terms, lane, nz):
    r, tot = rolled_sum(terms, nz, 1)
    wr = jnp.where(lane < 1, r[3], 0.0) + jnp.where(lane < 2, r[4], 0.0) + jnp.where(lane < 3, r[5], 0.0)
    wl = jnp.where(lane >= nz - 2, r[0], 0.0) + jnp.where(lane >= nz - 1, r[1], 0.0)
    return tot - wr - wl, wr, wl


def stencil_kernel(fp_ref, fm_ref, adj_ref, xf_ref, yf_ref, zf_ref, w_ref,
                   sec_ref, xl_ref, xr_ref, yl_ref, yr_ref, zz_ref, acc_ref):
    nf, nx, ny, nz = adj_ref.shape
    i = pl.program_id(0)
    row, lane = iotas(ny, nz)
    row8 = lax.broadcasted_iota(jnp.int32, (8, nz), 0)

    @pl.when(i == 0)
    def _():
        acc_ref[...] = jnp.zeros_like(acc_ref)
        zz_ref[...] = jnp.zeros_like(zz_ref)

    def flux(d, diff):
        plus, minus = [], []
        for f in range(nf):
            p = m = None
            for g in range(nf):
                tp = diff[g] * (STEP * fp_ref[d, g, f])
                tm = diff[g] * (STEP * fm_ref[d, g, f])
                p = tp if p is None else p + tp
                m = tm if m is None else m + tm
            plus.append(p)
            minus.append(m)
        return plus, minus

    yr_parts = {}
    yl_parts = {}
    for xl in range(XC):
        x = i * XC + xl
        last = x == nx - 1
        nxt = jnp.minimum(x + 1, nx - 1)
        a = [adj_ref[f, x] for f in range(nf)]
        plus, minus = flux(0, [jnp.where(last, xf_ref[g], adj_ref[g, nxt]) - a[g] for g in range(nf)])
        for f in range(nf):
            sx = offset_terms(plus[f], minus[f], lambda s, k: w_ref[0, s, k, f, xl])
            for o in range(6):
                acc_ref[f, x + o] = acc_ref[f, x + o] + sx[o]
        a = [adj_ref[f, x] for f in range(nf)]
        plus, minus = flux(1, [
            jnp.where(row == ny - 1, yf_ref[g, pl.ds(x, 1), :], pltpu.roll(a[g], ny - 1, 0)) - a[g]
            for g in range(nf)
        ])
        for f in range(nf):
            sy = offset_terms(plus[f], minus[f], lambda s, k: w_ref[1, s, k, f, xl])
            iy, wyr, wyl = split_rows(sy, row8, ny)
            acc_ref[f, x + 2] = acc_ref[f, x + 2] + iy
            rear = pltpu.roll(wyr, 4 * (xl % 2), 0)
            lead = pltpu.roll(wyl, (2 + 2 * (xl % 4)) % 8, 0)
            kr = (f, xl // 2)
            kl = (f, xl // 4)
            yr_parts[kr] = rear if kr not in yr_parts else yr_parts[kr] + rear
            yl_parts[kl] = lead if kl not in yl_parts else yl_parts[kl] + lead
        a = [adj_ref[f, x] for f in range(nf)]
        zshift = nz - 1 - x
        plus, minus = flux(2, [
            jnp.where(lane == nz - 1, pltpu.roll(zf_ref[g], zshift, 1), pltpu.roll(a[g], nz - 1, 1)) - a[g]
            for g in range(nf)
        ])
        for f in range(nf):
            sz = offset_terms(plus[f], minus[f], lambda s, k: w_ref[2, s, k, f, xl])
            iz, wzr, wzl = split_lanes(sz, lane, nz)
            acc_ref[f, x + 2] = acc_ref[f, x + 2] + iz
            zz_ref[0, f] = zz_ref[0, f] + pltpu.roll(wzl, 2 + 4 * x, 1)
            zz_ref[1, f] = zz_ref[1, f] + pltpu.roll(wzr, 4 * x, 1)
    for (f, t), v in yr_parts.items():
        yr_ref[f, t] = v
    for (f, t), v in yl_parts.items():
        yl_ref[f, t] = v

    @pl.when(i == pl.num_programs(0) - 1)
    def _():
        def body(x, c):
            for f in range(nf):
                sec_ref[f, x] = SECTION * (adj_ref[f, x] + acc_ref[f, x + 2])
            return c

        lax.fori_loop(0, nx, body, 0)
        for f in range(nf):
            xl_ref[f] = acc_ref[f, 0:2]
            xr_ref[f] = acc_ref[f, nx + 2:nx + 5]


def fix_kernel(row_ref, cnt_ref, sec_ref, axl_ref, axr_ref, ayl_ref, ayr_ref, az_ref,
               coef_ref, out_ref, wt_ref):
    nf, nx, ny, nz = sec_ref.shape
    row, lane = iotas(ny, nz)
    pad = jnp.zeros((ny - 8, nz), F32)
    for x in range(nx):
        for f in range(nf):
            ty = jnp.concatenate([ayr_ref[f, x // 2], pad], 0)
            add = jnp.where(row < 3, pltpu.roll(ty, (ny - 4 * (x % 2)) % ny, 0), 0.0)
            ty = jnp.concatenate([ayl_ref[f, x // 4], pad], 0)
            add = add + jnp.where(row >= ny - 2, pltpu.roll(ty, (ny - 2 - 2 * (x % 4)) % ny, 0), 0.0)
            add = add + jnp.where(lane < 3, pltpu.roll(az_ref[1, f], (nz - 4 * x) % nz, 1), 0.0)
            add = add + jnp.where(lane >= nz - 2, pltpu.roll(az_ref[0, f], (nz - 2 - 4 * x) % nz, 1), 0.0)
            if x < 3:
                add = add + axr_ref[f, x]
            if x >= nx - 2:
                add = add + axl_ref[f, x - (nx - 2)]
            out_ref[f, x] = sec_ref[f, x] + SECTION * add
    live_n = cnt_ref[0]
    for r in range(wt_ref.shape[0]):
        idx = row_ref[r]
        lx = idx // ny
        ly = idx % ny
        val = None
        for f in range(nf):
            v = out_ref[f, lx, pl.ds(ly, 1), :] * coef_ref[f, pl.ds(r, 1), :]
            val = v if val is None else val + v
        wt_ref[pl.ds(r, 1), :] = val * jnp.where(r < live_n, 1.0, 0.0).astype(F32)


def on_device(ndev, adjoint, stencil_weights, flux_plus, flux_minus, wall_row, wall_panel, wall_coef,
              wall_count, panel_owner):
    nf, nx, ny, nz = adjoint.shape
    assert nx % XC == 0 and XC % 4 == 0 and ny == 16 and nx * 4 <= nz
    ysl = adjoint[:, :, 0, :]
    yf = shift_from(ysl, "gy", -1)
    xf, zf = pl.pallas_call(
        fronts_kernel,
        out_shape=(
            jax.ShapeDtypeStruct((nf, ny, nz), F32),
            jax.ShapeDtypeStruct((nf, ny, nz), F32),
        ),
        in_specs=[VMEM, ANY],
        out_specs=(VMEM, VMEM),
    )(adjoint, ysl)
    xf = shift_from(xf, "gx", -1)
    zf = shift_from(zf, "gz", -1)
    const4 = lambda i: (0, 0, 0, 0)
    const3 = lambda i: (0, 0, 0)
    sec, xl, xr, yl, yr, zz = pl.pallas_call(
        stencil_kernel,
        grid=(nx // XC,),
        out_shape=(
            jax.ShapeDtypeStruct((nf, nx, ny, nz), F32),
            jax.ShapeDtypeStruct((nf, 2, ny, nz), F32),
            jax.ShapeDtypeStruct((nf, 3, ny, nz), F32),
            jax.ShapeDtypeStruct((nf, nx // 4, 8, nz), F32),
            jax.ShapeDtypeStruct((nf, nx // 2, 8, nz), F32),
            jax.ShapeDtypeStruct((2, nf, ny, nz), F32),
        ),
        in_specs=[
            SMEM,
            SMEM,
            pl.BlockSpec((nf, nx, ny, nz), const4),
            pl.BlockSpec((nf, ny, nz), const3),
            pl.BlockSpec((nf, nx, nz), const3),
            pl.BlockSpec((nf, ny, nz), const3),
            pl.BlockSpec((3, 2, 3, nf, XC, ny, nz), lambda i: (0, 0, 0, 0, i, 0, 0)),
        ],
        out_specs=(
            pl.BlockSpec((nf, nx, ny, nz), const4),
            pl.BlockSpec((nf, 2, ny, nz), const4),
            pl.BlockSpec((nf, 3, ny, nz), const4),
            pl.BlockSpec((nf, XC // 4, 8, nz), lambda i: (0, i, 0, 0)),
            pl.BlockSpec((nf, XC // 2, 8, nz), lambda i: (0, i, 0, 0)),
            pl.BlockSpec((2, nf, ny, nz), const4),
        ),
        scratch_shapes=[pltpu.VMEM((nf, nx + 5, ny, nz), F32)],
        compiler_params=pltpu.CompilerParams(dimension_semantics=("arbitrary",)),
    )(flux_plus, flux_minus, adjoint, xf, yf, zf, stencil_weights)
    axl = shift_from(xl, "gx", -1)
    axr = shift_from(xr, "gx", 1)
    ayl = shift_from(yl, "gy", -1)
    ayr = shift_from(yr, "gy", 1)
    if lax.axis_size("gz") == 2:
        az = shift_from(zz, "gz", 1)
    else:
        az = jnp.stack([shift_from(zz[0], "gz", -1), shift_from(zz[1], "gz", 1)])
    nr = wall_row.shape[0]
    section, wt = pl.pallas_call(
        fix_kernel,
        out_shape=(
            jax.ShapeDtypeStruct((nf, nx, ny, nz), F32),
            jax.ShapeDtypeStruct((nr, nz), F32),
        ),
        in_specs=[SMEM, SMEM] + [VMEM] * 7,
        out_specs=(VMEM, VMEM),
        input_output_aliases={2: 0},
    )(wall_row, wall_count, sec, axl, axr, ayl, ayr, az, wall_coef)

    npan = panel_owner.shape[0]
    per = npan // ndev
    nb = 32
    na = npan // nb
    own_oh = (panel_owner[:, None] == jnp.arange(ndev, dtype=jnp.int32)).astype(F32)
    oh3 = own_oh.reshape(na, nb, ndev)
    below_b = (jnp.arange(nb)[None, :] < jnp.arange(nb)[:, None]).astype(F32)
    below_a = (jnp.arange(na)[None, :] < jnp.arange(na)[:, None]).astype(F32)
    inner = jnp.einsum("bc,acd->abd", below_b, oh3, precision=HI)
    before = jnp.einsum("ac,cd->ad", below_a, jnp.sum(oh3, axis=1), precision=HI)
    rank = jnp.sum((inner + before[:, None, :]) * oh3, axis=2)
    oh_a = (wall_panel[..., None] // nb == jnp.arange(na, dtype=jnp.int32)).astype(F32)
    oh_b = (wall_panel[..., None] % nb == jnp.arange(nb, dtype=jnp.int32)).astype(F32)

    def lookup(table):
        picked = jnp.einsum("rza,ab->rzb", oh_a, table, precision=HI) * oh_b
        return jnp.round(jnp.sum(picked, axis=2)).astype(jnp.int32)

    cell_own = lookup(panel_owner.reshape(na, nb).astype(F32))
    cell_rank = lookup(rank)
    oh_o = (cell_own[..., None] == jnp.arange(ndev, dtype=jnp.int32)).astype(F32)
    oh_k = (cell_rank[..., None] == jnp.arange(per, dtype=jnp.int32)).astype(F32)
    t = jnp.einsum("rzo,rzk->ok", oh_o * wt[..., None], oh_k, precision=HI)
    got = lax.all_to_all(t, AXES, 0, 0, tiled=True)
    return section, jnp.sum(got, axis=0)


def solution(mesh):
    ndev = mesh.size
    placed = (
        P(None, "gx", "gy", "gz"),
        P(None, None, None, None, "gx", "gy", "gz"),
        P(),
        P(),
        P(AXES),
        P(AXES, None),
        P(None, AXES, None),
        P(AXES),
        P(),
    )
    return jax.shard_map(
        lambda *args: on_device(ndev, *args),
        mesh=mesh,
        in_specs=placed,
        out_specs=(P(None, "gx", "gy", "gz"), P(AXES)),
        check_vma=False,
    )
```

```python
import jax
import jax.numpy as jnp
from jax import lax
from jax.experimental import pallas as pl
from jax.experimental.pallas import tpu as pltpu
from jax.sharding import PartitionSpec as P

AXES = ("gx", "gy", "gz")
STEP = 0.4
SECTION = 0.25
XC = 8
F32 = jnp.float32
HI = lax.Precision.HIGHEST
VMEM = pl.BlockSpec(memory_space=pltpu.VMEM)
SMEM = pl.BlockSpec(memory_space=pltpu.SMEM)


def shift_from(x, axis, by):
    n = lax.axis_size(axis)
    return lax.ppermute(x, axis, [(i, (i + by) % n) for i in range(n)])


def iotas(ny, nz):
    return (
        lax.broadcasted_iota(jnp.int32, (ny, nz), 0),
        lax.broadcasted_iota(jnp.int32, (ny, nz), 1),
    )


def fronts_kernel(adj_ref, xf_ref, yf_ref, zf_ref):
    nf, nx, ny, nz = adj_ref.shape
    row, lane = iotas(ny, nz)
    for f in range(nf):
        xf_ref[f] = adj_ref[f, 0]
        zacc = jnp.zeros((ny, nz), F32)
        for x in range(nx):
            s = adj_ref[f, x]
            yf_ref[f, pl.ds(x, 1), :] = s[0:1, :]
            zacc = zacc + pltpu.roll(jnp.where(lane == 0, s, 0.0), x, 1)
        zf_ref[f] = zacc


def offset_terms(plus, minus, w):
    p0, p1, p2 = plus * w(0, 0), plus * w(0, 1), plus * w(0, 2)
    m0, m1, m2 = minus * w(1, 0), minus * w(1, 1), minus * w(1, 2)
    a = p1 + m2
    b = p2 + m1
    return [
        p0 * (1.0 / 3.0),
        p0 * (-7.0 / 6.0) + a * (-1.0 / 6.0),
        p0 * (11.0 / 6.0) + a * (5.0 / 6.0) + b * (1.0 / 3.0),
        a * (1.0 / 3.0) + b * (5.0 / 6.0) + m0 * (11.0 / 6.0),
        b * (-1.0 / 6.0) + m0 * (-7.0 / 6.0),
        m0 * (1.0 / 3.0),
    ]


def rolled_sum(terms, n, axis):
    r = {o: pltpu.roll(terms[o], (o - 2) % n, axis) for o in (0, 1, 3, 4, 5)}
    tot = terms[2] + r[0] + r[1] + r[3] + r[4] + r[5]
    return r, tot


def split_rows(terms, row8, ny):
    r, tot = rolled_sum(terms, ny, 0)
    h = ny - 8
    wr = (jnp.where(row8 < 1, r[3][0:8], 0.0) + jnp.where(row8 < 2, r[4][0:8], 0.0)
          + jnp.where(row8 < 3, r[5][0:8], 0.0))
    wl = jnp.where(row8 >= 6, r[0][h:ny], 0.0) + jnp.where(row8 >= 7, r[1][h:ny], 0.0)
    inner = jnp.concatenate([tot[0:8] - wr, tot[8:h], tot[h:ny] - wl], 0) if h > 8 else \
        jnp.concatenate([tot[0:8] - wr, tot[h:ny] - wl], 0)
    return inner, wr, wl


def split_lanes(terms, lane, nz):
    r, tot = rolled_sum(terms, nz, 1)
    wr = jnp.where(lane < 1, r[3], 0.0) + jnp.where(lane < 2, r[4], 0.0) + jnp.where(lane < 3, r[5], 0.0)
    wl = jnp.where(lane >= nz - 2, r[0], 0.0) + jnp.where(lane >= nz - 1, r[1], 0.0)
    return tot - wr - wl, wr, wl


def stencil_kernel(fp_ref, fm_ref, adj_ref, xf_ref, yf_ref, zf_ref, w_ref,
                   sec_ref, xl_ref, xr_ref, yl_ref, yr_ref, zz_ref, acc_ref):
    nf, nx, ny, nz = adj_ref.shape
    i = pl.program_id(0)
    row, lane = iotas(ny, nz)
    row8 = lax.broadcasted_iota(jnp.int32, (8, nz), 0)

    @pl.when(i == 0)
    def _():
        acc_ref[...] = jnp.zeros_like(acc_ref)
        zz_ref[...] = jnp.zeros_like(zz_ref)

    def flux(d, diff):
        plus, minus = [], []
        for f in range(nf):
            p = m = None
            for g in range(nf):
                tp = diff[g] * (STEP * fp_ref[d, g, f])
                tm = diff[g] * (STEP * fm_ref[d, g, f])
                p = tp if p is None else p + tp
                m = tm if m is None else m + tm
            plus.append(p)
            minus.append(m)
        return plus, minus

    yr_parts = {}
    yl_parts = {}
    for xl in range(XC):
        x = i * XC + xl
        last = x == nx - 1
        nxt = jnp.minimum(x + 1, nx - 1)
        a = [adj_ref[f, x] for f in range(nf)]
        plus, minus = flux(0, [jnp.where(last, xf_ref[g], adj_ref[g, nxt]) - a[g] for g in range(nf)])
        for f in range(nf):
            sx = offset_terms(plus[f], minus[f], lambda s, k: w_ref[0, s, k, f, xl])
            for o in range(6):
                acc_ref[f, x + o] = acc_ref[f, x + o] + sx[o]
        a = [adj_ref[f, x] for f in range(nf)]
        plus, minus = flux(1, [
            jnp.where(row == ny - 1, yf_ref[g, pl.ds(x, 1), :], pltpu.roll(a[g], ny - 1, 0)) - a[g]
            for g in range(nf)
        ])
        for f in range(nf):
            sy = offset_terms(plus[f], minus[f], lambda s, k: w_ref[1, s, k, f, xl])
            iy, wyr, wyl = split_rows(sy, row8, ny)
            acc_ref[f, x + 2] = acc_ref[f, x + 2] + iy
            rear = pltpu.roll(wyr, 4 * (xl % 2), 0)
            lead = pltpu.roll(wyl, (2 + 2 * (xl % 4)) % 8, 0)
            kr = (f, xl // 2)
            kl = (f, xl // 4)
            yr_parts[kr] = rear if kr not in yr_parts else yr_parts[kr] + rear
            yl_parts[kl] = lead if kl not in yl_parts else yl_parts[kl] + lead
        a = [adj_ref[f, x] for f in range(nf)]
        zshift = nz - 1 - x
        plus, minus = flux(2, [
            jnp.where(lane == nz - 1, pltpu.roll(zf_ref[g], zshift, 1), pltpu.roll(a[g], nz - 1, 1)) - a[g]
            for g in range(nf)
        ])
        for f in range(nf):
            sz = offset_terms(plus[f], minus[f], lambda s, k: w_ref[2, s, k, f, xl])
            iz, wzr, wzl = split_lanes(sz, lane, nz)
            acc_ref[f, x + 2] = acc_ref[f, x + 2] + iz
            zz_ref[0, f] = zz_ref[0, f] + pltpu.roll(wzl, 2 + 4 * x, 1)
            zz_ref[1, f] = zz_ref[1, f] + pltpu.roll(wzr, 4 * x, 1)
    for (f, t), v in yr_parts.items():
        yr_ref[f, t] = v
    for (f, t), v in yl_parts.items():
        yl_ref[f, t] = v

    @pl.when(i == pl.num_programs(0) - 1)
    def _():
        def body(x, c):
            for f in range(nf):
                sec_ref[f, x] = SECTION * (adj_ref[f, x] + acc_ref[f, x + 2])
            return c

        lax.fori_loop(0, nx, body, 0)
        for f in range(nf):
            xl_ref[f] = acc_ref[f, 0:2]
            xr_ref[f] = acc_ref[f, nx + 2:nx + 5]


def fix_kernel(row_ref, cnt_ref, sec_ref, axl_ref, axr_ref, ayl_ref, ayr_ref, az_ref,
               coef_ref, out_ref, wt_ref):
    nf, nx, ny, nz = sec_ref.shape
    row, lane = iotas(ny, nz)
    pad = jnp.zeros((ny - 8, nz), F32)
    for x in range(nx):
        for f in range(nf):
            ty = jnp.concatenate([ayr_ref[f, x // 2], pad], 0)
            add = jnp.where(row < 3, pltpu.roll(ty, (ny - 4 * (x % 2)) % ny, 0), 0.0)
            ty = jnp.concatenate([ayl_ref[f, x // 4], pad], 0)
            add = add + jnp.where(row >= ny - 2, pltpu.roll(ty, (ny - 2 - 2 * (x % 4)) % ny, 0), 0.0)
            add = add + jnp.where(lane < 3, pltpu.roll(az_ref[1, f], (nz - 4 * x) % nz, 1), 0.0)
            add = add + jnp.where(lane >= nz - 2, pltpu.roll(az_ref[0, f], (nz - 2 - 4 * x) % nz, 1), 0.0)
            if x < 3:
                add = add + axr_ref[f, x]
            if x >= nx - 2:
                add = add + axl_ref[f, x - (nx - 2)]
            out_ref[f, x] = sec_ref[f, x] + SECTION * add
    live_n = cnt_ref[0]
    for r in range(wt_ref.shape[0]):
        idx = row_ref[r]
        lx = idx // ny
        ly = idx % ny
        val = None
        for f in range(nf):
            v = out_ref[f, lx, pl.ds(ly, 1), :] * coef_ref[f, pl.ds(r, 1), :]
            val = v if val is None else val + v
        wt_ref[pl.ds(r, 1), :] = val * jnp.where(r < live_n, 1.0, 0.0).astype(F32)


def on_device(ndev, adjoint, stencil_weights, flux_plus, flux_minus, wall_row, wall_panel, wall_coef,
              wall_count, panel_owner):
    nf, nx, ny, nz = adjoint.shape
    assert nx % XC == 0 and XC % 4 == 0 and ny == 16 and nx * 4 <= nz
    xf, yf, zf = pl.pallas_call(
        fronts_kernel,
        out_shape=(
            jax.ShapeDtypeStruct((nf, ny, nz), F32),
            jax.ShapeDtypeStruct((nf, nx, nz), F32),
            jax.ShapeDtypeStruct((nf, ny, nz), F32),
        ),
        in_specs=[VMEM],
        out_specs=(VMEM, VMEM, VMEM),
    )(adjoint)
    xf = shift_from(xf, "gx", -1)
    yf = shift_from(yf, "gy", -1)
    zf = shift_from(zf, "gz", -1)
    const4 = lambda i: (0, 0, 0, 0)
    const3 = lambda i: (0, 0, 0)
    sec, xl, xr, yl, yr, zz = pl.pallas_call(
        stencil_kernel,
        grid=(nx // XC,),
        out_shape=(
            jax.ShapeDtypeStruct((nf, nx, ny, nz), F32),
            jax.ShapeDtypeStruct((nf, 2, ny, nz), F32),
            jax.ShapeDtypeStruct((nf, 3, ny, nz), F32),
            jax.ShapeDtypeStruct((nf, nx // 4, 8, nz), F32),
            jax.ShapeDtypeStruct((nf, nx // 2, 8, nz), F32),
            jax.ShapeDtypeStruct((2, nf, ny, nz), F32),
        ),
        in_specs=[
            SMEM,
            SMEM,
            pl.BlockSpec((nf, nx, ny, nz), const4),
            pl.BlockSpec((nf, ny, nz), const3),
            pl.BlockSpec((nf, nx, nz), const3),
            pl.BlockSpec((nf, ny, nz), const3),
            pl.BlockSpec((3, 2, 3, nf, XC, ny, nz), lambda i: (0, 0, 0, 0, i, 0, 0)),
        ],
        out_specs=(
            pl.BlockSpec((nf, nx, ny, nz), const4),
            pl.BlockSpec((nf, 2, ny, nz), const4),
            pl.BlockSpec((nf, 3, ny, nz), const4),
            pl.BlockSpec((nf, XC // 4, 8, nz), lambda i: (0, i, 0, 0)),
            pl.BlockSpec((nf, XC // 2, 8, nz), lambda i: (0, i, 0, 0)),
            pl.BlockSpec((2, nf, ny, nz), const4),
        ),
        scratch_shapes=[pltpu.VMEM((nf, nx + 5, ny, nz), F32)],
        compiler_params=pltpu.CompilerParams(dimension_semantics=("arbitrary",)),
    )(flux_plus, flux_minus, adjoint, xf, yf, zf, stencil_weights)
    axl = shift_from(xl, "gx", -1)
    axr = shift_from(xr, "gx", 1)
    ayl = shift_from(yl, "gy", -1)
    ayr = shift_from(yr, "gy", 1)
    if lax.axis_size("gz") == 2:
        az = shift_from(zz, "gz", 1)
    else:
        az = jnp.stack([shift_from(zz[0], "gz", -1), shift_from(zz[1], "gz", 1)])
    nr = wall_row.shape[0]
    section, wt = pl.pallas_call(
        fix_kernel,
        out_shape=(
            jax.ShapeDtypeStruct((nf, nx, ny, nz), F32),
            jax.ShapeDtypeStruct((nr, nz), F32),
        ),
        in_specs=[SMEM, SMEM] + [VMEM] * 7,
        out_specs=(VMEM, VMEM),
        input_output_aliases={2: 0},
    )(wall_row, wall_count, sec, axl, axr, ayl, ayr, az, wall_coef)

    npan = panel_owner.shape[0]
    per = npan // ndev
    nb = 32
    na = npan // nb
    own_oh = (panel_owner[:, None] == jnp.arange(ndev, dtype=jnp.int32)).astype(F32)
    oh3 = own_oh.reshape(na, nb, ndev)
    below_b = (jnp.arange(nb)[None, :] < jnp.arange(nb)[:, None]).astype(F32)
    below_a = (jnp.arange(na)[None, :] < jnp.arange(na)[:, None]).astype(F32)
    inner = jnp.einsum("bc,acd->abd", below_b, oh3, precision=HI)
    before = jnp.einsum("ac,cd->ad", below_a, jnp.sum(oh3, axis=1), precision=HI)
    rank = jnp.sum((inner + before[:, None, :]) * oh3, axis=2)
    oh_a = (wall_panel[..., None] // nb == jnp.arange(na, dtype=jnp.int32)).astype(F32)
    oh_b = (wall_panel[..., None] % nb == jnp.arange(nb, dtype=jnp.int32)).astype(F32)

    def lookup(table):
        picked = jnp.einsum("rza,ab->rzb", oh_a, table, precision=HI) * oh_b
        return jnp.round(jnp.sum(picked, axis=2)).astype(jnp.int32)

    cell_own = lookup(panel_owner.reshape(na, nb).astype(F32))
    cell_rank = lookup(rank)
    oh_o = (cell_own[..., None] == jnp.arange(ndev, dtype=jnp.int32)).astype(F32)
    oh_k = (cell_rank[..., None] == jnp.arange(per, dtype=jnp.int32)).astype(F32)
    t = jnp.einsum("rzo,rzk->ok", oh_o * wt[..., None], oh_k, precision=HI)
    got = lax.all_to_all(t, AXES, 0, 0, tiled=True)
    return section, jnp.sum(got, axis=0)


def solution(mesh):
    ndev = mesh.size
    placed = (
        P(None, "gx", "gy", "gz"),
        P(None, None, None, None, "gx", "gy", "gz"),
        P(),
        P(),
        P(AXES),
        P(AXES, None),
        P(None, AXES, None),
        P(AXES),
        P(),
    )
    return jax.shard_map(
        lambda *args: on_device(ndev, *args),
        mesh=mesh,
        in_specs=placed,
        out_specs=(P(None, "gx", "gy", "gz"), P(AXES)),
        check_vma=False,
    )
```

```python
import jax
import jax.numpy as jnp
from jax import lax
from jax.experimental import pallas as pl
from jax.experimental.pallas import tpu as pltpu
from jax.sharding import PartitionSpec as P

AXES = ("gx", "gy", "gz")
STEP = 0.4
SECTION = 0.25
XC = 4
F32 = jnp.float32
HI = lax.Precision.HIGHEST
VMEM = pl.BlockSpec(memory_space=pltpu.VMEM)
SMEM = pl.BlockSpec(memory_space=pltpu.SMEM)


def shift_from(x, axis, by):
    n = lax.axis_size(axis)
    return lax.ppermute(x, axis, [(i, (i + by) % n) for i in range(n)])


def iotas(ny, nz):
    return (
        lax.broadcasted_iota(jnp.int32, (ny, nz), 0),
        lax.broadcasted_iota(jnp.int32, (ny, nz), 1),
    )


def fronts_kernel(adj_ref, xf_ref, yf_ref, zf_ref):
    nf, nx, ny, nz = adj_ref.shape
    row, lane = iotas(ny, nz)
    for f in range(nf):
        xf_ref[f] = adj_ref[f, 0]
        zacc = jnp.zeros((ny, nz), F32)
        for x in range(nx):
            s = adj_ref[f, x]
            yf_ref[f, pl.ds(x, 1), :] = s[0:1, :]
            zacc = zacc + pltpu.roll(jnp.where(lane == 0, s, 0.0), x, 1)
        zf_ref[f] = zacc


def offset_terms(plus, minus, w):
    p0, p1, p2 = plus * w(0, 0), plus * w(0, 1), plus * w(0, 2)
    m0, m1, m2 = minus * w(1, 0), minus * w(1, 1), minus * w(1, 2)
    a = p1 + m2
    b = p2 + m1
    return [
        p0 * (1.0 / 3.0),
        p0 * (-7.0 / 6.0) + a * (-1.0 / 6.0),
        p0 * (11.0 / 6.0) + a * (5.0 / 6.0) + b * (1.0 / 3.0),
        a * (1.0 / 3.0) + b * (5.0 / 6.0) + m0 * (11.0 / 6.0),
        b * (-1.0 / 6.0) + m0 * (-7.0 / 6.0),
        m0 * (1.0 / 3.0),
    ]


def rolled_sum(terms, n, axis):
    r = {o: pltpu.roll(terms[o], (o - 2) % n, axis) for o in (0, 1, 3, 4, 5)}
    tot = terms[2] + r[0] + r[1] + r[3] + r[4] + r[5]
    return r, tot


def split_rows(terms, row8, ny):
    r, tot = rolled_sum(terms, ny, 0)
    h = ny - 8
    wr = (jnp.where(row8 < 1, r[3][0:8], 0.0) + jnp.where(row8 < 2, r[4][0:8], 0.0)
          + jnp.where(row8 < 3, r[5][0:8], 0.0))
    wl = jnp.where(row8 >= 6, r[0][h:ny], 0.0) + jnp.where(row8 >= 7, r[1][h:ny], 0.0)
    inner = jnp.concatenate([tot[0:8] - wr, tot[8:h], tot[h:ny] - wl], 0) if h > 8 else \
        jnp.concatenate([tot[0:8] - wr, tot[h:ny] - wl], 0)
    return inner, wr, wl


def split_lanes(terms, lane, nz):
    r, tot = rolled_sum(terms, nz, 1)
    wr = jnp.where(lane < 1, r[3], 0.0) + jnp.where(lane < 2, r[4], 0.0) + jnp.where(lane < 3, r[5], 0.0)
    wl = jnp.where(lane >= nz - 2, r[0], 0.0) + jnp.where(lane >= nz - 1, r[1], 0.0)
    return tot - wr - wl, wr, wl


def stencil_kernel(fp_ref, fm_ref, adj_ref, xf_ref, yf_ref, zf_ref, w_ref,
                   sec_ref, xl_ref, xr_ref, yl_ref, yr_ref, zz_ref, acc_ref):
    nf, nx, ny, nz = adj_ref.shape
    i = pl.program_id(0)
    row, lane = iotas(ny, nz)
    row8 = lax.broadcasted_iota(jnp.int32, (8, nz), 0)

    @pl.when(i == 0)
    def _():
        acc_ref[...] = jnp.zeros_like(acc_ref)
        zz_ref[...] = jnp.zeros_like(zz_ref)

    def flux(d, diff):
        plus, minus = [], []
        for f in range(nf):
            p = m = None
            for g in range(nf):
                tp = diff[g] * (STEP * fp_ref[d, g, f])
                tm = diff[g] * (STEP * fm_ref[d, g, f])
                p = tp if p is None else p + tp
                m = tm if m is None else m + tm
            plus.append(p)
            minus.append(m)
        return plus, minus

    yr_parts = {}
    yl_parts = {}
    for xl in range(XC):
        x = i * XC + xl
        last = x == nx - 1
        nxt = jnp.minimum(x + 1, nx - 1)
        a = [adj_ref[f, x] for f in range(nf)]
        plus, minus = flux(0, [jnp.where(last, xf_ref[g], adj_ref[g, nxt]) - a[g] for g in range(nf)])
        for f in range(nf):
            sx = offset_terms(plus[f], minus[f], lambda s, k: w_ref[0, s, k, f, xl])
            for o in range(6):
                acc_ref[f, x + o] = acc_ref[f, x + o] + sx[o]
        a = [adj_ref[f, x] for f in range(nf)]
        plus, minus = flux(1, [
            jnp.where(row == ny - 1, yf_ref[g, pl.ds(x, 1), :], pltpu.roll(a[g], ny - 1, 0)) - a[g]
            for g in range(nf)
        ])
        for f in range(nf):
            sy = offset_terms(plus[f], minus[f], lambda s, k: w_ref[1, s, k, f, xl])
            iy, wyr, wyl = split_rows(sy, row8, ny)
            acc_ref[f, x + 2] = acc_ref[f, x + 2] + iy
            rear = pltpu.roll(wyr, 4 * (xl % 2), 0)
            lead = pltpu.roll(wyl, (2 + 2 * (xl % 4)) % 8, 0)
            kr = (f, xl // 2)
            kl = (f, xl // 4)
            yr_parts[kr] = rear if kr not in yr_parts else yr_parts[kr] + rear
            yl_parts[kl] = lead if kl not in yl_parts else yl_parts[kl] + lead
        a = [adj_ref[f, x] for f in range(nf)]
        zshift = nz - 1 - x
        plus, minus = flux(2, [
            jnp.where(lane == nz - 1, pltpu.roll(zf_ref[g], zshift, 1), pltpu.roll(a[g], nz - 1, 1)) - a[g]
            for g in range(nf)
        ])
        for f in range(nf):
            sz = offset_terms(plus[f], minus[f], lambda s, k: w_ref[2, s, k, f, xl])
            iz, wzr, wzl = split_lanes(sz, lane, nz)
            acc_ref[f, x + 2] = acc_ref[f, x + 2] + iz
            zz_ref[0, f] = zz_ref[0, f] + pltpu.roll(wzl, 2 + 4 * x, 1)
            zz_ref[1, f] = zz_ref[1, f] + pltpu.roll(wzr, 4 * x, 1)
    for (f, t), v in yr_parts.items():
        yr_ref[f, t] = v
    for (f, t), v in yl_parts.items():
        yl_ref[f, t] = v

    @pl.when(i == pl.num_programs(0) - 1)
    def _():
        def body(x, c):
            for f in range(nf):
                sec_ref[f, x] = SECTION * (adj_ref[f, x] + acc_ref[f, x + 2])
            return c

        lax.fori_loop(0, nx, body, 0)
        for f in range(nf):
            xl_ref[f] = acc_ref[f, 0:2]
            xr_ref[f] = acc_ref[f, nx + 2:nx + 5]


def fix_kernel(row_ref, cnt_ref, sec_ref, axl_ref, axr_ref, ayl_ref, ayr_ref, az_ref,
               coef_ref, out_ref, wt_ref):
    nf, _, ny, nz = sec_ref.shape
    i = pl.program_id(0)
    last = pl.num_programs(0) - 1
    row, lane = iotas(ny, nz)
    pad = jnp.zeros((ny - 8, nz), F32)
    for xl in range(XC):
        x = i * XC + xl
        zr_shift = lax.rem(nz - 4 * x, nz)
        zl_shift = lax.rem(2 * nz - 2 - 4 * x, nz)
        for f in range(nf):
            ty = jnp.concatenate([ayr_ref[f, xl // 2], pad], 0)
            add = jnp.where(row < 3, pltpu.roll(ty, (ny - 4 * (xl % 2)) % ny, 0), 0.0)
            ty = jnp.concatenate([ayl_ref[f, xl // 4], pad], 0)
            add = add + jnp.where(row >= ny - 2, pltpu.roll(ty, (ny - 2 - 2 * (xl % 4)) % ny, 0), 0.0)
            add = add + jnp.where(lane < 3, pltpu.roll(az_ref[1, f], zr_shift, 1), 0.0)
            add = add + jnp.where(lane >= nz - 2, pltpu.roll(az_ref[0, f], zl_shift, 1), 0.0)
            if xl < 3:
                add = add + jnp.where(i == 0, axr_ref[f, xl], 0.0)
            if xl >= XC - 2:
                add = add + jnp.where(i == last, axl_ref[f, xl - (XC - 2)], 0.0)
            out_ref[f, xl] = sec_ref[f, xl] + SECTION * add
    live_n = cnt_ref[0]
    for r in range(wt_ref.shape[0]):
        idx = row_ref[r]
        lx = idx // ny
        ly = idx % ny

        @pl.when(lx // XC == i)
        def _():
            val = None
            for f in range(nf):
                v = out_ref[f, lx % XC, pl.ds(ly, 1), :] * coef_ref[f, pl.ds(r, 1), :]
                val = v if val is None else val + v
            wt_ref[pl.ds(r, 1), :] = val * jnp.where(r < live_n, 1.0, 0.0).astype(F32)


def on_device(ndev, adjoint, stencil_weights, flux_plus, flux_minus, wall_row, wall_panel, wall_coef,
              wall_count, panel_owner):
    nf, nx, ny, nz = adjoint.shape
    assert nx % XC == 0 and XC % 4 == 0 and ny == 16 and nx * 4 <= nz
    xf, yf, zf = pl.pallas_call(
        fronts_kernel,
        out_shape=(
            jax.ShapeDtypeStruct((nf, ny, nz), F32),
            jax.ShapeDtypeStruct((nf, nx, nz), F32),
            jax.ShapeDtypeStruct((nf, ny, nz), F32),
        ),
        in_specs=[VMEM],
        out_specs=(VMEM, VMEM, VMEM),
    )(adjoint)
    xf = shift_from(xf, "gx", -1)
    yf = shift_from(yf, "gy", -1)
    zf = shift_from(zf, "gz", -1)
    const4 = lambda i: (0, 0, 0, 0)
    const3 = lambda i: (0, 0, 0)
    sec, xl, xr, yl, yr, zz = pl.pallas_call(
        stencil_kernel,
        grid=(nx // XC,),
        out_shape=(
            jax.ShapeDtypeStruct((nf, nx, ny, nz), F32),
            jax.ShapeDtypeStruct((nf, 2, ny, nz), F32),
            jax.ShapeDtypeStruct((nf, 3, ny, nz), F32),
            jax.ShapeDtypeStruct((nf, nx // 4, 8, nz), F32),
            jax.ShapeDtypeStruct((nf, nx // 2, 8, nz), F32),
            jax.ShapeDtypeStruct((2, nf, ny, nz), F32),
        ),
        in_specs=[
            SMEM,
            SMEM,
            pl.BlockSpec((nf, nx, ny, nz), const4),
            pl.BlockSpec((nf, ny, nz), const3),
            pl.BlockSpec((nf, nx, nz), const3),
            pl.BlockSpec((nf, ny, nz), const3),
            pl.BlockSpec((3, 2, 3, nf, XC, ny, nz), lambda i: (0, 0, 0, 0, i, 0, 0)),
        ],
        out_specs=(
            pl.BlockSpec((nf, nx, ny, nz), const4),
            pl.BlockSpec((nf, 2, ny, nz), const4),
            pl.BlockSpec((nf, 3, ny, nz), const4),
            pl.BlockSpec((nf, XC // 4, 8, nz), lambda i: (0, i, 0, 0)),
            pl.BlockSpec((nf, XC // 2, 8, nz), lambda i: (0, i, 0, 0)),
            pl.BlockSpec((2, nf, ny, nz), const4),
        ),
        scratch_shapes=[pltpu.VMEM((nf, nx + 5, ny, nz), F32)],
        compiler_params=pltpu.CompilerParams(dimension_semantics=("arbitrary",)),
    )(flux_plus, flux_minus, adjoint, xf, yf, zf, stencil_weights)
    axl = shift_from(xl, "gx", -1)
    axr = shift_from(xr, "gx", 1)
    ayl = shift_from(yl, "gy", -1)
    ayr = shift_from(yr, "gy", 1)
    if lax.axis_size("gz") == 2:
        az = shift_from(zz, "gz", 1)
    else:
        az = jnp.stack([shift_from(zz[0], "gz", -1), shift_from(zz[1], "gz", 1)])
    nr = wall_row.shape[0]
    section, wt = pl.pallas_call(
        fix_kernel,
        grid=(nx // XC,),
        out_shape=(
            jax.ShapeDtypeStruct((nf, nx, ny, nz), F32),
            jax.ShapeDtypeStruct((nr, nz), F32),
        ),
        in_specs=[
            SMEM,
            SMEM,
            pl.BlockSpec((nf, XC, ny, nz), lambda i: (0, i, 0, 0)),
            pl.BlockSpec((nf, 2, ny, nz), const4),
            pl.BlockSpec((nf, 3, ny, nz), const4),
            pl.BlockSpec((nf, XC // 4, 8, nz), lambda i: (0, i, 0, 0)),
            pl.BlockSpec((nf, XC // 2, 8, nz), lambda i: (0, i, 0, 0)),
            pl.BlockSpec((2, nf, ny, nz), const4),
            pl.BlockSpec((nf, nr, nz), const3),
        ],
        out_specs=(
            pl.BlockSpec((nf, XC, ny, nz), lambda i: (0, i, 0, 0)),
            pl.BlockSpec((nr, nz), lambda i: (0, 0)),
        ),
        input_output_aliases={2: 0},
        compiler_params=pltpu.CompilerParams(dimension_semantics=("arbitrary",)),
    )(wall_row, wall_count, sec, axl, axr, ayl, ayr, az, wall_coef)

    npan = panel_owner.shape[0]
    per = npan // ndev
    nb = 32
    na = npan // nb
    own_oh = (panel_owner[:, None] == jnp.arange(ndev, dtype=jnp.int32)).astype(F32)
    oh3 = own_oh.reshape(na, nb, ndev)
    below_b = (jnp.arange(nb)[None, :] < jnp.arange(nb)[:, None]).astype(F32)
    below_a = (jnp.arange(na)[None, :] < jnp.arange(na)[:, None]).astype(F32)
    inner = jnp.einsum("bc,acd->abd", below_b, oh3, precision=HI)
    before = jnp.einsum("ac,cd->ad", below_a, jnp.sum(oh3, axis=1), precision=HI)
    rank = jnp.sum((inner + before[:, None, :]) * oh3, axis=2)
    oh_a = (wall_panel[..., None] // nb == jnp.arange(na, dtype=jnp.int32)).astype(F32)
    oh_b = (wall_panel[..., None] % nb == jnp.arange(nb, dtype=jnp.int32)).astype(F32)

    def lookup(table):
        picked = jnp.einsum("rza,ab->rzb", oh_a, table, precision=HI) * oh_b
        return jnp.round(jnp.sum(picked, axis=2)).astype(jnp.int32)

    cell_own = lookup(panel_owner.reshape(na, nb).astype(F32))
    cell_rank = lookup(rank)
    oh_o = (cell_own[..., None] == jnp.arange(ndev, dtype=jnp.int32)).astype(F32)
    oh_k = (cell_rank[..., None] == jnp.arange(per, dtype=jnp.int32)).astype(F32)
    t = jnp.einsum("rzo,rzk->ok", oh_o * wt[..., None], oh_k, precision=HI)
    got = lax.all_to_all(t, AXES, 0, 0, tiled=True)
    return section, jnp.sum(got, axis=0)


def solution(mesh):
    ndev = mesh.size
    placed = (
        P(None, "gx", "gy", "gz"),
        P(None, None, None, None, "gx", "gy", "gz"),
        P(),
        P(),
        P(AXES),
        P(AXES, None),
        P(None, AXES, None),
        P(AXES),
        P(),
    )
    return jax.shard_map(
        lambda *args: on_device(ndev, *args),
        mesh=mesh,
        in_specs=placed,
        out_specs=(P(None, "gx", "gy", "gz"), P(AXES)),
        check_vma=False,
    )
```

```python
import jax
import jax.numpy as jnp
from jax import lax
from jax.experimental import pallas as pl
from jax.experimental.pallas import tpu as pltpu
from jax.sharding import PartitionSpec as P

AXES = ("gx", "gy", "gz")
STEP = 0.4
SECTION = 0.25
XC = 4
F32 = jnp.float32
HI = lax.Precision.HIGHEST
VMEM = pl.BlockSpec(memory_space=pltpu.VMEM)
SMEM = pl.BlockSpec(memory_space=pltpu.SMEM)


def shift_from(x, axis, by):
    n = lax.axis_size(axis)
    return lax.ppermute(x, axis, [(i, (i + by) % n) for i in range(n)])


def iotas(ny, nz):
    return (
        lax.broadcasted_iota(jnp.int32, (ny, nz), 0),
        lax.broadcasted_iota(jnp.int32, (ny, nz), 1),
    )


def fronts_kernel(adj_ref, xf_ref, yf_ref, zf_ref):
    nf, nx, ny, nz = adj_ref.shape
    row, lane = iotas(ny, nz)
    for f in range(nf):
        xf_ref[f] = adj_ref[f, 0]
        zacc = jnp.zeros((ny, nz), F32)
        for x in range(nx):
            s = adj_ref[f, x]
            yf_ref[f, pl.ds(x, 1), :] = s[0:1, :]
            zacc = zacc + pltpu.roll(jnp.where(lane == 0, s, 0.0), x, 1)
        zf_ref[f] = zacc


def offset_terms(plus, minus, w):
    p0, p1, p2 = plus * w(0, 0), plus * w(0, 1), plus * w(0, 2)
    m0, m1, m2 = minus * w(1, 0), minus * w(1, 1), minus * w(1, 2)
    a = p1 + m2
    b = p2 + m1
    return [
        p0 * (1.0 / 3.0),
        p0 * (-7.0 / 6.0) + a * (-1.0 / 6.0),
        p0 * (11.0 / 6.0) + a * (5.0 / 6.0) + b * (1.0 / 3.0),
        a * (1.0 / 3.0) + b * (5.0 / 6.0) + m0 * (11.0 / 6.0),
        b * (-1.0 / 6.0) + m0 * (-7.0 / 6.0),
        m0 * (1.0 / 3.0),
    ]


def rolled_sum(terms, n, axis):
    r = {o: pltpu.roll(terms[o], (o - 2) % n, axis) for o in (0, 1, 3, 4, 5)}
    tot = terms[2] + r[0] + r[1] + r[3] + r[4] + r[5]
    return r, tot


def split_rows(terms, row8, ny):
    r, tot = rolled_sum(terms, ny, 0)
    h = ny - 8
    wr = (jnp.where(row8 < 1, r[3][0:8], 0.0) + jnp.where(row8 < 2, r[4][0:8], 0.0)
          + jnp.where(row8 < 3, r[5][0:8], 0.0))
    wl = jnp.where(row8 >= 6, r[0][h:ny], 0.0) + jnp.where(row8 >= 7, r[1][h:ny], 0.0)
    inner = jnp.concatenate([tot[0:8] - wr, tot[8:h], tot[h:ny] - wl], 0) if h > 8 else \
        jnp.concatenate([tot[0:8] - wr, tot[h:ny] - wl], 0)
    return inner, wr, wl


def split_lanes(terms, lane, nz):
    r, tot = rolled_sum(terms, nz, 1)
    wr = jnp.where(lane < 1, r[3], 0.0) + jnp.where(lane < 2, r[4], 0.0) + jnp.where(lane < 3, r[5], 0.0)
    wl = jnp.where(lane >= nz - 2, r[0], 0.0) + jnp.where(lane >= nz - 1, r[1], 0.0)
    return tot - wr - wl, wr, wl


def stencil_kernel(fp_ref, fm_ref, adj_ref, adjn_ref, xf_ref, yf_ref, zf_ref, w_ref,
                   sec_ref, xl_ref, xr_ref, yl_ref, yr_ref, zz_ref, acc_ref):
    nf, nx, ny, nz = sec_ref.shape
    i = pl.program_id(0)
    row, lane = iotas(ny, nz)
    row8 = lax.broadcasted_iota(jnp.int32, (8, nz), 0)

    @pl.when(i == 0)
    def _():
        acc_ref[...] = jnp.zeros_like(acc_ref)
        zz_ref[...] = jnp.zeros_like(zz_ref)

    def flux(d, diff):
        plus, minus = [], []
        for f in range(nf):
            p = m = None
            for g in range(nf):
                tp = diff[g] * (STEP * fp_ref[d, g, f])
                tm = diff[g] * (STEP * fm_ref[d, g, f])
                p = tp if p is None else p + tp
                m = tm if m is None else m + tm
            plus.append(p)
            minus.append(m)
        return plus, minus

    yr_parts = {}
    yl_parts = {}
    for xl in range(XC):
        x = i * XC + xl
        a = [adj_ref[f, xl] for f in range(nf)]
        if xl < XC - 1:
            an_x = [adj_ref[g, xl + 1] for g in range(nf)]
        else:
            last = i == pl.num_programs(0) - 1
            an_x = [jnp.where(last, xf_ref[g], adjn_ref[g, 0]) for g in range(nf)]
        plus, minus = flux(0, [an_x[g] - a[g] for g in range(nf)])
        for f in range(nf):
            sx = offset_terms(plus[f], minus[f], lambda s, k: w_ref[0, s, k, f, xl])
            for o in range(6):
                acc_ref[f, x + o] = acc_ref[f, x + o] + sx[o]
        a = [adj_ref[f, xl] for f in range(nf)]
        plus, minus = flux(1, [
            jnp.where(row == ny - 1, yf_ref[g, pl.ds(x, 1), :], pltpu.roll(a[g], ny - 1, 0)) - a[g]
            for g in range(nf)
        ])
        for f in range(nf):
            sy = offset_terms(plus[f], minus[f], lambda s, k: w_ref[1, s, k, f, xl])
            iy, wyr, wyl = split_rows(sy, row8, ny)
            acc_ref[f, x + 2] = acc_ref[f, x + 2] + (iy + adj_ref[f, xl])
            rear = pltpu.roll(wyr, 4 * (xl % 2), 0)
            lead = pltpu.roll(wyl, (2 + 2 * (xl % 4)) % 8, 0)
            kr = (f, xl // 2)
            kl = (f, xl // 4)
            yr_parts[kr] = rear if kr not in yr_parts else yr_parts[kr] + rear
            yl_parts[kl] = lead if kl not in yl_parts else yl_parts[kl] + lead
        a = [adj_ref[f, xl] for f in range(nf)]
        zshift = nz - 1 - x
        plus, minus = flux(2, [
            jnp.where(lane == nz - 1, pltpu.roll(zf_ref[g], zshift, 1), pltpu.roll(a[g], nz - 1, 1)) - a[g]
            for g in range(nf)
        ])
        for f in range(nf):
            sz = offset_terms(plus[f], minus[f], lambda s, k: w_ref[2, s, k, f, xl])
            iz, wzr, wzl = split_lanes(sz, lane, nz)
            acc_ref[f, x + 2] = acc_ref[f, x + 2] + iz
            zz_ref[0, f] = zz_ref[0, f] + pltpu.roll(wzl, 2 + 4 * x, 1)
            zz_ref[1, f] = zz_ref[1, f] + pltpu.roll(wzr, 4 * x, 1)
    for (f, t), v in yr_parts.items():
        yr_ref[f, t] = v
    for (f, t), v in yl_parts.items():
        yl_ref[f, t] = v

    @pl.when(i == pl.num_programs(0) - 1)
    def _():
        def body(x, c):
            for f in range(nf):
                sec_ref[f, x] = SECTION * acc_ref[f, x + 2]
            return c

        lax.fori_loop(0, nx, body, 0)
        for f in range(nf):
            xl_ref[f] = acc_ref[f, 0:2]
            xr_ref[f] = acc_ref[f, nx + 2:nx + 5]


def fix_kernel(row_ref, cnt_ref, sec_ref, axl_ref, axr_ref, ayl_ref, ayr_ref, az_ref,
               coef_ref, out_ref, wt_ref):
    nf, nx, ny, nz = sec_ref.shape
    row, lane = iotas(ny, nz)
    pad = jnp.zeros((ny - 8, nz), F32)
    for x in range(nx):
        for f in range(nf):
            ty = jnp.concatenate([ayr_ref[f, x // 2], pad], 0)
            add = jnp.where(row < 3, pltpu.roll(ty, (ny - 4 * (x % 2)) % ny, 0), 0.0)
            ty = jnp.concatenate([ayl_ref[f, x // 4], pad], 0)
            add = add + jnp.where(row >= ny - 2, pltpu.roll(ty, (ny - 2 - 2 * (x % 4)) % ny, 0), 0.0)
            add = add + jnp.where(lane < 3, pltpu.roll(az_ref[1, f], (nz - 4 * x) % nz, 1), 0.0)
            add = add + jnp.where(lane >= nz - 2, pltpu.roll(az_ref[0, f], (nz - 2 - 4 * x) % nz, 1), 0.0)
            if x < 3:
                add = add + axr_ref[f, x]
            if x >= nx - 2:
                add = add + axl_ref[f, x - (nx - 2)]
            out_ref[f, x] = sec_ref[f, x] + SECTION * add
    live_n = cnt_ref[0]
    for r in range(wt_ref.shape[0]):
        idx = row_ref[r]
        lx = idx // ny
        ly = idx % ny
        val = None
        for f in range(nf):
            v = out_ref[f, lx, pl.ds(ly, 1), :] * coef_ref[f, pl.ds(r, 1), :]
            val = v if val is None else val + v
        wt_ref[pl.ds(r, 1), :] = val * jnp.where(r < live_n, 1.0, 0.0).astype(F32)


def on_device(ndev, adjoint, stencil_weights, flux_plus, flux_minus, wall_row, wall_panel, wall_coef,
              wall_count, panel_owner):
    nf, nx, ny, nz = adjoint.shape
    assert nx % XC == 0 and XC % 4 == 0 and ny == 16 and nx * 4 <= nz
    xf, yf, zf = pl.pallas_call(
        fronts_kernel,
        out_shape=(
            jax.ShapeDtypeStruct((nf, ny, nz), F32),
            jax.ShapeDtypeStruct((nf, nx, nz), F32),
            jax.ShapeDtypeStruct((nf, ny, nz), F32),
        ),
        in_specs=[VMEM],
        out_specs=(VMEM, VMEM, VMEM),
    )(adjoint)
    xf = shift_from(xf, "gx", -1)
    yf = shift_from(yf, "gy", -1)
    zf = shift_from(zf, "gz", -1)
    const4 = lambda i: (0, 0, 0, 0)
    const3 = lambda i: (0, 0, 0)
    sec, xl, xr, yl, yr, zz = pl.pallas_call(
        stencil_kernel,
        grid=(nx // XC,),
        out_shape=(
            jax.ShapeDtypeStruct((nf, nx, ny, nz), F32),
            jax.ShapeDtypeStruct((nf, 2, ny, nz), F32),
            jax.ShapeDtypeStruct((nf, 3, ny, nz), F32),
            jax.ShapeDtypeStruct((nf, nx // 4, 8, nz), F32),
            jax.ShapeDtypeStruct((nf, nx // 2, 8, nz), F32),
            jax.ShapeDtypeStruct((2, nf, ny, nz), F32),
        ),
        in_specs=[
            SMEM,
            SMEM,
            pl.BlockSpec((nf, XC, ny, nz), lambda i: (0, i, 0, 0)),
            pl.BlockSpec((nf, 1, ny, nz), lambda i: (0, jnp.minimum((i + 1) * XC, nx - 1), 0, 0)),
            pl.BlockSpec((nf, ny, nz), const3),
            pl.BlockSpec((nf, nx, nz), const3),
            pl.BlockSpec((nf, ny, nz), const3),
            pl.BlockSpec((3, 2, 3, nf, XC, ny, nz), lambda i: (0, 0, 0, 0, i, 0, 0)),
        ],
        out_specs=(
            pl.BlockSpec((nf, nx, ny, nz), const4),
            pl.BlockSpec((nf, 2, ny, nz), const4),
            pl.BlockSpec((nf, 3, ny, nz), const4),
            pl.BlockSpec((nf, XC // 4, 8, nz), lambda i: (0, i, 0, 0)),
            pl.BlockSpec((nf, XC // 2, 8, nz), lambda i: (0, i, 0, 0)),
            pl.BlockSpec((2, nf, ny, nz), const4),
        ),
        scratch_shapes=[pltpu.VMEM((nf, nx + 5, ny, nz), F32)],
        compiler_params=pltpu.CompilerParams(dimension_semantics=("arbitrary",)),
    )(flux_plus, flux_minus, adjoint, adjoint, xf, yf, zf, stencil_weights)
    axl = shift_from(xl, "gx", -1)
    axr = shift_from(xr, "gx", 1)
    ayl = shift_from(yl, "gy", -1)
    ayr = shift_from(yr, "gy", 1)
    if lax.axis_size("gz") == 2:
        az = shift_from(zz, "gz", 1)
    else:
        az = jnp.stack([shift_from(zz[0], "gz", -1), shift_from(zz[1], "gz", 1)])
    nr = wall_row.shape[0]
    section, wt = pl.pallas_call(
        fix_kernel,
        out_shape=(
            jax.ShapeDtypeStruct((nf, nx, ny, nz), F32),
            jax.ShapeDtypeStruct((nr, nz), F32),
        ),
        in_specs=[SMEM, SMEM] + [VMEM] * 7,
        out_specs=(VMEM, VMEM),
        input_output_aliases={2: 0},
    )(wall_row, wall_count, sec, axl, axr, ayl, ayr, az, wall_coef)

    npan = panel_owner.shape[0]
    per = npan // ndev
    nb = 32
    na = npan // nb
    own_oh = (panel_owner[:, None] == jnp.arange(ndev, dtype=jnp.int32)).astype(F32)
    oh3 = own_oh.reshape(na, nb, ndev)
    below_b = (jnp.arange(nb)[None, :] < jnp.arange(nb)[:, None]).astype(F32)
    below_a = (jnp.arange(na)[None, :] < jnp.arange(na)[:, None]).astype(F32)
    inner = jnp.einsum("bc,acd->abd", below_b, oh3, precision=HI)
    before = jnp.einsum("ac,cd->ad", below_a, jnp.sum(oh3, axis=1), precision=HI)
    rank = jnp.sum((inner + before[:, None, :]) * oh3, axis=2)
    oh_a = (wall_panel[..., None] // nb == jnp.arange(na, dtype=jnp.int32)).astype(F32)
    oh_b = (wall_panel[..., None] % nb == jnp.arange(nb, dtype=jnp.int32)).astype(F32)

    def lookup(table):
        picked = jnp.einsum("rza,ab->rzb", oh_a, table, precision=HI) * oh_b
        return jnp.round(jnp.sum(picked, axis=2)).astype(jnp.int32)

    cell_own = lookup(panel_owner.reshape(na, nb).astype(F32))
    cell_rank = lookup(rank)
    oh_o = (cell_own[..., None] == jnp.arange(ndev, dtype=jnp.int32)).astype(F32)
    oh_k = (cell_rank[..., None] == jnp.arange(per, dtype=jnp.int32)).astype(F32)
    t = jnp.einsum("rzo,rzk->ok", oh_o * wt[..., None], oh_k, precision=HI)
    got = lax.all_to_all(t, AXES, 0, 0, tiled=True)
    return section, jnp.sum(got, axis=0)


def solution(mesh):
    ndev = mesh.size
    placed = (
        P(None, "gx", "gy", "gz"),
        P(None, None, None, None, "gx", "gy", "gz"),
        P(),
        P(),
        P(AXES),
        P(AXES, None),
        P(None, AXES, None),
        P(AXES),
        P(),
    )
    return jax.shard_map(
        lambda *args: on_device(ndev, *args),
        mesh=mesh,
        in_specs=placed,
        out_specs=(P(None, "gx", "gy", "gz"), P(AXES)),
        check_vma=False,
    )
```

```python
import jax
import jax.numpy as jnp
from jax import lax
from jax.experimental import pallas as pl
from jax.experimental.pallas import tpu as pltpu
from jax.sharding import PartitionSpec as P

AXES = ("gx", "gy", "gz")
STEP = 0.4
SECTION = 0.25
XC = 4
F32 = jnp.float32
HI = lax.Precision.HIGHEST
VMEM = pl.BlockSpec(memory_space=pltpu.VMEM)
SMEM = pl.BlockSpec(memory_space=pltpu.SMEM)


def shift_from(x, axis, by):
    n = lax.axis_size(axis)
    return lax.ppermute(x, axis, [(i, (i + by) % n) for i in range(n)])


def iotas(ny, nz):
    return (
        lax.broadcasted_iota(jnp.int32, (ny, nz), 0),
        lax.broadcasted_iota(jnp.int32, (ny, nz), 1),
    )


def fronts_kernel(adj_ref, xf_ref, yf_ref, zf_ref):
    _, nx, ny, nz = adj_ref.shape
    row, lane = iotas(ny, nz)
    xf_ref[0] = adj_ref[0, 0]
    zacc = jnp.zeros((ny, nz), F32)
    for x in range(nx):
        s = adj_ref[0, x]
        yf_ref[0, pl.ds(x, 1), :] = s[0:1, :]
        zacc = zacc + pltpu.roll(jnp.where(lane == 0, s, 0.0), x, 1)
    zf_ref[0] = zacc


def offset_terms(plus, minus, w):
    p0, p1, p2 = plus * w(0, 0), plus * w(0, 1), plus * w(0, 2)
    m0, m1, m2 = minus * w(1, 0), minus * w(1, 1), minus * w(1, 2)
    a = p1 + m2
    b = p2 + m1
    return [
        p0 * (1.0 / 3.0),
        p0 * (-7.0 / 6.0) + a * (-1.0 / 6.0),
        p0 * (11.0 / 6.0) + a * (5.0 / 6.0) + b * (1.0 / 3.0),
        a * (1.0 / 3.0) + b * (5.0 / 6.0) + m0 * (11.0 / 6.0),
        b * (-1.0 / 6.0) + m0 * (-7.0 / 6.0),
        m0 * (1.0 / 3.0),
    ]


def rolled_sum(terms, n, axis):
    r = {o: pltpu.roll(terms[o], (o - 2) % n, axis) for o in (0, 1, 3, 4, 5)}
    tot = terms[2] + r[0] + r[1] + r[3] + r[4] + r[5]
    return r, tot


def split_rows(terms, row8, ny):
    r, tot = rolled_sum(terms, ny, 0)
    h = ny - 8
    wr = (jnp.where(row8 < 1, r[3][0:8], 0.0) + jnp.where(row8 < 2, r[4][0:8], 0.0)
          + jnp.where(row8 < 3, r[5][0:8], 0.0))
    wl = jnp.where(row8 >= 6, r[0][h:ny], 0.0) + jnp.where(row8 >= 7, r[1][h:ny], 0.0)
    inner = jnp.concatenate([tot[0:8] - wr, tot[8:h], tot[h:ny] - wl], 0) if h > 8 else \
        jnp.concatenate([tot[0:8] - wr, tot[h:ny] - wl], 0)
    return inner, wr, wl


def split_lanes(terms, lane, nz):
    r, tot = rolled_sum(terms, nz, 1)
    wr = jnp.where(lane < 1, r[3], 0.0) + jnp.where(lane < 2, r[4], 0.0) + jnp.where(lane < 3, r[5], 0.0)
    wl = jnp.where(lane >= nz - 2, r[0], 0.0) + jnp.where(lane >= nz - 1, r[1], 0.0)
    return tot - wr - wl, wr, wl


def stencil_kernel(fp_ref, fm_ref, adj_ref, xf_ref, yf_ref, zf_ref, w_ref,
                   sec_ref, xl_ref, xr_ref, yl_ref, yr_ref, zz_ref, acc_ref):
    nf, nx, ny, nz = adj_ref.shape
    i = pl.program_id(0)
    row, lane = iotas(ny, nz)
    row8 = lax.broadcasted_iota(jnp.int32, (8, nz), 0)

    @pl.when(i == 0)
    def _():
        acc_ref[...] = jnp.zeros_like(acc_ref)
        zz_ref[...] = jnp.zeros_like(zz_ref)

    def flux(d, diff):
        plus, minus = [], []
        for f in range(nf):
            p = m = None
            for g in range(nf):
                tp = diff[g] * (STEP * fp_ref[d, g, f])
                tm = diff[g] * (STEP * fm_ref[d, g, f])
                p = tp if p is None else p + tp
                m = tm if m is None else m + tm
            plus.append(p)
            minus.append(m)
        return plus, minus

    yr_parts = {}
    yl_parts = {}
    for xl in range(XC):
        x = i * XC + xl
        last = x == nx - 1
        nxt = jnp.minimum(x + 1, nx - 1)
        a = [adj_ref[f, x] for f in range(nf)]
        plus, minus = flux(0, [jnp.where(last, xf_ref[g], adj_ref[g, nxt]) - a[g] for g in range(nf)])
        for f in range(nf):
            sx = offset_terms(plus[f], minus[f], lambda s, k: w_ref[0, s, k, f, xl])
            for o in range(6):
                acc_ref[f, x + o] = acc_ref[f, x + o] + sx[o]
        a = [adj_ref[f, x] for f in range(nf)]
        plus, minus = flux(1, [
            jnp.where(row == ny - 1, yf_ref[g, pl.ds(x, 1), :], pltpu.roll(a[g], ny - 1, 0)) - a[g]
            for g in range(nf)
        ])
        for f in range(nf):
            sy = offset_terms(plus[f], minus[f], lambda s, k: w_ref[1, s, k, f, xl])
            iy, wyr, wyl = split_rows(sy, row8, ny)
            acc_ref[f, x + 2] = acc_ref[f, x + 2] + iy
            rear = pltpu.roll(wyr, 4 * (xl % 2), 0)
            lead = pltpu.roll(wyl, (2 + 2 * (xl % 4)) % 8, 0)
            kr = (f, xl // 2)
            kl = (f, xl // 4)
            yr_parts[kr] = rear if kr not in yr_parts else yr_parts[kr] + rear
            yl_parts[kl] = lead if kl not in yl_parts else yl_parts[kl] + lead
        a = [adj_ref[f, x] for f in range(nf)]
        zshift = nz - 1 - x
        plus, minus = flux(2, [
            jnp.where(lane == nz - 1, pltpu.roll(zf_ref[g], zshift, 1), pltpu.roll(a[g], nz - 1, 1)) - a[g]
            for g in range(nf)
        ])
        for f in range(nf):
            sz = offset_terms(plus[f], minus[f], lambda s, k: w_ref[2, s, k, f, xl])
            iz, wzr, wzl = split_lanes(sz, lane, nz)
            acc_ref[f, x + 2] = acc_ref[f, x + 2] + iz
            zz_ref[0, f] = zz_ref[0, f] + pltpu.roll(wzl, 2 + 4 * x, 1)
            zz_ref[1, f] = zz_ref[1, f] + pltpu.roll(wzr, 4 * x, 1)
    for (f, t), v in yr_parts.items():
        yr_ref[f, t] = v
    for (f, t), v in yl_parts.items():
        yl_ref[f, t] = v

    @pl.when(i == pl.num_programs(0) - 1)
    def _():
        def body(x, c):
            for f in range(nf):
                sec_ref[f, x] = SECTION * (adj_ref[f, x] + acc_ref[f, x + 2])
            return c

        lax.fori_loop(0, nx, body, 0)
        for f in range(nf):
            xl_ref[f] = acc_ref[f, 0:2]
            xr_ref[f] = acc_ref[f, nx + 2:nx + 5]


def fix_kernel(row_ref, cnt_ref, sec_ref, axl_ref, axr_ref, ayl_ref, ayr_ref, az_ref,
               coef_ref, out_ref, wt_ref):
    nf, nx, ny, nz = sec_ref.shape
    row, lane = iotas(ny, nz)
    pad = jnp.zeros((ny - 8, nz), F32)
    for x in range(nx):
        for f in range(nf):
            ty = jnp.concatenate([ayr_ref[f, x // 2], pad], 0)
            add = jnp.where(row < 3, pltpu.roll(ty, (ny - 4 * (x % 2)) % ny, 0), 0.0)
            ty = jnp.concatenate([ayl_ref[f, x // 4], pad], 0)
            add = add + jnp.where(row >= ny - 2, pltpu.roll(ty, (ny - 2 - 2 * (x % 4)) % ny, 0), 0.0)
            add = add + jnp.where(lane < 3, pltpu.roll(az_ref[1, f], (nz - 4 * x) % nz, 1), 0.0)
            add = add + jnp.where(lane >= nz - 2, pltpu.roll(az_ref[0, f], (nz - 2 - 4 * x) % nz, 1), 0.0)
            if x < 3:
                add = add + axr_ref[f, x]
            if x >= nx - 2:
                add = add + axl_ref[f, x - (nx - 2)]
            out_ref[f, x] = sec_ref[f, x] + SECTION * add
    live_n = cnt_ref[0]
    for r in range(wt_ref.shape[0]):
        idx = row_ref[r]
        lx = idx // ny
        ly = idx % ny
        val = None
        for f in range(nf):
            v = out_ref[f, lx, pl.ds(ly, 1), :] * coef_ref[f, pl.ds(r, 1), :]
            val = v if val is None else val + v
        wt_ref[pl.ds(r, 1), :] = val * jnp.where(r < live_n, 1.0, 0.0).astype(F32)


def on_device(ndev, adjoint, stencil_weights, flux_plus, flux_minus, wall_row, wall_panel, wall_coef,
              wall_count, panel_owner):
    nf, nx, ny, nz = adjoint.shape
    assert nx % XC == 0 and XC % 4 == 0 and ny == 16 and nx * 4 <= nz
    xf, yf, zf = pl.pallas_call(
        fronts_kernel,
        grid=(nf,),
        out_shape=(
            jax.ShapeDtypeStruct((nf, ny, nz), F32),
            jax.ShapeDtypeStruct((nf, nx, nz), F32),
            jax.ShapeDtypeStruct((nf, ny, nz), F32),
        ),
        in_specs=[pl.BlockSpec((1, nx, ny, nz), lambda f: (f, 0, 0, 0))],
        out_specs=(
            pl.BlockSpec((1, ny, nz), lambda f: (f, 0, 0)),
            pl.BlockSpec((1, nx, nz), lambda f: (f, 0, 0)),
            pl.BlockSpec((1, ny, nz), lambda f: (f, 0, 0)),
        ),
        compiler_params=pltpu.CompilerParams(dimension_semantics=("arbitrary",)),
    )(adjoint)
    xf = shift_from(xf, "gx", -1)
    yf = shift_from(yf, "gy", -1)
    zf = shift_from(zf, "gz", -1)
    const4 = lambda i: (0, 0, 0, 0)
    const3 = lambda i: (0, 0, 0)
    sec, xl, xr, yl, yr, zz = pl.pallas_call(
        stencil_kernel,
        grid=(nx // XC,),
        out_shape=(
            jax.ShapeDtypeStruct((nf, nx, ny, nz), F32),
            jax.ShapeDtypeStruct((nf, 2, ny, nz), F32),
            jax.ShapeDtypeStruct((nf, 3, ny, nz), F32),
            jax.ShapeDtypeStruct((nf, nx // 4, 8, nz), F32),
            jax.ShapeDtypeStruct((nf, nx // 2, 8, nz), F32),
            jax.ShapeDtypeStruct((2, nf, ny, nz), F32),
        ),
        in_specs=[
            SMEM,
            SMEM,
            pl.BlockSpec((nf, nx, ny, nz), const4),
            pl.BlockSpec((nf, ny, nz), const3),
            pl.BlockSpec((nf, nx, nz), const3),
            pl.BlockSpec((nf, ny, nz), const3),
            pl.BlockSpec((3, 2, 3, nf, XC, ny, nz), lambda i: (0, 0, 0, 0, i, 0, 0)),
        ],
        out_specs=(
            pl.BlockSpec((nf, nx, ny, nz), const4),
            pl.BlockSpec((nf, 2, ny, nz), const4),
            pl.BlockSpec((nf, 3, ny, nz), const4),
            pl.BlockSpec((nf, XC // 4, 8, nz), lambda i: (0, i, 0, 0)),
            pl.BlockSpec((nf, XC // 2, 8, nz), lambda i: (0, i, 0, 0)),
            pl.BlockSpec((2, nf, ny, nz), const4),
        ),
        scratch_shapes=[pltpu.VMEM((nf, nx + 5, ny, nz), F32)],
        compiler_params=pltpu.CompilerParams(dimension_semantics=("arbitrary",)),
    )(flux_plus, flux_minus, adjoint, xf, yf, zf, stencil_weights)
    axl = shift_from(xl, "gx", -1)
    axr = shift_from(xr, "gx", 1)
    ayl = shift_from(yl, "gy", -1)
    ayr = shift_from(yr, "gy", 1)
    if lax.axis_size("gz") == 2:
        az = shift_from(zz, "gz", 1)
    else:
        az = jnp.stack([shift_from(zz[0], "gz", -1), shift_from(zz[1], "gz", 1)])
    nr = wall_row.shape[0]
    section, wt = pl.pallas_call(
        fix_kernel,
        out_shape=(
            jax.ShapeDtypeStruct((nf, nx, ny, nz), F32),
            jax.ShapeDtypeStruct((nr, nz), F32),
        ),
        in_specs=[SMEM, SMEM] + [VMEM] * 7,
        out_specs=(VMEM, VMEM),
        input_output_aliases={2: 0},
    )(wall_row, wall_count, sec, axl, axr, ayl, ayr, az, wall_coef)

    npan = panel_owner.shape[0]
    per = npan // ndev
    nb = 32
    na = npan // nb
    own_oh = (panel_owner[:, None] == jnp.arange(ndev, dtype=jnp.int32)).astype(F32)
    oh3 = own_oh.reshape(na, nb, ndev)
    below_b = (jnp.arange(nb)[None, :] < jnp.arange(nb)[:, None]).astype(F32)
    below_a = (jnp.arange(na)[None, :] < jnp.arange(na)[:, None]).astype(F32)
    inner = jnp.einsum("bc,acd->abd", below_b, oh3, precision=HI)
    before = jnp.einsum("ac,cd->ad", below_a, jnp.sum(oh3, axis=1), precision=HI)
    rank = jnp.sum((inner + before[:, None, :]) * oh3, axis=2)
    oh_a = (wall_panel[..., None] // nb == jnp.arange(na, dtype=jnp.int32)).astype(F32)
    oh_b = (wall_panel[..., None] % nb == jnp.arange(nb, dtype=jnp.int32)).astype(F32)

    def lookup(table):
        picked = jnp.einsum("rza,ab->rzb", oh_a, table, precision=HI) * oh_b
        return jnp.round(jnp.sum(picked, axis=2)).astype(jnp.int32)

    cell_own = lookup(panel_owner.reshape(na, nb).astype(F32))
    cell_rank = lookup(rank)
    oh_o = (cell_own[..., None] == jnp.arange(ndev, dtype=jnp.int32)).astype(F32)
    oh_k = (cell_rank[..., None] == jnp.arange(per, dtype=jnp.int32)).astype(F32)
    t = jnp.einsum("rzo,rzk->ok", oh_o * wt[..., None], oh_k, precision=HI)
    got = lax.all_to_all(t, AXES, 0, 0, tiled=True)
    return section, jnp.sum(got, axis=0)


def solution(mesh):
    ndev = mesh.size
    placed = (
        P(None, "gx", "gy", "gz"),
        P(None, None, None, None, "gx", "gy", "gz"),
        P(),
        P(),
        P(AXES),
        P(AXES, None),
        P(None, AXES, None),
        P(AXES),
        P(),
    )
    return jax.shard_map(
        lambda *args: on_device(ndev, *args),
        mesh=mesh,
        in_specs=placed,
        out_specs=(P(None, "gx", "gy", "gz"), P(AXES)),
        check_vma=False,
    )
```

```python
import jax
import jax.numpy as jnp
from jax import lax
from jax.experimental import pallas as pl
from jax.experimental.pallas import tpu as pltpu
from jax.sharding import PartitionSpec as P

AXES = ("gx", "gy", "gz")
STEP = 0.4
SECTION = 0.25
XC = 4
F32 = jnp.float32
HI = lax.Precision.HIGHEST
VMEM = pl.BlockSpec(memory_space=pltpu.VMEM)
SMEM = pl.BlockSpec(memory_space=pltpu.SMEM)


def shift_from(x, axis, by):
    n = lax.axis_size(axis)
    return lax.ppermute(x, axis, [(i, (i + by) % n) for i in range(n)])


def iotas(ny, nz):
    return (
        lax.broadcasted_iota(jnp.int32, (ny, nz), 0),
        lax.broadcasted_iota(jnp.int32, (ny, nz), 1),
    )


def fronts_kernel(adj_hbm, xf_ref, yf_ref, zf_ref, adj_ref, sems):
    nf, nx, ny, nz = adj_ref.shape
    row, lane = iotas(ny, nz)
    copies = [pltpu.make_async_copy(adj_hbm.at[f], adj_ref.at[f], sems.at[f]) for f in range(nf)]
    for c in copies:
        c.start()
    for f in range(nf):
        copies[f].wait()
        xf_ref[f] = adj_ref[f, 0]
        zacc = jnp.zeros((ny, nz), F32)
        for x in range(nx):
            s = adj_ref[f, x]
            yf_ref[f, pl.ds(x, 1), :] = s[0:1, :]
            zacc = zacc + pltpu.roll(jnp.where(lane == 0, s, 0.0), x, 1)
        zf_ref[f] = zacc


def offset_terms(plus, minus, w):
    p0, p1, p2 = plus * w(0, 0), plus * w(0, 1), plus * w(0, 2)
    m0, m1, m2 = minus * w(1, 0), minus * w(1, 1), minus * w(1, 2)
    a = p1 + m2
    b = p2 + m1
    return [
        p0 * (1.0 / 3.0),
        p0 * (-7.0 / 6.0) + a * (-1.0 / 6.0),
        p0 * (11.0 / 6.0) + a * (5.0 / 6.0) + b * (1.0 / 3.0),
        a * (1.0 / 3.0) + b * (5.0 / 6.0) + m0 * (11.0 / 6.0),
        b * (-1.0 / 6.0) + m0 * (-7.0 / 6.0),
        m0 * (1.0 / 3.0),
    ]


def rolled_sum(terms, n, axis):
    r = {o: pltpu.roll(terms[o], (o - 2) % n, axis) for o in (0, 1, 3, 4, 5)}
    tot = terms[2] + r[0] + r[1] + r[3] + r[4] + r[5]
    return r, tot


def split_rows(terms, row8, ny):
    r, tot = rolled_sum(terms, ny, 0)
    h = ny - 8
    wr = (jnp.where(row8 < 1, r[3][0:8], 0.0) + jnp.where(row8 < 2, r[4][0:8], 0.0)
          + jnp.where(row8 < 3, r[5][0:8], 0.0))
    wl = jnp.where(row8 >= 6, r[0][h:ny], 0.0) + jnp.where(row8 >= 7, r[1][h:ny], 0.0)
    inner = jnp.concatenate([tot[0:8] - wr, tot[8:h], tot[h:ny] - wl], 0) if h > 8 else \
        jnp.concatenate([tot[0:8] - wr, tot[h:ny] - wl], 0)
    return inner, wr, wl


def split_lanes(terms, lane, nz):
    r, tot = rolled_sum(terms, nz, 1)
    wr = jnp.where(lane < 1, r[3], 0.0) + jnp.where(lane < 2, r[4], 0.0) + jnp.where(lane < 3, r[5], 0.0)
    wl = jnp.where(lane >= nz - 2, r[0], 0.0) + jnp.where(lane >= nz - 1, r[1], 0.0)
    return tot - wr - wl, wr, wl


def stencil_kernel(fp_ref, fm_ref, adj_ref, xf_ref, yf_ref, zf_ref, w_ref,
                   sec_ref, xl_ref, xr_ref, yl_ref, yr_ref, zz_ref, acc_ref):
    nf, nx, ny, nz = adj_ref.shape
    i = pl.program_id(0)
    row, lane = iotas(ny, nz)
    row8 = lax.broadcasted_iota(jnp.int32, (8, nz), 0)

    @pl.when(i == 0)
    def _():
        acc_ref[...] = jnp.zeros_like(acc_ref)
        zz_ref[...] = jnp.zeros_like(zz_ref)

    def flux(d, diff):
        plus, minus = [], []
        for f in range(nf):
            p = m = None
            for g in range(nf):
                tp = diff[g] * (STEP * fp_ref[d, g, f])
                tm = diff[g] * (STEP * fm_ref[d, g, f])
                p = tp if p is None else p + tp
                m = tm if m is None else m + tm
            plus.append(p)
            minus.append(m)
        return plus, minus

    yr_parts = {}
    yl_parts = {}
    for xl in range(XC):
        x = i * XC + xl
        last = x == nx - 1
        nxt = jnp.minimum(x + 1, nx - 1)
        a = [adj_ref[f, x] for f in range(nf)]
        plus, minus = flux(0, [jnp.where(last, xf_ref[g], adj_ref[g, nxt]) - a[g] for g in range(nf)])
        for f in range(nf):
            sx = offset_terms(plus[f], minus[f], lambda s, k: w_ref[0, s, k, f, xl])
            for o in range(6):
                acc_ref[f, x + o] = acc_ref[f, x + o] + sx[o]
        a = [adj_ref[f, x] for f in range(nf)]
        plus, minus = flux(1, [
            jnp.where(row == ny - 1, yf_ref[g, pl.ds(x, 1), :], pltpu.roll(a[g], ny - 1, 0)) - a[g]
            for g in range(nf)
        ])
        for f in range(nf):
            sy = offset_terms(plus[f], minus[f], lambda s, k: w_ref[1, s, k, f, xl])
            iy, wyr, wyl = split_rows(sy, row8, ny)
            acc_ref[f, x + 2] = acc_ref[f, x + 2] + iy
            rear = pltpu.roll(wyr, 4 * (xl % 2), 0)
            lead = pltpu.roll(wyl, (2 + 2 * (xl % 4)) % 8, 0)
            kr = (f, xl // 2)
            kl = (f, xl // 4)
            yr_parts[kr] = rear if kr not in yr_parts else yr_parts[kr] + rear
            yl_parts[kl] = lead if kl not in yl_parts else yl_parts[kl] + lead
        a = [adj_ref[f, x] for f in range(nf)]
        zshift = nz - 1 - x
        plus, minus = flux(2, [
            jnp.where(lane == nz - 1, pltpu.roll(zf_ref[g], zshift, 1), pltpu.roll(a[g], nz - 1, 1)) - a[g]
            for g in range(nf)
        ])
        for f in range(nf):
            sz = offset_terms(plus[f], minus[f], lambda s, k: w_ref[2, s, k, f, xl])
            iz, wzr, wzl = split_lanes(sz, lane, nz)
            acc_ref[f, x + 2] = acc_ref[f, x + 2] + iz
            zz_ref[0, f] = zz_ref[0, f] + pltpu.roll(wzl, 2 + 4 * x, 1)
            zz_ref[1, f] = zz_ref[1, f] + pltpu.roll(wzr, 4 * x, 1)
    for (f, t), v in yr_parts.items():
        yr_ref[f, t] = v
    for (f, t), v in yl_parts.items():
        yl_ref[f, t] = v

    @pl.when(i == pl.num_programs(0) - 1)
    def _():
        def body(x, c):
            for f in range(nf):
                sec_ref[f, x] = SECTION * (adj_ref[f, x] + acc_ref[f, x + 2])
            return c

        lax.fori_loop(0, nx, body, 0)
        for f in range(nf):
            xl_ref[f] = acc_ref[f, 0:2]
            xr_ref[f] = acc_ref[f, nx + 2:nx + 5]


def fix_kernel(row_ref, cnt_ref, sec_ref, axl_ref, axr_ref, ayl_ref, ayr_ref, az_ref,
               coef_ref, out_ref, wt_ref):
    nf, nx, ny, nz = sec_ref.shape
    row, lane = iotas(ny, nz)
    pad = jnp.zeros((ny - 8, nz), F32)
    for x in range(nx):
        for f in range(nf):
            ty = jnp.concatenate([ayr_ref[f, x // 2], pad], 0)
            add = jnp.where(row < 3, pltpu.roll(ty, (ny - 4 * (x % 2)) % ny, 0), 0.0)
            ty = jnp.concatenate([ayl_ref[f, x // 4], pad], 0)
            add = add + jnp.where(row >= ny - 2, pltpu.roll(ty, (ny - 2 - 2 * (x % 4)) % ny, 0), 0.0)
            add = add + jnp.where(lane < 3, pltpu.roll(az_ref[1, f], (nz - 4 * x) % nz, 1), 0.0)
            add = add + jnp.where(lane >= nz - 2, pltpu.roll(az_ref[0, f], (nz - 2 - 4 * x) % nz, 1), 0.0)
            if x < 3:
                add = add + axr_ref[f, x]
            if x >= nx - 2:
                add = add + axl_ref[f, x - (nx - 2)]
            out_ref[f, x] = sec_ref[f, x] + SECTION * add
    live_n = cnt_ref[0]
    for r in range(wt_ref.shape[0]):
        idx = row_ref[r]
        lx = idx // ny
        ly = idx % ny
        val = None
        for f in range(nf):
            v = out_ref[f, lx, pl.ds(ly, 1), :] * coef_ref[f, pl.ds(r, 1), :]
            val = v if val is None else val + v
        wt_ref[pl.ds(r, 1), :] = val * jnp.where(r < live_n, 1.0, 0.0).astype(F32)


def on_device(ndev, adjoint, stencil_weights, flux_plus, flux_minus, wall_row, wall_panel, wall_coef,
              wall_count, panel_owner):
    nf, nx, ny, nz = adjoint.shape
    assert nx % XC == 0 and XC % 4 == 0 and ny == 16 and nx * 4 <= nz
    xf, yf, zf = pl.pallas_call(
        fronts_kernel,
        out_shape=(
            jax.ShapeDtypeStruct((nf, ny, nz), F32),
            jax.ShapeDtypeStruct((nf, nx, nz), F32),
            jax.ShapeDtypeStruct((nf, ny, nz), F32),
        ),
        in_specs=[pl.BlockSpec(memory_space=pl.ANY)],
        out_specs=(VMEM, VMEM, VMEM),
        scratch_shapes=[pltpu.VMEM((nf, nx, ny, nz), F32), pltpu.SemaphoreType.DMA((nf,))],
    )(adjoint)
    xf = shift_from(xf, "gx", -1)
    yf = shift_from(yf, "gy", -1)
    zf = shift_from(zf, "gz", -1)
    const4 = lambda i: (0, 0, 0, 0)
    const3 = lambda i: (0, 0, 0)
    sec, xl, xr, yl, yr, zz = pl.pallas_call(
        stencil_kernel,
        grid=(nx // XC,),
        out_shape=(
            jax.ShapeDtypeStruct((nf, nx, ny, nz), F32),
            jax.ShapeDtypeStruct((nf, 2, ny, nz), F32),
            jax.ShapeDtypeStruct((nf, 3, ny, nz), F32),
            jax.ShapeDtypeStruct((nf, nx // 4, 8, nz), F32),
            jax.ShapeDtypeStruct((nf, nx // 2, 8, nz), F32),
            jax.ShapeDtypeStruct((2, nf, ny, nz), F32),
        ),
        in_specs=[
            SMEM,
            SMEM,
            pl.BlockSpec((nf, nx, ny, nz), const4),
            pl.BlockSpec((nf, ny, nz), const3),
            pl.BlockSpec((nf, nx, nz), const3),
            pl.BlockSpec((nf, ny, nz), const3),
            pl.BlockSpec((3, 2, 3, nf, XC, ny, nz), lambda i: (0, 0, 0, 0, i, 0, 0)),
        ],
        out_specs=(
            pl.BlockSpec((nf, nx, ny, nz), const4),
            pl.BlockSpec((nf, 2, ny, nz), const4),
            pl.BlockSpec((nf, 3, ny, nz), const4),
            pl.BlockSpec((nf, XC // 4, 8, nz), lambda i: (0, i, 0, 0)),
            pl.BlockSpec((nf, XC // 2, 8, nz), lambda i: (0, i, 0, 0)),
            pl.BlockSpec((2, nf, ny, nz), const4),
        ),
        scratch_shapes=[pltpu.VMEM((nf, nx + 5, ny, nz), F32)],
        compiler_params=pltpu.CompilerParams(dimension_semantics=("arbitrary",)),
    )(flux_plus, flux_minus, adjoint, xf, yf, zf, stencil_weights)
    axl = shift_from(xl, "gx", -1)
    axr = shift_from(xr, "gx", 1)
    ayl = shift_from(yl, "gy", -1)
    ayr = shift_from(yr, "gy", 1)
    if lax.axis_size("gz") == 2:
        az = shift_from(zz, "gz", 1)
    else:
        az = jnp.stack([shift_from(zz[0], "gz", -1), shift_from(zz[1], "gz", 1)])
    nr = wall_row.shape[0]
    section, wt = pl.pallas_call(
        fix_kernel,
        out_shape=(
            jax.ShapeDtypeStruct((nf, nx, ny, nz), F32),
            jax.ShapeDtypeStruct((nr, nz), F32),
        ),
        in_specs=[SMEM, SMEM] + [VMEM] * 7,
        out_specs=(VMEM, VMEM),
        input_output_aliases={2: 0},
    )(wall_row, wall_count, sec, axl, axr, ayl, ayr, az, wall_coef)

    npan = panel_owner.shape[0]
    per = npan // ndev
    nb = 32
    na = npan // nb
    own_oh = (panel_owner[:, None] == jnp.arange(ndev, dtype=jnp.int32)).astype(F32)
    oh3 = own_oh.reshape(na, nb, ndev)
    below_b = (jnp.arange(nb)[None, :] < jnp.arange(nb)[:, None]).astype(F32)
    below_a = (jnp.arange(na)[None, :] < jnp.arange(na)[:, None]).astype(F32)
    inner = jnp.einsum("bc,acd->abd", below_b, oh3, precision=HI)
    before = jnp.einsum("ac,cd->ad", below_a, jnp.sum(oh3, axis=1), precision=HI)
    rank = jnp.sum((inner + before[:, None, :]) * oh3, axis=2)
    oh_a = (wall_panel[..., None] // nb == jnp.arange(na, dtype=jnp.int32)).astype(F32)
    oh_b = (wall_panel[..., None] % nb == jnp.arange(nb, dtype=jnp.int32)).astype(F32)

    def lookup(table):
        picked = jnp.einsum("rza,ab->rzb", oh_a, table, precision=HI) * oh_b
        return jnp.round(jnp.sum(picked, axis=2)).astype(jnp.int32)

    cell_own = lookup(panel_owner.reshape(na, nb).astype(F32))
    cell_rank = lookup(rank)
    oh_o = (cell_own[..., None] == jnp.arange(ndev, dtype=jnp.int32)).astype(F32)
    oh_k = (cell_rank[..., None] == jnp.arange(per, dtype=jnp.int32)).astype(F32)
    t = jnp.einsum("rzo,rzk->ok", oh_o * wt[..., None], oh_k, precision=HI)
    got = lax.all_to_all(t, AXES, 0, 0, tiled=True)
    return section, jnp.sum(got, axis=0)


def solution(mesh):
    ndev = mesh.size
    placed = (
        P(None, "gx", "gy", "gz"),
        P(None, None, None, None, "gx", "gy", "gz"),
        P(),
        P(),
        P(AXES),
        P(AXES, None),
        P(None, AXES, None),
        P(AXES),
        P(),
    )
    return jax.shard_map(
        lambda *args: on_device(ndev, *args),
        mesh=mesh,
        in_specs=placed,
        out_specs=(P(None, "gx", "gy", "gz"), P(AXES)),
        check_vma=False,
    )
```

```python
import jax
import jax.numpy as jnp
from jax import lax
from jax.experimental import pallas as pl
from jax.experimental.pallas import tpu as pltpu
from jax.sharding import PartitionSpec as P

AXES = ("gx", "gy", "gz")
STEP = 0.4
SECTION = 0.25
XC = 4
F32 = jnp.float32
HI = lax.Precision.HIGHEST
VMEM = pl.BlockSpec(memory_space=pltpu.VMEM)
SMEM = pl.BlockSpec(memory_space=pltpu.SMEM)
HBM = pl.BlockSpec(memory_space=pltpu.HBM)


def shift_from(x, axis, by):
    n = lax.axis_size(axis)
    return lax.ppermute(x, axis, [(i, (i + by) % n) for i in range(n)])


def iotas(ny, nz):
    return (
        lax.broadcasted_iota(jnp.int32, (ny, nz), 0),
        lax.broadcasted_iota(jnp.int32, (ny, nz), 1),
    )


def fronts_kernel(adj_ref, xf_ref, yf_ref, zf_ref):
    nf, nx, ny, nz = adj_ref.shape
    row, lane = iotas(ny, nz)
    for f in range(nf):
        xf_ref[f] = adj_ref[f, 0]
        zacc = jnp.zeros((ny, nz), F32)
        for x in range(nx):
            s = adj_ref[f, x]
            yf_ref[f, pl.ds(x, 1), :] = s[0:1, :]
            zacc = zacc + pltpu.roll(jnp.where(lane == 0, s, 0.0), x, 1)
        zf_ref[f] = zacc


def offset_terms(plus, minus, w):
    p0, p1, p2 = plus * w(0, 0), plus * w(0, 1), plus * w(0, 2)
    m0, m1, m2 = minus * w(1, 0), minus * w(1, 1), minus * w(1, 2)
    a = p1 + m2
    b = p2 + m1
    return [
        p0 * (1.0 / 3.0),
        p0 * (-7.0 / 6.0) + a * (-1.0 / 6.0),
        p0 * (11.0 / 6.0) + a * (5.0 / 6.0) + b * (1.0 / 3.0),
        a * (1.0 / 3.0) + b * (5.0 / 6.0) + m0 * (11.0 / 6.0),
        b * (-1.0 / 6.0) + m0 * (-7.0 / 6.0),
        m0 * (1.0 / 3.0),
    ]


def rolled_sum(terms, n, axis):
    r = {o: pltpu.roll(terms[o], (o - 2) % n, axis) for o in (0, 1, 3, 4, 5)}
    tot = terms[2] + r[0] + r[1] + r[3] + r[4] + r[5]
    return r, tot


def split_rows(terms, row8, ny):
    r, tot = rolled_sum(terms, ny, 0)
    h = ny - 8
    wr = (jnp.where(row8 < 1, r[3][0:8], 0.0) + jnp.where(row8 < 2, r[4][0:8], 0.0)
          + jnp.where(row8 < 3, r[5][0:8], 0.0))
    wl = jnp.where(row8 >= 6, r[0][h:ny], 0.0) + jnp.where(row8 >= 7, r[1][h:ny], 0.0)
    inner = jnp.concatenate([tot[0:8] - wr, tot[8:h], tot[h:ny] - wl], 0) if h > 8 else \
        jnp.concatenate([tot[0:8] - wr, tot[h:ny] - wl], 0)
    return inner, wr, wl


def split_lanes(terms, lane, nz):
    r, tot = rolled_sum(terms, nz, 1)
    wr = jnp.where(lane < 1, r[3], 0.0) + jnp.where(lane < 2, r[4], 0.0) + jnp.where(lane < 3, r[5], 0.0)
    wl = jnp.where(lane >= nz - 2, r[0], 0.0) + jnp.where(lane >= nz - 1, r[1], 0.0)
    return tot - wr - wl, wr, wl


def stencil_kernel(fp_ref, fm_ref, adj_ref, xf_ref, yf_ref, zf_ref, w_ref,
                   sec_ref, xl_ref, xr_ref, yl_ref, yr_ref, zz_ref, acc_ref):
    nf, nx, ny, nz = adj_ref.shape
    i = pl.program_id(0)
    row, lane = iotas(ny, nz)
    row8 = lax.broadcasted_iota(jnp.int32, (8, nz), 0)

    @pl.when(i == 0)
    def _():
        acc_ref[...] = jnp.zeros_like(acc_ref)
        zz_ref[...] = jnp.zeros_like(zz_ref)

    def flux(d, diff):
        plus, minus = [], []
        for f in range(nf):
            p = m = None
            for g in range(nf):
                tp = diff[g] * (STEP * fp_ref[d, g, f])
                tm = diff[g] * (STEP * fm_ref[d, g, f])
                p = tp if p is None else p + tp
                m = tm if m is None else m + tm
            plus.append(p)
            minus.append(m)
        return plus, minus

    yr_parts = {}
    yl_parts = {}
    for xl in range(XC):
        x = i * XC + xl
        last = x == nx - 1
        nxt = jnp.minimum(x + 1, nx - 1)
        a = [adj_ref[f, x] for f in range(nf)]
        plus, minus = flux(0, [jnp.where(last, xf_ref[g], adj_ref[g, nxt]) - a[g] for g in range(nf)])
        for f in range(nf):
            sx = offset_terms(plus[f], minus[f], lambda s, k: w_ref[0, s, k, f, xl])
            for o in range(6):
                acc_ref[f, x + o] = acc_ref[f, x + o] + sx[o]
        a = [adj_ref[f, x] for f in range(nf)]
        plus, minus = flux(1, [
            jnp.where(row == ny - 1, yf_ref[g, pl.ds(x, 1), :], pltpu.roll(a[g], ny - 1, 0)) - a[g]
            for g in range(nf)
        ])
        for f in range(nf):
            sy = offset_terms(plus[f], minus[f], lambda s, k: w_ref[1, s, k, f, xl])
            iy, wyr, wyl = split_rows(sy, row8, ny)
            acc_ref[f, x + 2] = acc_ref[f, x + 2] + iy
            rear = pltpu.roll(wyr, 4 * (xl % 2), 0)
            lead = pltpu.roll(wyl, (2 + 2 * (xl % 4)) % 8, 0)
            kr = (f, xl // 2)
            kl = (f, xl // 4)
            yr_parts[kr] = rear if kr not in yr_parts else yr_parts[kr] + rear
            yl_parts[kl] = lead if kl not in yl_parts else yl_parts[kl] + lead
        a = [adj_ref[f, x] for f in range(nf)]
        zshift = nz - 1 - x
        plus, minus = flux(2, [
            jnp.where(lane == nz - 1, pltpu.roll(zf_ref[g], zshift, 1), pltpu.roll(a[g], nz - 1, 1)) - a[g]
            for g in range(nf)
        ])
        for f in range(nf):
            sz = offset_terms(plus[f], minus[f], lambda s, k: w_ref[2, s, k, f, xl])
            iz, wzr, wzl = split_lanes(sz, lane, nz)
            acc_ref[f, x + 2] = acc_ref[f, x + 2] + iz
            zz_ref[0, f] = zz_ref[0, f] + pltpu.roll(wzl, 2 + 4 * x, 1)
            zz_ref[1, f] = zz_ref[1, f] + pltpu.roll(wzr, 4 * x, 1)
    for (f, t), v in yr_parts.items():
        yr_ref[f, t] = v
    for (f, t), v in yl_parts.items():
        yl_ref[f, t] = v

    @pl.when(i == pl.num_programs(0) - 1)
    def _():
        def body(x, c):
            for f in range(nf):
                sec_ref[f, x] = SECTION * (adj_ref[f, x] + acc_ref[f, x + 2])
            return c

        lax.fori_loop(0, nx, body, 0)
        for f in range(nf):
            xl_ref[f] = acc_ref[f, 0:2]
            xr_ref[f] = acc_ref[f, nx + 2:nx + 5]


def fix_kernel(row_ref, cnt_ref, sec_hbm, axl_ref, axr_ref, ayl_ref, ayr_ref, az_ref,
               coef_ref, out_hbm, wt_ref, buf, in_sems, out_sems):
    nf, nx, ny, nz = buf.shape
    nch = nx // XC
    chunk = lambda ref, c: ref.at[:, pl.ds(c * XC, XC)]
    loads = [pltpu.make_async_copy(chunk(sec_hbm, c), chunk(buf, c), in_sems.at[c]) for c in range(nch)]
    stores = [pltpu.make_async_copy(chunk(buf, c), chunk(out_hbm, c), out_sems.at[c]) for c in range(nch)]
    for cp in loads:
        cp.start()
    row, lane = iotas(ny, nz)
    pad = jnp.zeros((ny - 8, nz), F32)
    for c in range(nch):
        loads[c].wait()
        for x in range(c * XC, (c + 1) * XC):
            for f in range(nf):
                ty = jnp.concatenate([ayr_ref[f, x // 2], pad], 0)
                add = jnp.where(row < 3, pltpu.roll(ty, (ny - 4 * (x % 2)) % ny, 0), 0.0)
                ty = jnp.concatenate([ayl_ref[f, x // 4], pad], 0)
                add = add + jnp.where(row >= ny - 2, pltpu.roll(ty, (ny - 2 - 2 * (x % 4)) % ny, 0), 0.0)
                add = add + jnp.where(lane < 3, pltpu.roll(az_ref[1, f], (nz - 4 * x) % nz, 1), 0.0)
                add = add + jnp.where(lane >= nz - 2, pltpu.roll(az_ref[0, f], (nz - 2 - 4 * x) % nz, 1), 0.0)
                if x < 3:
                    add = add + axr_ref[f, x]
                if x >= nx - 2:
                    add = add + axl_ref[f, x - (nx - 2)]
                buf[f, x] = buf[f, x] + SECTION * add
        stores[c].start()
    live_n = cnt_ref[0]
    for r in range(wt_ref.shape[0]):
        idx = row_ref[r]
        lx = idx // ny
        ly = idx % ny
        val = None
        for f in range(nf):
            v = buf[f, lx, pl.ds(ly, 1), :] * coef_ref[f, pl.ds(r, 1), :]
            val = v if val is None else val + v
        wt_ref[pl.ds(r, 1), :] = val * jnp.where(r < live_n, 1.0, 0.0).astype(F32)
    for cp in stores:
        cp.wait()


def on_device(ndev, adjoint, stencil_weights, flux_plus, flux_minus, wall_row, wall_panel, wall_coef,
              wall_count, panel_owner):
    nf, nx, ny, nz = adjoint.shape
    assert nx % XC == 0 and XC % 4 == 0 and ny == 16 and nx * 4 <= nz
    xf, yf, zf = pl.pallas_call(
        fronts_kernel,
        out_shape=(
            jax.ShapeDtypeStruct((nf, ny, nz), F32),
            jax.ShapeDtypeStruct((nf, nx, nz), F32),
            jax.ShapeDtypeStruct((nf, ny, nz), F32),
        ),
        in_specs=[VMEM],
        out_specs=(VMEM, VMEM, VMEM),
    )(adjoint)
    xf = shift_from(xf, "gx", -1)
    yf = shift_from(yf, "gy", -1)
    zf = shift_from(zf, "gz", -1)
    const4 = lambda i: (0, 0, 0, 0)
    const3 = lambda i: (0, 0, 0)
    sec, xl, xr, yl, yr, zz = pl.pallas_call(
        stencil_kernel,
        grid=(nx // XC,),
        out_shape=(
            jax.ShapeDtypeStruct((nf, nx, ny, nz), F32),
            jax.ShapeDtypeStruct((nf, 2, ny, nz), F32),
            jax.ShapeDtypeStruct((nf, 3, ny, nz), F32),
            jax.ShapeDtypeStruct((nf, nx // 4, 8, nz), F32),
            jax.ShapeDtypeStruct((nf, nx // 2, 8, nz), F32),
            jax.ShapeDtypeStruct((2, nf, ny, nz), F32),
        ),
        in_specs=[
            SMEM,
            SMEM,
            pl.BlockSpec((nf, nx, ny, nz), const4),
            pl.BlockSpec((nf, ny, nz), const3),
            pl.BlockSpec((nf, nx, nz), const3),
            pl.BlockSpec((nf, ny, nz), const3),
            pl.BlockSpec((3, 2, 3, nf, XC, ny, nz), lambda i: (0, 0, 0, 0, i, 0, 0)),
        ],
        out_specs=(
            pl.BlockSpec((nf, nx, ny, nz), const4),
            pl.BlockSpec((nf, 2, ny, nz), const4),
            pl.BlockSpec((nf, 3, ny, nz), const4),
            pl.BlockSpec((nf, XC // 4, 8, nz), lambda i: (0, i, 0, 0)),
            pl.BlockSpec((nf, XC // 2, 8, nz), lambda i: (0, i, 0, 0)),
            pl.BlockSpec((2, nf, ny, nz), const4),
        ),
        scratch_shapes=[pltpu.VMEM((nf, nx + 5, ny, nz), F32)],
        compiler_params=pltpu.CompilerParams(dimension_semantics=("arbitrary",)),
    )(flux_plus, flux_minus, adjoint, xf, yf, zf, stencil_weights)
    axl = shift_from(xl, "gx", -1)
    axr = shift_from(xr, "gx", 1)
    ayl = shift_from(yl, "gy", -1)
    ayr = shift_from(yr, "gy", 1)
    if lax.axis_size("gz") == 2:
        az = shift_from(zz, "gz", 1)
    else:
        az = jnp.stack([shift_from(zz[0], "gz", -1), shift_from(zz[1], "gz", 1)])
    nr = wall_row.shape[0]
    section, wt = pl.pallas_call(
        fix_kernel,
        out_shape=(
            jax.ShapeDtypeStruct((nf, nx, ny, nz), F32),
            jax.ShapeDtypeStruct((nr, nz), F32),
        ),
        in_specs=[SMEM, SMEM, HBM] + [VMEM] * 6,
        out_specs=(HBM, VMEM),
        scratch_shapes=[
            pltpu.VMEM((nf, nx, ny, nz), F32),
            pltpu.SemaphoreType.DMA((nx // XC,)),
            pltpu.SemaphoreType.DMA((nx // XC,)),
        ],
        input_output_aliases={2: 0},
    )(wall_row, wall_count, sec, axl, axr, ayl, ayr, az, wall_coef)

    npan = panel_owner.shape[0]
    per = npan // ndev
    nb = 32
    na = npan // nb
    own_oh = (panel_owner[:, None] == jnp.arange(ndev, dtype=jnp.int32)).astype(F32)
    oh3 = own_oh.reshape(na, nb, ndev)
    below_b = (jnp.arange(nb)[None, :] < jnp.arange(nb)[:, None]).astype(F32)
    below_a = (jnp.arange(na)[None, :] < jnp.arange(na)[:, None]).astype(F32)
    inner = jnp.einsum("bc,acd->abd", below_b, oh3, precision=HI)
    before = jnp.einsum("ac,cd->ad", below_a, jnp.sum(oh3, axis=1), precision=HI)
    rank = jnp.sum((inner + before[:, None, :]) * oh3, axis=2)
    oh_a = (wall_panel[..., None] // nb == jnp.arange(na, dtype=jnp.int32)).astype(F32)
    oh_b = (wall_panel[..., None] % nb == jnp.arange(nb, dtype=jnp.int32)).astype(F32)

    def lookup(table):
        picked = jnp.einsum("rza,ab->rzb", oh_a, table, precision=HI) * oh_b
        return jnp.round(jnp.sum(picked, axis=2)).astype(jnp.int32)

    cell_own = lookup(panel_owner.reshape(na, nb).astype(F32))
    cell_rank = lookup(rank)
    oh_o = (cell_own[..., None] == jnp.arange(ndev, dtype=jnp.int32)).astype(F32)
    oh_k = (cell_rank[..., None] == jnp.arange(per, dtype=jnp.int32)).astype(F32)
    t = jnp.einsum("rzo,rzk->ok", oh_o * wt[..., None], oh_k, precision=HI)
    got = lax.all_to_all(t, AXES, 0, 0, tiled=True)
    return section, jnp.sum(got, axis=0)


def solution(mesh):
    ndev = mesh.size
    placed = (
        P(None, "gx", "gy", "gz"),
        P(None, None, None, None, "gx", "gy", "gz"),
        P(),
        P(),
        P(AXES),
        P(AXES, None),
        P(None, AXES, None),
        P(AXES),
        P(),
    )
    return jax.shard_map(
        lambda *args: on_device(ndev, *args),
        mesh=mesh,
        in_specs=placed,
        out_specs=(P(None, "gx", "gy", "gz"), P(AXES)),
        check_vma=False,
    )
```

```python
import jax
import jax.numpy as jnp
from jax import lax
from jax.experimental import pallas as pl
from jax.experimental.pallas import tpu as pltpu
from jax.sharding import PartitionSpec as P

AXES = ("gx", "gy", "gz")
STEP = 0.4
SECTION = 0.25
XC = 4
F32 = jnp.float32
HI = lax.Precision.HIGHEST
VMEM = pl.BlockSpec(memory_space=pltpu.VMEM)
SMEM = pl.BlockSpec(memory_space=pltpu.SMEM)


def shift_from(x, axis, by):
    n = lax.axis_size(axis)
    return lax.ppermute(x, axis, [(i, (i + by) % n) for i in range(n)])


def iotas(ny, nz):
    return (
        lax.broadcasted_iota(jnp.int32, (ny, nz), 0),
        lax.broadcasted_iota(jnp.int32, (ny, nz), 1),
    )


def fronts_kernel(adj_ref, xf_ref, yf_ref, zf_ref):
    nf, nx, ny, nz = adj_ref.shape
    row, lane = iotas(ny, nz)
    for f in range(nf):
        xf_ref[f] = adj_ref[f, 0]
        zacc = jnp.zeros((ny, nz), F32)
        for x in range(nx):
            s = adj_ref[f, x]
            yf_ref[f, pl.ds(x, 1), :] = s[0:1, :]
            zacc = zacc + pltpu.roll(jnp.where(lane == 0, s, 0.0), x, 1)
        zf_ref[f] = zacc


def offset_terms(plus, minus, w):
    p0, p1, p2 = plus * w(0, 0), plus * w(0, 1), plus * w(0, 2)
    m0, m1, m2 = minus * w(1, 0), minus * w(1, 1), minus * w(1, 2)
    a = p1 + m2
    b = p2 + m1
    return [
        p0 * (1.0 / 3.0),
        p0 * (-7.0 / 6.0) + a * (-1.0 / 6.0),
        p0 * (11.0 / 6.0) + a * (5.0 / 6.0) + b * (1.0 / 3.0),
        a * (1.0 / 3.0) + b * (5.0 / 6.0) + m0 * (11.0 / 6.0),
        b * (-1.0 / 6.0) + m0 * (-7.0 / 6.0),
        m0 * (1.0 / 3.0),
    ]


def rolled_sum(terms, n, axis):
    r = {o: pltpu.roll(terms[o], (o - 2) % n, axis) for o in (0, 1, 3, 4, 5)}
    tot = terms[2] + r[0] + r[1] + r[3] + r[4] + r[5]
    return r, tot


def split_rows(terms, row8, ny):
    r, tot = rolled_sum(terms, ny, 0)
    h = ny - 8
    wr = (jnp.where(row8 < 1, r[3][0:8], 0.0) + jnp.where(row8 < 2, r[4][0:8], 0.0)
          + jnp.where(row8 < 3, r[5][0:8], 0.0))
    wl = jnp.where(row8 >= 6, r[0][h:ny], 0.0) + jnp.where(row8 >= 7, r[1][h:ny], 0.0)
    inner = jnp.concatenate([tot[0:8] - wr, tot[8:h], tot[h:ny] - wl], 0) if h > 8 else \
        jnp.concatenate([tot[0:8] - wr, tot[h:ny] - wl], 0)
    return inner, wr, wl


def split_lanes(terms, lane, nz):
    r, tot = rolled_sum(terms, nz, 1)
    wr = jnp.where(lane < 1, r[3], 0.0) + jnp.where(lane < 2, r[4], 0.0) + jnp.where(lane < 3, r[5], 0.0)
    wl = jnp.where(lane >= nz - 2, r[0], 0.0) + jnp.where(lane >= nz - 1, r[1], 0.0)
    return tot - wr - wl, wr, wl


def stencil_kernel(fp_ref, fm_ref, adj_ref, xf_ref, yf_ref, zf_ref, w_ref,
                   sec_ref, xl_ref, xr_ref, yl_ref, yr_ref, zz_ref, acc_ref):
    nf, nx, ny, nz = adj_ref.shape
    i = pl.program_id(0)
    row, lane = iotas(ny, nz)
    row8 = lax.broadcasted_iota(jnp.int32, (8, nz), 0)

    @pl.when(i == 0)
    def _():
        acc_ref[...] = jnp.zeros_like(acc_ref)
        zz_ref[...] = jnp.zeros_like(zz_ref)

    def flux(d, diff):
        plus, minus = [], []
        for f in range(nf):
            p = m = None
            for g in range(nf):
                tp = diff[g] * (STEP * fp_ref[d, g, f])
                tm = diff[g] * (STEP * fm_ref[d, g, f])
                p = tp if p is None else p + tp
                m = tm if m is None else m + tm
            plus.append(p)
            minus.append(m)
        return plus, minus

    yr_parts = {}
    yl_parts = {}
    for xl in range(XC):
        x = i * XC + xl
        last = x == nx - 1
        nxt = jnp.minimum(x + 1, nx - 1)
        a = [adj_ref[f, x] for f in range(nf)]
        plus, minus = flux(0, [jnp.where(last, xf_ref[g], adj_ref[g, nxt]) - a[g] for g in range(nf)])
        for f in range(nf):
            sx = offset_terms(plus[f], minus[f], lambda s, k: w_ref[0, s, k, f, xl])
            for o in range(6):
                acc_ref[f, x + o] = acc_ref[f, x + o] + sx[o]
        a = [adj_ref[f, x] for f in range(nf)]
        plus, minus = flux(1, [
            jnp.where(row == ny - 1, yf_ref[g, pl.ds(x, 1), :], pltpu.roll(a[g], ny - 1, 0)) - a[g]
            for g in range(nf)
        ])
        for f in range(nf):
            sy = offset_terms(plus[f], minus[f], lambda s, k: w_ref[1, s, k, f, xl])
            iy, wyr, wyl = split_rows(sy, row8, ny)
            acc_ref[f, x + 2] = acc_ref[f, x + 2] + iy
            rear = pltpu.roll(wyr, 4 * (xl % 2), 0)
            lead = pltpu.roll(wyl, (2 + 2 * (xl % 4)) % 8, 0)
            kr = (f, xl // 2)
            kl = (f, xl // 4)
            yr_parts[kr] = rear if kr not in yr_parts else yr_parts[kr] + rear
            yl_parts[kl] = lead if kl not in yl_parts else yl_parts[kl] + lead
        a = [adj_ref[f, x] for f in range(nf)]
        zshift = nz - 1 - x
        plus, minus = flux(2, [
            jnp.where(lane == nz - 1, pltpu.roll(zf_ref[g], zshift, 1), pltpu.roll(a[g], nz - 1, 1)) - a[g]
            for g in range(nf)
        ])
        for f in range(nf):
            sz = offset_terms(plus[f], minus[f], lambda s, k: w_ref[2, s, k, f, xl])
            iz, wzr, wzl = split_lanes(sz, lane, nz)
            acc_ref[f, x + 2] = acc_ref[f, x + 2] + iz
            zz_ref[0, f] = zz_ref[0, f] + pltpu.roll(wzl, 2 + 4 * x, 1)
            zz_ref[1, f] = zz_ref[1, f] + pltpu.roll(wzr, 4 * x, 1)
    for (f, t), v in yr_parts.items():
        yr_ref[f, t] = v
    for (f, t), v in yl_parts.items():
        yl_ref[f, t] = v

    @pl.when(i == pl.num_programs(0) - 1)
    def _():
        def body(x, c):
            for f in range(nf):
                sec_ref[f, x] = SECTION * (adj_ref[f, x] + acc_ref[f, x + 2])
            return c

        lax.fori_loop(0, nx, body, 0)
        for f in range(nf):
            xl_ref[f] = acc_ref[f, 0:2]
            xr_ref[f] = acc_ref[f, nx + 2:nx + 5]


def fix_kernel(row_ref, cnt_ref, sec_ref, axl_ref, axr_ref, ayl_ref, ayr_ref, az_ref,
               coef_ref, own_ref, rank_ref, out_ref, t_ref):
    nf, nx, ny, nz = sec_ref.shape
    row, lane = iotas(ny, nz)
    pad = jnp.zeros((ny - 8, nz), F32)
    for x in range(nx):
        for f in range(nf):
            ty = jnp.concatenate([ayr_ref[f, x // 2], pad], 0)
            add = jnp.where(row < 3, pltpu.roll(ty, (ny - 4 * (x % 2)) % ny, 0), 0.0)
            ty = jnp.concatenate([ayl_ref[f, x // 4], pad], 0)
            add = add + jnp.where(row >= ny - 2, pltpu.roll(ty, (ny - 2 - 2 * (x % 4)) % ny, 0), 0.0)
            add = add + jnp.where(lane < 3, pltpu.roll(az_ref[1, f], (nz - 4 * x) % nz, 1), 0.0)
            add = add + jnp.where(lane >= nz - 2, pltpu.roll(az_ref[0, f], (nz - 2 - 4 * x) % nz, 1), 0.0)
            if x < 3:
                add = add + axr_ref[f, x]
            if x >= nx - 2:
                add = add + axl_ref[f, x - (nx - 2)]
            out_ref[f, x] = sec_ref[f, x] + SECTION * add
    live_n = cnt_ref[0]
    ndev, per = t_ref.shape
    own_ids = lax.broadcasted_iota(jnp.int32, (ndev, nz), 0)
    rank_ids = lax.broadcasted_iota(jnp.int32, (per, nz), 0)
    total = jnp.zeros((ndev, per), F32)
    for r in range(coef_ref.shape[1]):
        idx = row_ref[r]
        lx = idx // ny
        ly = idx % ny
        val = None
        for f in range(nf):
            v = out_ref[f, lx, pl.ds(ly, 1), :] * coef_ref[f, pl.ds(r, 1), :]
            val = v if val is None else val + v
        val = val * jnp.where(r < live_n, 1.0, 0.0).astype(F32)
        a = jnp.where(own_ref[pl.ds(r, 1), :] == own_ids, val, 0.0)
        b = jnp.where(rank_ref[pl.ds(r, 1), :] == rank_ids, 1.0, 0.0)
        total = total + lax.dot_general(a, b, (((1,), (1,)), ((), ())), precision=HI,
                                        preferred_element_type=F32)
    t_ref[...] = total


def on_device(ndev, adjoint, stencil_weights, flux_plus, flux_minus, wall_row, wall_panel, wall_coef,
              wall_count, panel_owner):
    nf, nx, ny, nz = adjoint.shape
    assert nx % XC == 0 and XC % 4 == 0 and ny == 16 and nx * 4 <= nz
    xf, yf, zf = pl.pallas_call(
        fronts_kernel,
        out_shape=(
            jax.ShapeDtypeStruct((nf, ny, nz), F32),
            jax.ShapeDtypeStruct((nf, nx, nz), F32),
            jax.ShapeDtypeStruct((nf, ny, nz), F32),
        ),
        in_specs=[VMEM],
        out_specs=(VMEM, VMEM, VMEM),
    )(adjoint)
    xf = shift_from(xf, "gx", -1)
    yf = shift_from(yf, "gy", -1)
    zf = shift_from(zf, "gz", -1)
    const4 = lambda i: (0, 0, 0, 0)
    const3 = lambda i: (0, 0, 0)
    sec, xl, xr, yl, yr, zz = pl.pallas_call(
        stencil_kernel,
        grid=(nx // XC,),
        out_shape=(
            jax.ShapeDtypeStruct((nf, nx, ny, nz), F32),
            jax.ShapeDtypeStruct((nf, 2, ny, nz), F32),
            jax.ShapeDtypeStruct((nf, 3, ny, nz), F32),
            jax.ShapeDtypeStruct((nf, nx // 4, 8, nz), F32),
            jax.ShapeDtypeStruct((nf, nx // 2, 8, nz), F32),
            jax.ShapeDtypeStruct((2, nf, ny, nz), F32),
        ),
        in_specs=[
            SMEM,
            SMEM,
            pl.BlockSpec((nf, nx, ny, nz), const4),
            pl.BlockSpec((nf, ny, nz), const3),
            pl.BlockSpec((nf, nx, nz), const3),
            pl.BlockSpec((nf, ny, nz), const3),
            pl.BlockSpec((3, 2, 3, nf, XC, ny, nz), lambda i: (0, 0, 0, 0, i, 0, 0)),
        ],
        out_specs=(
            pl.BlockSpec((nf, nx, ny, nz), const4),
            pl.BlockSpec((nf, 2, ny, nz), const4),
            pl.BlockSpec((nf, 3, ny, nz), const4),
            pl.BlockSpec((nf, XC // 4, 8, nz), lambda i: (0, i, 0, 0)),
            pl.BlockSpec((nf, XC // 2, 8, nz), lambda i: (0, i, 0, 0)),
            pl.BlockSpec((2, nf, ny, nz), const4),
        ),
        scratch_shapes=[pltpu.VMEM((nf, nx + 5, ny, nz), F32)],
        compiler_params=pltpu.CompilerParams(dimension_semantics=("arbitrary",)),
    )(flux_plus, flux_minus, adjoint, xf, yf, zf, stencil_weights)
    axl = shift_from(xl, "gx", -1)
    axr = shift_from(xr, "gx", 1)
    ayl = shift_from(yl, "gy", -1)
    ayr = shift_from(yr, "gy", 1)
    if lax.axis_size("gz") == 2:
        az = shift_from(zz, "gz", 1)
    else:
        az = jnp.stack([shift_from(zz[0], "gz", -1), shift_from(zz[1], "gz", 1)])
    npan = panel_owner.shape[0]
    per = npan // ndev
    nb = 32
    na = npan // nb
    own_oh = (panel_owner[:, None] == jnp.arange(ndev, dtype=jnp.int32)).astype(F32)
    oh3 = own_oh.reshape(na, nb, ndev)
    below_b = (jnp.arange(nb)[None, :] < jnp.arange(nb)[:, None]).astype(F32)
    below_a = (jnp.arange(na)[None, :] < jnp.arange(na)[:, None]).astype(F32)
    inner = jnp.einsum("bc,acd->abd", below_b, oh3, precision=HI)
    before = jnp.einsum("ac,cd->ad", below_a, jnp.sum(oh3, axis=1), precision=HI)
    rank = jnp.sum((inner + before[:, None, :]) * oh3, axis=2)
    oh_a = (wall_panel[..., None] // nb == jnp.arange(na, dtype=jnp.int32)).astype(F32)
    oh_b = (wall_panel[..., None] % nb == jnp.arange(nb, dtype=jnp.int32)).astype(F32)

    def lookup(table):
        picked = jnp.einsum("rza,ab->rzb", oh_a, table, precision=HI) * oh_b
        return jnp.round(jnp.sum(picked, axis=2)).astype(jnp.int32)

    cell_own = lookup(panel_owner.reshape(na, nb).astype(F32))
    cell_rank = lookup(rank)
    nr = wall_row.shape[0]
    section, t = pl.pallas_call(
        fix_kernel,
        out_shape=(
            jax.ShapeDtypeStruct((nf, nx, ny, nz), F32),
            jax.ShapeDtypeStruct((ndev, per), F32),
        ),
        in_specs=[SMEM, SMEM] + [VMEM] * 9,
        out_specs=(VMEM, VMEM),
        input_output_aliases={2: 0},
    )(wall_row, wall_count, sec, axl, axr, ayl, ayr, az, wall_coef, cell_own, cell_rank)

    got = lax.all_to_all(t, AXES, 0, 0, tiled=True)
    return section, jnp.sum(got, axis=0)


def solution(mesh):
    ndev = mesh.size
    placed = (
        P(None, "gx", "gy", "gz"),
        P(None, None, None, None, "gx", "gy", "gz"),
        P(),
        P(),
        P(AXES),
        P(AXES, None),
        P(None, AXES, None),
        P(AXES),
        P(),
    )
    return jax.shard_map(
        lambda *args: on_device(ndev, *args),
        mesh=mesh,
        in_specs=placed,
        out_specs=(P(None, "gx", "gy", "gz"), P(AXES)),
        check_vma=False,
    )
```

```python
import jax
import jax.numpy as jnp
from jax import lax
from jax.experimental import pallas as pl
from jax.experimental.pallas import tpu as pltpu
from jax.sharding import PartitionSpec as P

AXES = ("gx", "gy", "gz")
STEP = 0.4
SECTION = 0.25
XC = 4
F32 = jnp.float32
HI = lax.Precision.HIGHEST
VMEM = pl.BlockSpec(memory_space=pltpu.VMEM)
SMEM = pl.BlockSpec(memory_space=pltpu.SMEM)


def shift_from(x, axis, by):
    n = lax.axis_size(axis)
    return lax.ppermute(x, axis, [(i, (i + by) % n) for i in range(n)])


def iotas(ny, nz):
    return (
        lax.broadcasted_iota(jnp.int32, (ny, nz), 0),
        lax.broadcasted_iota(jnp.int32, (ny, nz), 1),
    )


def fronts_kernel(adj_ref, xf_ref, yf_ref, zf_ref):
    nf, nx, ny, nz = adj_ref.shape
    row, lane = iotas(ny, nz)
    for f in range(nf):
        xf_ref[f] = adj_ref[f, 0]
        zacc = jnp.zeros((ny, nz), F32)
        for x in range(nx):
            s = adj_ref[f, x]
            yf_ref[f, pl.ds(x, 1), :] = s[0:1, :]
            zacc = zacc + pltpu.roll(jnp.where(lane == 0, s, 0.0), x, 1)
        zf_ref[f] = zacc


def offset_terms(plus, minus, w):
    p0, p1, p2 = plus * w(0, 0), plus * w(0, 1), plus * w(0, 2)
    m0, m1, m2 = minus * w(1, 0), minus * w(1, 1), minus * w(1, 2)
    a = p1 + m2
    b = p2 + m1
    return [
        p0 * (1.0 / 3.0),
        p0 * (-7.0 / 6.0) + a * (-1.0 / 6.0),
        p0 * (11.0 / 6.0) + a * (5.0 / 6.0) + b * (1.0 / 3.0),
        a * (1.0 / 3.0) + b * (5.0 / 6.0) + m0 * (11.0 / 6.0),
        b * (-1.0 / 6.0) + m0 * (-7.0 / 6.0),
        m0 * (1.0 / 3.0),
    ]


def rolled_sum(terms, n, axis):
    r = {o: pltpu.roll(terms[o], (o - 2) % n, axis) for o in (0, 1, 3, 4, 5)}
    tot = terms[2] + r[0] + r[1] + r[3] + r[4] + r[5]
    return r, tot


def split_rows(terms, row8, ny):
    r, tot = rolled_sum(terms, ny, 0)
    h = ny - 8
    wr = (jnp.where(row8 < 1, r[3][0:8], 0.0) + jnp.where(row8 < 2, r[4][0:8], 0.0)
          + jnp.where(row8 < 3, r[5][0:8], 0.0))
    wl = jnp.where(row8 >= 6, r[0][h:ny], 0.0) + jnp.where(row8 >= 7, r[1][h:ny], 0.0)
    inner = jnp.concatenate([tot[0:8] - wr, tot[8:h], tot[h:ny] - wl], 0) if h > 8 else \
        jnp.concatenate([tot[0:8] - wr, tot[h:ny] - wl], 0)
    return inner, wr, wl


def split_lanes(terms, lane, nz):
    r, tot = rolled_sum(terms, nz, 1)
    wr = jnp.where(lane < 1, r[3], 0.0) + jnp.where(lane < 2, r[4], 0.0) + jnp.where(lane < 3, r[5], 0.0)
    wl = jnp.where(lane >= nz - 2, r[0], 0.0) + jnp.where(lane >= nz - 1, r[1], 0.0)
    return tot - wr - wl, wr, wl


def stencil_kernel(fp_ref, fm_ref, adj_ref, xf_ref, yf_ref, zf_ref, w_ref,
                   sec_ref, xl_ref, xr_ref, yl_ref, yr_ref, zz_ref, acc_ref):
    nf, nx, ny, nz = adj_ref.shape
    i = pl.program_id(0)
    row, lane = iotas(ny, nz)
    row8 = lax.broadcasted_iota(jnp.int32, (8, nz), 0)

    @pl.when(i == 0)
    def _():
        acc_ref[...] = jnp.zeros_like(acc_ref)
        zz_ref[...] = jnp.zeros_like(zz_ref)

    def flux(d, diff):
        plus, minus = [], []
        for f in range(nf):
            p = m = None
            for g in range(nf):
                tp = diff[g] * (STEP * fp_ref[d, g, f])
                tm = diff[g] * (STEP * fm_ref[d, g, f])
                p = tp if p is None else p + tp
                m = tm if m is None else m + tm
            plus.append(p)
            minus.append(m)
        return plus, minus

    yr_parts = {}
    yl_parts = {}
    for xl in range(XC):
        x = i * XC + xl
        last = x == nx - 1
        nxt = jnp.minimum(x + 1, nx - 1)
        a = [adj_ref[f, x] for f in range(nf)]
        plus, minus = flux(0, [jnp.where(last, xf_ref[g], adj_ref[g, nxt]) - a[g] for g in range(nf)])
        for f in range(nf):
            sx = offset_terms(plus[f], minus[f], lambda s, k: w_ref[0, s, k, f, xl])
            for o in range(6):
                acc_ref[f, x + o] = acc_ref[f, x + o] + sx[o]
        a = [adj_ref[f, x] for f in range(nf)]
        plus, minus = flux(1, [
            jnp.where(row == ny - 1, yf_ref[g, pl.ds(x, 1), :], pltpu.roll(a[g], ny - 1, 0)) - a[g]
            for g in range(nf)
        ])
        for f in range(nf):
            sy = offset_terms(plus[f], minus[f], lambda s, k: w_ref[1, s, k, f, xl])
            iy, wyr, wyl = split_rows(sy, row8, ny)
            acc_ref[f, x + 2] = acc_ref[f, x + 2] + iy
            rear = pltpu.roll(wyr, 4 * (xl % 2), 0)
            lead = pltpu.roll(wyl, (2 + 2 * (xl % 4)) % 8, 0)
            kr = (f, xl // 2)
            kl = (f, xl // 4)
            yr_parts[kr] = rear if kr not in yr_parts else yr_parts[kr] + rear
            yl_parts[kl] = lead if kl not in yl_parts else yl_parts[kl] + lead
        a = [adj_ref[f, x] for f in range(nf)]
        zshift = nz - 1 - x
        plus, minus = flux(2, [
            jnp.where(lane == nz - 1, pltpu.roll(zf_ref[g], zshift, 1), pltpu.roll(a[g], nz - 1, 1)) - a[g]
            for g in range(nf)
        ])
        for f in range(nf):
            sz = offset_terms(plus[f], minus[f], lambda s, k: w_ref[2, s, k, f, xl])
            iz, wzr, wzl = split_lanes(sz, lane, nz)
            acc_ref[f, x + 2] = acc_ref[f, x + 2] + iz
            zz_ref[0, f] = zz_ref[0, f] + pltpu.roll(wzl, 2 + 4 * x, 1)
            zz_ref[1, f] = zz_ref[1, f] + pltpu.roll(wzr, 4 * x, 1)
    for (f, t), v in yr_parts.items():
        yr_ref[f, t] = v
    for (f, t), v in yl_parts.items():
        yl_ref[f, t] = v

    @pl.when(i == pl.num_programs(0) - 1)
    def _():
        def body(x, c):
            for f in range(nf):
                sec_ref[f, x] = SECTION * (adj_ref[f, x] + acc_ref[f, x + 2])
            return c

        lax.fori_loop(0, nx, body, 0)
        for f in range(nf):
            xl_ref[f] = acc_ref[f, 0:2]
            xr_ref[f] = acc_ref[f, nx + 2:nx + 5]


def fix_kernel(row_ref, cnt_ref, sec_ref, axl_ref, axr_ref, ayl_ref, ayr_ref, az_ref,
               coef_ref, own_ref, rank_ref, out_ref, t_ref):
    nf, nx, ny, nz = sec_ref.shape
    row, lane = iotas(ny, nz)
    pad = jnp.zeros((ny - 8, nz), F32)
    for x in range(nx):
        for f in range(nf):
            ty = jnp.concatenate([ayr_ref[f, x // 2], pad], 0)
            add = jnp.where(row < 3, pltpu.roll(ty, (ny - 4 * (x % 2)) % ny, 0), 0.0)
            ty = jnp.concatenate([ayl_ref[f, x // 4], pad], 0)
            add = add + jnp.where(row >= ny - 2, pltpu.roll(ty, (ny - 2 - 2 * (x % 4)) % ny, 0), 0.0)
            add = add + jnp.where(lane < 3, pltpu.roll(az_ref[1, f], (nz - 4 * x) % nz, 1), 0.0)
            add = add + jnp.where(lane >= nz - 2, pltpu.roll(az_ref[0, f], (nz - 2 - 4 * x) % nz, 1), 0.0)
            if x < 3:
                add = add + axr_ref[f, x]
            if x >= nx - 2:
                add = add + axl_ref[f, x - (nx - 2)]
            out_ref[f, x] = sec_ref[f, x] + SECTION * add
    live_n = cnt_ref[0]
    ndev, per = t_ref.shape
    own_ids = lax.broadcasted_iota(jnp.int32, (ndev, nz), 0)
    rank_ids = lax.broadcasted_iota(jnp.int32, (per, nz), 0)
    total = jnp.zeros((ndev, per), F32)
    for r in range(coef_ref.shape[1]):
        idx = row_ref[r]
        lx = idx // ny
        ly = idx % ny
        val = None
        for f in range(nf):
            v = out_ref[f, lx, pl.ds(ly, 1), :] * coef_ref[f, pl.ds(r, 1), :]
            val = v if val is None else val + v
        val = val * jnp.where(r < live_n, 1.0, 0.0).astype(F32)
        a = jnp.where(own_ref[pl.ds(r, 1), :] == own_ids, val, 0.0)
        b = jnp.where(rank_ref[pl.ds(r, 1), :] == rank_ids, 1.0, 0.0)
        total = total + lax.dot_general(a, b, (((1,), (1,)), ((), ())), precision=HI,
                                        preferred_element_type=F32)
    t_ref[...] = total


def on_device(ndev, adjoint, stencil_weights, flux_plus, flux_minus, wall_row, wall_panel, wall_coef,
              wall_count, panel_owner):
    nf, nx, ny, nz = adjoint.shape
    assert nx % XC == 0 and XC % 4 == 0 and ny == 16 and nx * 4 <= nz
    xf, yf, zf = pl.pallas_call(
        fronts_kernel,
        out_shape=(
            jax.ShapeDtypeStruct((nf, ny, nz), F32),
            jax.ShapeDtypeStruct((nf, nx, nz), F32),
            jax.ShapeDtypeStruct((nf, ny, nz), F32),
        ),
        in_specs=[VMEM],
        out_specs=(VMEM, VMEM, VMEM),
    )(adjoint)
    xf = shift_from(xf, "gx", -1)
    yf = shift_from(yf, "gy", -1)
    zf = shift_from(zf, "gz", -1)
    const4 = lambda i: (0, 0, 0, 0)
    const3 = lambda i: (0, 0, 0)
    sec, xl, xr, yl, yr, zz = pl.pallas_call(
        stencil_kernel,
        grid=(nx // XC,),
        out_shape=(
            jax.ShapeDtypeStruct((nf, nx, ny, nz), F32),
            jax.ShapeDtypeStruct((nf, 2, ny, nz), F32),
            jax.ShapeDtypeStruct((nf, 3, ny, nz), F32),
            jax.ShapeDtypeStruct((nf, nx // 4, 8, nz), F32),
            jax.ShapeDtypeStruct((nf, nx // 2, 8, nz), F32),
            jax.ShapeDtypeStruct((2, nf, ny, nz), F32),
        ),
        in_specs=[
            SMEM,
            SMEM,
            pl.BlockSpec((nf, nx, ny, nz), const4),
            pl.BlockSpec((nf, ny, nz), const3),
            pl.BlockSpec((nf, nx, nz), const3),
            pl.BlockSpec((nf, ny, nz), const3),
            pl.BlockSpec((3, 2, 3, nf, XC, ny, nz), lambda i: (0, 0, 0, 0, i, 0, 0)),
        ],
        out_specs=(
            pl.BlockSpec((nf, nx, ny, nz), const4),
            pl.BlockSpec((nf, 2, ny, nz), const4),
            pl.BlockSpec((nf, 3, ny, nz), const4),
            pl.BlockSpec((nf, XC // 4, 8, nz), lambda i: (0, i, 0, 0)),
            pl.BlockSpec((nf, XC // 2, 8, nz), lambda i: (0, i, 0, 0)),
            pl.BlockSpec((2, nf, ny, nz), const4),
        ),
        scratch_shapes=[pltpu.VMEM((nf, nx + 5, ny, nz), F32)],
        compiler_params=pltpu.CompilerParams(dimension_semantics=("arbitrary",)),
    )(flux_plus, flux_minus, adjoint, xf, yf, zf, stencil_weights)
    axl = shift_from(xl, "gx", -1)
    axr = shift_from(xr, "gx", 1)
    ayl = shift_from(yl, "gy", -1)
    ayr = shift_from(yr, "gy", 1)
    if lax.axis_size("gz") == 2:
        az = shift_from(zz, "gz", 1)
    else:
        az = jnp.stack([shift_from(zz[0], "gz", -1), shift_from(zz[1], "gz", 1)])
    az, wall_panel, panel_owner = lax.optimization_barrier((az, wall_panel, panel_owner))
    npan = panel_owner.shape[0]
    per = npan // ndev
    nb = 32
    na = npan // nb
    own_oh = (panel_owner[:, None] == jnp.arange(ndev, dtype=jnp.int32)).astype(F32)
    oh3 = own_oh.reshape(na, nb, ndev)
    below_b = (jnp.arange(nb)[None, :] < jnp.arange(nb)[:, None]).astype(F32)
    below_a = (jnp.arange(na)[None, :] < jnp.arange(na)[:, None]).astype(F32)
    inner = jnp.einsum("bc,acd->abd", below_b, oh3, precision=HI)
    before = jnp.einsum("ac,cd->ad", below_a, jnp.sum(oh3, axis=1), precision=HI)
    rank = jnp.sum((inner + before[:, None, :]) * oh3, axis=2)
    oh_a = (wall_panel[..., None] // nb == jnp.arange(na, dtype=jnp.int32)).astype(F32)
    oh_b = (wall_panel[..., None] % nb == jnp.arange(nb, dtype=jnp.int32)).astype(F32)

    def lookup(table):
        picked = jnp.einsum("rza,ab->rzb", oh_a, table, precision=HI) * oh_b
        return jnp.round(jnp.sum(picked, axis=2)).astype(jnp.int32)

    cell_own = lookup(panel_owner.reshape(na, nb).astype(F32))
    cell_rank = lookup(rank)
    nr = wall_row.shape[0]
    section, t = pl.pallas_call(
        fix_kernel,
        out_shape=(
            jax.ShapeDtypeStruct((nf, nx, ny, nz), F32),
            jax.ShapeDtypeStruct((ndev, per), F32),
        ),
        in_specs=[SMEM, SMEM] + [VMEM] * 9,
        out_specs=(VMEM, VMEM),
        input_output_aliases={2: 0},
    )(wall_row, wall_count, sec, axl, axr, ayl, ayr, az, wall_coef, cell_own, cell_rank)

    got = lax.all_to_all(t, AXES, 0, 0, tiled=True)
    return section, jnp.sum(got, axis=0)


def solution(mesh):
    ndev = mesh.size
    placed = (
        P(None, "gx", "gy", "gz"),
        P(None, None, None, None, "gx", "gy", "gz"),
        P(),
        P(),
        P(AXES),
        P(AXES, None),
        P(None, AXES, None),
        P(AXES),
        P(),
    )
    return jax.shard_map(
        lambda *args: on_device(ndev, *args),
        mesh=mesh,
        in_specs=placed,
        out_specs=(P(None, "gx", "gy", "gz"), P(AXES)),
        check_vma=False,
    )
```

```python
import jax
import jax.numpy as jnp
from jax import lax
from jax.experimental import pallas as pl
from jax.experimental.pallas import tpu as pltpu
from jax.sharding import PartitionSpec as P

AXES = ("gx", "gy", "gz")
STEP = 0.4
SECTION = 0.25
XC = 4
F32 = jnp.float32
HI = lax.Precision.HIGHEST
VMEM = pl.BlockSpec(memory_space=pltpu.VMEM)
SMEM = pl.BlockSpec(memory_space=pltpu.SMEM)


def shift_from(x, axis, by):
    n = lax.axis_size(axis)
    return lax.ppermute(x, axis, [(i, (i + by) % n) for i in range(n)])


def iotas(ny, nz):
    return (
        lax.broadcasted_iota(jnp.int32, (ny, nz), 0),
        lax.broadcasted_iota(jnp.int32, (ny, nz), 1),
    )


def fronts_kernel(adj_ref, xf_ref, yf_ref, zf_ref):
    nf, nx, ny, nz = adj_ref.shape
    row, lane = iotas(ny, nz)
    for f in range(nf):
        xf_ref[f] = adj_ref[f, 0]
        zacc = jnp.zeros((ny, nz), F32)
        for x in range(nx):
            s = adj_ref[f, x]
            yf_ref[f, pl.ds(x, 1), :] = s[0:1, :]
            zacc = zacc + pltpu.roll(jnp.where(lane == 0, s, 0.0), x, 1)
        zf_ref[f] = zacc


def offset_terms(plus, minus, w):
    p0, p1, p2 = plus * w(0, 0), plus * w(0, 1), plus * w(0, 2)
    m0, m1, m2 = minus * w(1, 0), minus * w(1, 1), minus * w(1, 2)
    a = p1 + m2
    b = p2 + m1
    return [
        p0 * (1.0 / 3.0),
        p0 * (-7.0 / 6.0) + a * (-1.0 / 6.0),
        p0 * (11.0 / 6.0) + a * (5.0 / 6.0) + b * (1.0 / 3.0),
        a * (1.0 / 3.0) + b * (5.0 / 6.0) + m0 * (11.0 / 6.0),
        b * (-1.0 / 6.0) + m0 * (-7.0 / 6.0),
        m0 * (1.0 / 3.0),
    ]


def rolled_sum(terms, n, axis):
    r = {o: pltpu.roll(terms[o], (o - 2) % n, axis) for o in (0, 1, 3, 4, 5)}
    tot = terms[2] + r[0] + r[1] + r[3] + r[4] + r[5]
    return r, tot


def split_rows(terms, row8, ny):
    r, tot = rolled_sum(terms, ny, 0)
    h = ny - 8
    wr = (jnp.where(row8 < 1, r[3][0:8], 0.0) + jnp.where(row8 < 2, r[4][0:8], 0.0)
          + jnp.where(row8 < 3, r[5][0:8], 0.0))
    wl = jnp.where(row8 >= 6, r[0][h:ny], 0.0) + jnp.where(row8 >= 7, r[1][h:ny], 0.0)
    inner = jnp.concatenate([tot[0:8] - wr, tot[8:h], tot[h:ny] - wl], 0) if h > 8 else \
        jnp.concatenate([tot[0:8] - wr, tot[h:ny] - wl], 0)
    return inner, wr, wl


def split_lanes(terms, lane, nz):
    r, tot = rolled_sum(terms, nz, 1)
    wr = jnp.where(lane < 1, r[3], 0.0) + jnp.where(lane < 2, r[4], 0.0) + jnp.where(lane < 3, r[5], 0.0)
    wl = jnp.where(lane >= nz - 2, r[0], 0.0) + jnp.where(lane >= nz - 1, r[1], 0.0)
    return tot - wr - wl, wr, wl


def stencil_kernel(fp_ref, fm_ref, adj_ref, xf_ref, yf_ref, zf_ref, w_ref,
                   sec_ref, xl_ref, xr_ref, yl_ref, yr_ref, zz_ref, acc_ref):
    nf, nx, ny, nz = adj_ref.shape
    i = pl.program_id(0)
    row, lane = iotas(ny, nz)
    row8 = lax.broadcasted_iota(jnp.int32, (8, nz), 0)

    @pl.when(i == 0)
    def _():
        acc_ref[...] = jnp.zeros_like(acc_ref)
        zz_ref[...] = jnp.zeros_like(zz_ref)

    def flux(d, diff):
        plus, minus = [], []
        for f in range(nf):
            p = m = None
            for g in range(nf):
                tp = diff[g] * (STEP * fp_ref[d, g, f])
                tm = diff[g] * (STEP * fm_ref[d, g, f])
                p = tp if p is None else p + tp
                m = tm if m is None else m + tm
            plus.append(p)
            minus.append(m)
        return plus, minus

    n = pl.num_programs(0) - 1

    @pl.when(i < n)
    def _():
        yr_parts = {}
        yl_parts = {}
        for xl in range(XC):
            x = i * XC + xl
            last = x == nx - 1
            nxt = jnp.minimum(x + 1, nx - 1)
            a = [adj_ref[f, x] for f in range(nf)]
            plus, minus = flux(0, [jnp.where(last, xf_ref[g], adj_ref[g, nxt]) - a[g] for g in range(nf)])
            for f in range(nf):
                sx = offset_terms(plus[f], minus[f], lambda s, k: w_ref[0, s, k, f, xl])
                for o in range(6):
                    acc_ref[f, x + o] = acc_ref[f, x + o] + sx[o]
            a = [adj_ref[f, x] for f in range(nf)]
            plus, minus = flux(1, [
                jnp.where(row == ny - 1, yf_ref[g, pl.ds(x, 1), :], pltpu.roll(a[g], ny - 1, 0)) - a[g]
                for g in range(nf)
            ])
            for f in range(nf):
                sy = offset_terms(plus[f], minus[f], lambda s, k: w_ref[1, s, k, f, xl])
                iy, wyr, wyl = split_rows(sy, row8, ny)
                acc_ref[f, x + 2] = acc_ref[f, x + 2] + iy
                rear = pltpu.roll(wyr, 4 * (xl % 2), 0)
                lead = pltpu.roll(wyl, (2 + 2 * (xl % 4)) % 8, 0)
                kr = (f, xl // 2)
                kl = (f, xl // 4)
                yr_parts[kr] = rear if kr not in yr_parts else yr_parts[kr] + rear
                yl_parts[kl] = lead if kl not in yl_parts else yl_parts[kl] + lead
            a = [adj_ref[f, x] for f in range(nf)]
            zshift = nz - 1 - x
            plus, minus = flux(2, [
                jnp.where(lane == nz - 1, pltpu.roll(zf_ref[g], zshift, 1), pltpu.roll(a[g], nz - 1, 1)) - a[g]
                for g in range(nf)
            ])
            for f in range(nf):
                sz = offset_terms(plus[f], minus[f], lambda s, k: w_ref[2, s, k, f, xl])
                iz, wzr, wzl = split_lanes(sz, lane, nz)
                acc_ref[f, x + 2] = acc_ref[f, x + 2] + iz
                zz_ref[0, f] = zz_ref[0, f] + pltpu.roll(wzl, 2 + 4 * x, 1)
                zz_ref[1, f] = zz_ref[1, f] + pltpu.roll(wzr, 4 * x, 1)
        for (f, t), v in yr_parts.items():
            yr_ref[f, t] = v
        for (f, t), v in yl_parts.items():
            yl_ref[f, t] = v

    @pl.when(i >= 1)
    def _():
        for xl in range(XC):
            x = (i - 1) * XC + xl
            for f in range(nf):
                sec_ref[f, xl] = SECTION * (adj_ref[f, x] + acc_ref[f, x + 2])

    @pl.when(i == n)
    def _():
        for f in range(nf):
            xl_ref[f] = acc_ref[f, 0:2]
            xr_ref[f] = acc_ref[f, nx + 2:nx + 5]


def fix_kernel(row_ref, cnt_ref, sec_ref, axl_ref, axr_ref, ayl_ref, ayr_ref, az_ref,
               coef_ref, own_ref, rank_ref, out_ref, t_ref):
    nf, nx, ny, nz = sec_ref.shape
    row, lane = iotas(ny, nz)
    pad = jnp.zeros((ny - 8, nz), F32)
    for x in range(nx):
        for f in range(nf):
            ty = jnp.concatenate([ayr_ref[f, x // 2], pad], 0)
            add = jnp.where(row < 3, pltpu.roll(ty, (ny - 4 * (x % 2)) % ny, 0), 0.0)
            ty = jnp.concatenate([ayl_ref[f, x // 4], pad], 0)
            add = add + jnp.where(row >= ny - 2, pltpu.roll(ty, (ny - 2 - 2 * (x % 4)) % ny, 0), 0.0)
            add = add + jnp.where(lane < 3, pltpu.roll(az_ref[1, f], (nz - 4 * x) % nz, 1), 0.0)
            add = add + jnp.where(lane >= nz - 2, pltpu.roll(az_ref[0, f], (nz - 2 - 4 * x) % nz, 1), 0.0)
            if x < 3:
                add = add + axr_ref[f, x]
            if x >= nx - 2:
                add = add + axl_ref[f, x - (nx - 2)]
            out_ref[f, x] = sec_ref[f, x] + SECTION * add
    live_n = cnt_ref[0]
    ndev, per = t_ref.shape
    own_ids = lax.broadcasted_iota(jnp.int32, (ndev, nz), 0)
    rank_ids = lax.broadcasted_iota(jnp.int32, (per, nz), 0)
    total = jnp.zeros((ndev, per), F32)
    for r in range(coef_ref.shape[1]):
        idx = row_ref[r]
        lx = idx // ny
        ly = idx % ny
        val = None
        for f in range(nf):
            v = out_ref[f, lx, pl.ds(ly, 1), :] * coef_ref[f, pl.ds(r, 1), :]
            val = v if val is None else val + v
        val = val * jnp.where(r < live_n, 1.0, 0.0).astype(F32)
        a = jnp.where(own_ref[pl.ds(r, 1), :] == own_ids, val, 0.0)
        b = jnp.where(rank_ref[pl.ds(r, 1), :] == rank_ids, 1.0, 0.0)
        total = total + lax.dot_general(a, b, (((1,), (1,)), ((), ())), precision=HI,
                                        preferred_element_type=F32)
    t_ref[...] = total


def on_device(ndev, adjoint, stencil_weights, flux_plus, flux_minus, wall_row, wall_panel, wall_coef,
              wall_count, panel_owner):
    nf, nx, ny, nz = adjoint.shape
    assert nx % XC == 0 and XC % 4 == 0 and ny == 16 and nx * 4 <= nz
    xf, yf, zf = pl.pallas_call(
        fronts_kernel,
        out_shape=(
            jax.ShapeDtypeStruct((nf, ny, nz), F32),
            jax.ShapeDtypeStruct((nf, nx, nz), F32),
            jax.ShapeDtypeStruct((nf, ny, nz), F32),
        ),
        in_specs=[VMEM],
        out_specs=(VMEM, VMEM, VMEM),
    )(adjoint)
    xf = shift_from(xf, "gx", -1)
    yf = shift_from(yf, "gy", -1)
    zf = shift_from(zf, "gz", -1)
    const4 = lambda i: (0, 0, 0, 0)
    last = nx // XC - 1
    const3 = lambda i: (0, 0, 0)
    sec, xl, xr, yl, yr, zz = pl.pallas_call(
        stencil_kernel,
        grid=(nx // XC + 1,),
        out_shape=(
            jax.ShapeDtypeStruct((nf, nx, ny, nz), F32),
            jax.ShapeDtypeStruct((nf, 2, ny, nz), F32),
            jax.ShapeDtypeStruct((nf, 3, ny, nz), F32),
            jax.ShapeDtypeStruct((nf, nx // 4, 8, nz), F32),
            jax.ShapeDtypeStruct((nf, nx // 2, 8, nz), F32),
            jax.ShapeDtypeStruct((2, nf, ny, nz), F32),
        ),
        in_specs=[
            SMEM,
            SMEM,
            pl.BlockSpec((nf, nx, ny, nz), const4),
            pl.BlockSpec((nf, ny, nz), const3),
            pl.BlockSpec((nf, nx, nz), const3),
            pl.BlockSpec((nf, ny, nz), const3),
            pl.BlockSpec((3, 2, 3, nf, XC, ny, nz), lambda i: (0, 0, 0, 0, jnp.minimum(i, last), 0, 0)),
        ],
        out_specs=(
            pl.BlockSpec((nf, XC, ny, nz), lambda i: (0, jnp.maximum(i - 1, 0), 0, 0)),
            pl.BlockSpec((nf, 2, ny, nz), const4),
            pl.BlockSpec((nf, 3, ny, nz), const4),
            pl.BlockSpec((nf, XC // 4, 8, nz), lambda i: (0, jnp.minimum(i, last), 0, 0)),
            pl.BlockSpec((nf, XC // 2, 8, nz), lambda i: (0, jnp.minimum(i, last), 0, 0)),
            pl.BlockSpec((2, nf, ny, nz), const4),
        ),
        scratch_shapes=[pltpu.VMEM((nf, nx + 5, ny, nz), F32)],
        compiler_params=pltpu.CompilerParams(dimension_semantics=("arbitrary",)),
    )(flux_plus, flux_minus, adjoint, xf, yf, zf, stencil_weights)
    axl = shift_from(xl, "gx", -1)
    axr = shift_from(xr, "gx", 1)
    ayl = shift_from(yl, "gy", -1)
    ayr = shift_from(yr, "gy", 1)
    if lax.axis_size("gz") == 2:
        az = shift_from(zz, "gz", 1)
    else:
        az = jnp.stack([shift_from(zz[0], "gz", -1), shift_from(zz[1], "gz", 1)])
    npan = panel_owner.shape[0]
    per = npan // ndev
    nb = 32
    na = npan // nb
    own_oh = (panel_owner[:, None] == jnp.arange(ndev, dtype=jnp.int32)).astype(F32)
    oh3 = own_oh.reshape(na, nb, ndev)
    below_b = (jnp.arange(nb)[None, :] < jnp.arange(nb)[:, None]).astype(F32)
    below_a = (jnp.arange(na)[None, :] < jnp.arange(na)[:, None]).astype(F32)
    inner = jnp.einsum("bc,acd->abd", below_b, oh3, precision=HI)
    before = jnp.einsum("ac,cd->ad", below_a, jnp.sum(oh3, axis=1), precision=HI)
    rank = jnp.sum((inner + before[:, None, :]) * oh3, axis=2)
    oh_a = (wall_panel[..., None] // nb == jnp.arange(na, dtype=jnp.int32)).astype(F32)
    oh_b = (wall_panel[..., None] % nb == jnp.arange(nb, dtype=jnp.int32)).astype(F32)

    def lookup(table):
        picked = jnp.einsum("rza,ab->rzb", oh_a, table, precision=HI) * oh_b
        return jnp.round(jnp.sum(picked, axis=2)).astype(jnp.int32)

    cell_own = lookup(panel_owner.reshape(na, nb).astype(F32))
    cell_rank = lookup(rank)
    nr = wall_row.shape[0]
    section, t = pl.pallas_call(
        fix_kernel,
        out_shape=(
            jax.ShapeDtypeStruct((nf, nx, ny, nz), F32),
            jax.ShapeDtypeStruct((ndev, per), F32),
        ),
        in_specs=[SMEM, SMEM] + [VMEM] * 9,
        out_specs=(VMEM, VMEM),
        input_output_aliases={2: 0},
    )(wall_row, wall_count, sec, axl, axr, ayl, ayr, az, wall_coef, cell_own, cell_rank)

    got = lax.all_to_all(t, AXES, 0, 0, tiled=True)
    return section, jnp.sum(got, axis=0)


def solution(mesh):
    ndev = mesh.size
    placed = (
        P(None, "gx", "gy", "gz"),
        P(None, None, None, None, "gx", "gy", "gz"),
        P(),
        P(),
        P(AXES),
        P(AXES, None),
        P(None, AXES, None),
        P(AXES),
        P(),
    )
    return jax.shard_map(
        lambda *args: on_device(ndev, *args),
        mesh=mesh,
        in_specs=placed,
        out_specs=(P(None, "gx", "gy", "gz"), P(AXES)),
        check_vma=False,
    )
```

```python
import jax
import jax.numpy as jnp
from jax import lax
from jax.experimental import pallas as pl
from jax.experimental.pallas import tpu as pltpu
from jax.sharding import PartitionSpec as P

AXES = ("gx", "gy", "gz")
STEP = 0.4
SECTION = 0.25
XC = 4
F32 = jnp.float32
HI = lax.Precision.HIGHEST
VMEM = pl.BlockSpec(memory_space=pltpu.VMEM)
SMEM = pl.BlockSpec(memory_space=pltpu.SMEM)


def shift_from(x, axis, by):
    n = lax.axis_size(axis)
    return lax.ppermute(x, axis, [(i, (i + by) % n) for i in range(n)])


def iotas(ny, nz):
    return (
        lax.broadcasted_iota(jnp.int32, (ny, nz), 0),
        lax.broadcasted_iota(jnp.int32, (ny, nz), 1),
    )


def fronts_kernel(adj_ref, xf_ref, yf_ref, zf_ref):
    nf, nx, ny, nz = adj_ref.shape
    row, lane = iotas(ny, nz)
    for f in range(nf):
        xf_ref[f] = adj_ref[f, 0]
        zacc = jnp.zeros((ny, nz), F32)
        for x in range(nx):
            s = adj_ref[f, x]
            yf_ref[f, pl.ds(x, 1), :] = s[0:1, :]
            zacc = zacc + pltpu.roll(jnp.where(lane == 0, s, 0.0), x, 1)
        zf_ref[f] = zacc


def offset_terms(plus, minus, w):
    p0, p1, p2 = plus * w(0, 0), plus * w(0, 1), plus * w(0, 2)
    m0, m1, m2 = minus * w(1, 0), minus * w(1, 1), minus * w(1, 2)
    a = p1 + m2
    b = p2 + m1
    return [
        p0 * (1.0 / 3.0),
        p0 * (-7.0 / 6.0) + a * (-1.0 / 6.0),
        p0 * (11.0 / 6.0) + a * (5.0 / 6.0) + b * (1.0 / 3.0),
        a * (1.0 / 3.0) + b * (5.0 / 6.0) + m0 * (11.0 / 6.0),
        b * (-1.0 / 6.0) + m0 * (-7.0 / 6.0),
        m0 * (1.0 / 3.0),
    ]


def rolled_sum(terms, n, axis):
    r = {o: pltpu.roll(terms[o], (o - 2) % n, axis) for o in (0, 1, 3, 4, 5)}
    tot = terms[2] + r[0] + r[1] + r[3] + r[4] + r[5]
    return r, tot


def split_rows(terms, row8, ny):
    r, tot = rolled_sum(terms, ny, 0)
    h = ny - 8
    wr = (jnp.where(row8 < 1, r[3][0:8], 0.0) + jnp.where(row8 < 2, r[4][0:8], 0.0)
          + jnp.where(row8 < 3, r[5][0:8], 0.0))
    wl = jnp.where(row8 >= 6, r[0][h:ny], 0.0) + jnp.where(row8 >= 7, r[1][h:ny], 0.0)
    inner = jnp.concatenate([tot[0:8] - wr, tot[8:h], tot[h:ny] - wl], 0) if h > 8 else \
        jnp.concatenate([tot[0:8] - wr, tot[h:ny] - wl], 0)
    return inner, wr, wl


def split_lanes(terms, lane, nz):
    r, tot = rolled_sum(terms, nz, 1)
    wr = jnp.where(lane < 1, r[3], 0.0) + jnp.where(lane < 2, r[4], 0.0) + jnp.where(lane < 3, r[5], 0.0)
    wl = jnp.where(lane >= nz - 2, r[0], 0.0) + jnp.where(lane >= nz - 1, r[1], 0.0)
    return tot - wr - wl, wr, wl


def stencil_kernel(fp_ref, fm_ref, adj_ref, xf_ref, yf_ref, zf_ref, w_ref,
                   sec_ref, xl_ref, xr_ref, yl_ref, yr_ref, zz_ref, acc_ref):
    nf, nx, ny, nz = adj_ref.shape
    i = pl.program_id(0)
    row, lane = iotas(ny, nz)
    row8 = lax.broadcasted_iota(jnp.int32, (8, nz), 0)

    @pl.when(i == 0)
    def _():
        acc_ref[...] = jnp.zeros_like(acc_ref)
        zz_ref[...] = jnp.zeros_like(zz_ref)

    def flux(d, diff):
        plus, minus = [], []
        for f in range(nf):
            p = m = None
            for g in range(nf):
                tp = diff[g] * (STEP * fp_ref[d, g, f])
                tm = diff[g] * (STEP * fm_ref[d, g, f])
                p = tp if p is None else p + tp
                m = tm if m is None else m + tm
            plus.append(p)
            minus.append(m)
        return plus, minus

    n = pl.num_programs(0) - 1

    @pl.when(i < n)
    def _():
        yr_parts = {}
        yl_parts = {}
        for xl in range(XC):
            x = i * XC + xl
            last = x == nx - 1
            nxt = jnp.minimum(x + 1, nx - 1)
            a = [adj_ref[f, x] for f in range(nf)]
            plus, minus = flux(0, [jnp.where(last, xf_ref[g], adj_ref[g, nxt]) - a[g] for g in range(nf)])
            for f in range(nf):
                sx = offset_terms(plus[f], minus[f], lambda s, k: w_ref[0, s, k, f, xl])
                for o in range(6):
                    acc_ref[f, x + o] = acc_ref[f, x + o] + sx[o]
            a = [adj_ref[f, x] for f in range(nf)]
            plus, minus = flux(1, [
                jnp.where(row == ny - 1, yf_ref[g, pl.ds(x, 1), :], pltpu.roll(a[g], ny - 1, 0)) - a[g]
                for g in range(nf)
            ])
            for f in range(nf):
                sy = offset_terms(plus[f], minus[f], lambda s, k: w_ref[1, s, k, f, xl])
                iy, wyr, wyl = split_rows(sy, row8, ny)
                acc_ref[f, x + 2] = acc_ref[f, x + 2] + iy
                rear = pltpu.roll(wyr, 4 * (xl % 2), 0)
                lead = pltpu.roll(wyl, (2 + 2 * (xl % 4)) % 8, 0)
                kr = (f, xl // 2)
                kl = (f, xl // 4)
                yr_parts[kr] = rear if kr not in yr_parts else yr_parts[kr] + rear
                yl_parts[kl] = lead if kl not in yl_parts else yl_parts[kl] + lead
            a = [adj_ref[f, x] for f in range(nf)]
            zshift = nz - 1 - x
            plus, minus = flux(2, [
                jnp.where(lane == nz - 1, pltpu.roll(zf_ref[g], zshift, 1), pltpu.roll(a[g], nz - 1, 1)) - a[g]
                for g in range(nf)
            ])
            for f in range(nf):
                sz = offset_terms(plus[f], minus[f], lambda s, k: w_ref[2, s, k, f, xl])
                iz, wzr, wzl = split_lanes(sz, lane, nz)
                acc_ref[f, x + 2] = acc_ref[f, x + 2] + iz
                zz_ref[0, f] = zz_ref[0, f] + pltpu.roll(wzl, 2 + 4 * x, 1)
                zz_ref[1, f] = zz_ref[1, f] + pltpu.roll(wzr, 4 * x, 1)
        for (f, t), v in yr_parts.items():
            yr_ref[f, t] = v
        for (f, t), v in yl_parts.items():
            yl_ref[f, t] = v

    @pl.when(i >= 1)
    def _():
        for xl in range(XC):
            x = (i - 1) * XC + xl
            for f in range(nf):
                sec_ref[f, xl] = SECTION * (adj_ref[f, x] + acc_ref[f, x + 2])

    @pl.when(i == n)
    def _():
        for f in range(nf):
            xl_ref[f] = acc_ref[f, 0:2]
            xr_ref[f] = acc_ref[f, nx + 2:nx + 5]


def fix_kernel(row_ref, cnt_ref, sec_ref, axl_ref, axr_ref, ayl_ref, ayr_ref, az_ref,
               coef_ref, own_ref, rank_ref, out_ref, t_ref):
    nf, nx, ny, nz = sec_ref.shape
    row, lane = iotas(ny, nz)
    pad = jnp.zeros((ny - 8, nz), F32)
    for x in range(nx):
        for f in range(nf):
            ty = jnp.concatenate([ayr_ref[f, x // 2], pad], 0)
            add = jnp.where(row < 3, pltpu.roll(ty, (ny - 4 * (x % 2)) % ny, 0), 0.0)
            ty = jnp.concatenate([ayl_ref[f, x // 4], pad], 0)
            add = add + jnp.where(row >= ny - 2, pltpu.roll(ty, (ny - 2 - 2 * (x % 4)) % ny, 0), 0.0)
            add = add + jnp.where(lane < 3, pltpu.roll(az_ref[1, f], (nz - 4 * x) % nz, 1), 0.0)
            add = add + jnp.where(lane >= nz - 2, pltpu.roll(az_ref[0, f], (nz - 2 - 4 * x) % nz, 1), 0.0)
            if x < 3:
                add = add + axr_ref[f, x]
            if x >= nx - 2:
                add = add + axl_ref[f, x - (nx - 2)]
            out_ref[f, x] = sec_ref[f, x] + SECTION * add
    live_n = cnt_ref[0]
    ndev, per = t_ref.shape
    own_ids = lax.broadcasted_iota(jnp.int32, (ndev, nz), 0)
    rank_ids = lax.broadcasted_iota(jnp.int32, (per, nz), 0)
    total = jnp.zeros((ndev, per), F32)
    for r in range(coef_ref.shape[1]):
        idx = row_ref[r]
        lx = idx // ny
        ly = idx % ny
        val = None
        for f in range(nf):
            v = out_ref[f, lx, pl.ds(ly, 1), :] * coef_ref[f, pl.ds(r, 1), :]
            val = v if val is None else val + v
        val = val * jnp.where(r < live_n, 1.0, 0.0).astype(F32)
        a = jnp.where(own_ref[pl.ds(r, 1), :] == own_ids, val, 0.0)
        b = jnp.where(rank_ref[pl.ds(r, 1), :] == rank_ids, 1.0, 0.0)
        total = total + lax.dot_general(a, b, (((1,), (1,)), ((), ())), precision=HI,
                                        preferred_element_type=F32)
    t_ref[...] = total


def on_device(ndev, adjoint, stencil_weights, flux_plus, flux_minus, wall_row, wall_panel, wall_coef,
              wall_count, panel_owner):
    nf, nx, ny, nz = adjoint.shape
    assert nx % XC == 0 and XC % 4 == 0 and ny == 16 and nx * 4 <= nz
    xf, yf, zf = pl.pallas_call(
        fronts_kernel,
        out_shape=(
            jax.ShapeDtypeStruct((nf, ny, nz), F32),
            jax.ShapeDtypeStruct((nf, nx, nz), F32),
            jax.ShapeDtypeStruct((nf, ny, nz), F32),
        ),
        in_specs=[VMEM],
        out_specs=(VMEM, VMEM, VMEM),
    )(adjoint)
    xf = shift_from(xf, "gx", -1)
    yf = shift_from(yf, "gy", -1)
    zf = shift_from(zf, "gz", -1)
    const4 = lambda i: (0, 0, 0, 0)
    last = nx // XC - 1
    const3 = lambda i: (0, 0, 0)
    sec, xl, xr, yl, yr, zz = pl.pallas_call(
        stencil_kernel,
        grid=(nx // XC + 1,),
        out_shape=(
            jax.ShapeDtypeStruct((nf, nx, ny, nz), F32),
            jax.ShapeDtypeStruct((nf, 2, ny, nz), F32),
            jax.ShapeDtypeStruct((nf, 3, ny, nz), F32),
            jax.ShapeDtypeStruct((nf, nx // 4, 8, nz), F32),
            jax.ShapeDtypeStruct((nf, nx // 2, 8, nz), F32),
            jax.ShapeDtypeStruct((2, nf, ny, nz), F32),
        ),
        in_specs=[
            SMEM,
            SMEM,
            pl.BlockSpec((nf, nx, ny, nz), const4),
            pl.BlockSpec((nf, ny, nz), const3),
            pl.BlockSpec((nf, nx, nz), const3),
            pl.BlockSpec((nf, ny, nz), const3),
            pl.BlockSpec((3, 2, 3, nf, XC, ny, nz), lambda i: (0, 0, 0, 0, jnp.minimum(i, last), 0, 0)),
        ],
        out_specs=(
            pl.BlockSpec((nf, XC, ny, nz), lambda i: (0, jnp.maximum(i - 1, 0), 0, 0)),
            pl.BlockSpec((nf, 2, ny, nz), const4),
            pl.BlockSpec((nf, 3, ny, nz), const4),
            pl.BlockSpec((nf, XC // 4, 8, nz), lambda i: (0, jnp.minimum(i, last), 0, 0)),
            pl.BlockSpec((nf, XC // 2, 8, nz), lambda i: (0, jnp.minimum(i, last), 0, 0)),
            pl.BlockSpec((2, nf, ny, nz), const4),
        ),
        scratch_shapes=[pltpu.VMEM((nf, nx + 5, ny, nz), F32)],
        compiler_params=pltpu.CompilerParams(dimension_semantics=("arbitrary",)),
    )(flux_plus, flux_minus, adjoint, xf, yf, zf, stencil_weights)
    axl = shift_from(xl, "gx", -1)
    axr = shift_from(xr, "gx", 1)
    ayl = shift_from(yl, "gy", -1)
    ayr = shift_from(yr, "gy", 1)
    if lax.axis_size("gz") == 2:
        az = shift_from(zz, "gz", 1)
    else:
        az = jnp.stack([shift_from(zz[0], "gz", -1), shift_from(zz[1], "gz", 1)])
    npan = panel_owner.shape[0]
    per = npan // ndev
    nb = 32
    na = npan // nb
    own_oh = (panel_owner[:, None] == jnp.arange(ndev, dtype=jnp.int32)).astype(F32)
    oh3 = own_oh.reshape(na, nb, ndev)
    below_b = (jnp.arange(nb)[None, :] < jnp.arange(nb)[:, None]).astype(F32)
    below_a = (jnp.arange(na)[None, :] < jnp.arange(na)[:, None]).astype(F32)
    inner = jnp.einsum("bc,acd->abd", below_b, oh3, precision=HI)
    before = jnp.einsum("ac,cd->ad", below_a, jnp.sum(oh3, axis=1), precision=HI)
    rank = jnp.sum((inner + before[:, None, :]) * oh3, axis=2)
    oh_a = (wall_panel[..., None] // nb == jnp.arange(na, dtype=jnp.int32)).astype(F32)
    oh_b = (wall_panel[..., None] % nb == jnp.arange(nb, dtype=jnp.int32)).astype(F32)

    def lookup(table):
        picked = jnp.einsum("rza,ab->rzb", oh_a, table, precision=HI) * oh_b
        return jnp.round(jnp.sum(picked, axis=2)).astype(jnp.int32)

    cell_own = lookup(panel_owner.reshape(na, nb).astype(F32))
    cell_rank = lookup(rank)
    nr = wall_row.shape[0]
    section, t = pl.pallas_call(
        fix_kernel,
        out_shape=(
            jax.ShapeDtypeStruct((nf, nx, ny, nz), F32),
            jax.ShapeDtypeStruct((ndev, per), F32),
        ),
        in_specs=[SMEM, SMEM] + [VMEM] * 9,
        out_specs=(VMEM, VMEM),
        input_output_aliases={2: 0},
        compiler_params=pltpu.CompilerParams(vmem_limit_bytes=16 * 1024 * 1024),
    )(wall_row, wall_count, sec, axl, axr, ayl, ayr, az, wall_coef, cell_own, cell_rank)

    got = lax.all_to_all(t, AXES, 0, 0, tiled=True)
    return section, jnp.sum(got, axis=0)


def solution(mesh):
    ndev = mesh.size
    placed = (
        P(None, "gx", "gy", "gz"),
        P(None, None, None, None, "gx", "gy", "gz"),
        P(),
        P(),
        P(AXES),
        P(AXES, None),
        P(None, AXES, None),
        P(AXES),
        P(),
    )
    return jax.shard_map(
        lambda *args: on_device(ndev, *args),
        mesh=mesh,
        in_specs=placed,
        out_specs=(P(None, "gx", "gy", "gz"), P(AXES)),
        check_vma=False,
    )
```

```python
import jax
import jax.numpy as jnp
from jax import lax
from jax.experimental import pallas as pl
from jax.experimental.pallas import tpu as pltpu
from jax.sharding import PartitionSpec as P

AXES = ("gx", "gy", "gz")
STEP = 0.4
SECTION = 0.25
XC = 4
F32 = jnp.float32
HI = lax.Precision.HIGHEST
VMEM = pl.BlockSpec(memory_space=pltpu.VMEM)
SMEM = pl.BlockSpec(memory_space=pltpu.SMEM)


def shift_from(x, axis, by):
    n = lax.axis_size(axis)
    return lax.ppermute(x, axis, [(i, (i + by) % n) for i in range(n)])


def iotas(ny, nz):
    return (
        lax.broadcasted_iota(jnp.int32, (ny, nz), 0),
        lax.broadcasted_iota(jnp.int32, (ny, nz), 1),
    )


def fronts_kernel(adj_ref, xf_ref, yf_ref, zf_ref):
    nf, nx, ny, nz = adj_ref.shape
    row, lane = iotas(ny, nz)
    for f in range(nf):
        xf_ref[f] = adj_ref[f, 0]
        zacc = jnp.zeros((ny, nz), F32)
        for x in range(nx):
            s = adj_ref[f, x]
            yf_ref[f, pl.ds(x, 1), :] = s[0:1, :]
            zacc = zacc + pltpu.roll(jnp.where(lane == 0, s, 0.0), x, 1)
        zf_ref[f] = zacc


def offset_terms(plus, minus, w):
    p0, p1, p2 = plus * w(0, 0), plus * w(0, 1), plus * w(0, 2)
    m0, m1, m2 = minus * w(1, 0), minus * w(1, 1), minus * w(1, 2)
    a = p1 + m2
    b = p2 + m1
    return [
        p0 * (1.0 / 3.0),
        p0 * (-7.0 / 6.0) + a * (-1.0 / 6.0),
        p0 * (11.0 / 6.0) + a * (5.0 / 6.0) + b * (1.0 / 3.0),
        a * (1.0 / 3.0) + b * (5.0 / 6.0) + m0 * (11.0 / 6.0),
        b * (-1.0 / 6.0) + m0 * (-7.0 / 6.0),
        m0 * (1.0 / 3.0),
    ]


def rolled_sum(terms, n, axis):
    r = {o: pltpu.roll(terms[o], (o - 2) % n, axis) for o in (0, 1, 3, 4, 5)}
    tot = terms[2] + r[0] + r[1] + r[3] + r[4] + r[5]
    return r, tot


def split_rows(terms, row8, ny):
    r, tot = rolled_sum(terms, ny, 0)
    h = ny - 8
    wr = (jnp.where(row8 < 1, r[3][0:8], 0.0) + jnp.where(row8 < 2, r[4][0:8], 0.0)
          + jnp.where(row8 < 3, r[5][0:8], 0.0))
    wl = jnp.where(row8 >= 6, r[0][h:ny], 0.0) + jnp.where(row8 >= 7, r[1][h:ny], 0.0)
    inner = jnp.concatenate([tot[0:8] - wr, tot[8:h], tot[h:ny] - wl], 0) if h > 8 else \
        jnp.concatenate([tot[0:8] - wr, tot[h:ny] - wl], 0)
    return inner, wr, wl


def split_lanes(terms, lane, nz):
    r, tot = rolled_sum(terms, nz, 1)
    wr = jnp.where(lane < 1, r[3], 0.0) + jnp.where(lane < 2, r[4], 0.0) + jnp.where(lane < 3, r[5], 0.0)
    wl = jnp.where(lane >= nz - 2, r[0], 0.0) + jnp.where(lane >= nz - 1, r[1], 0.0)
    return tot - wr - wl, wr, wl


def stencil_kernel(fp_ref, fm_ref, adj_ref, xf_ref, yf_ref, zf_ref, w_ref,
                   sec_ref, xl_ref, xr_ref, yl_ref, yr_ref, zz_ref, acc_ref):
    nf, nx, ny, nz = adj_ref.shape
    i = pl.program_id(0)
    row, lane = iotas(ny, nz)
    row8 = lax.broadcasted_iota(jnp.int32, (8, nz), 0)

    @pl.when(i == 0)
    def _():
        acc_ref[...] = jnp.zeros_like(acc_ref)
        zz_ref[...] = jnp.zeros_like(zz_ref)

    def flux(d, diff):
        plus, minus = [], []
        for f in range(nf):
            p = m = None
            for g in range(nf):
                tp = diff[g] * (STEP * fp_ref[d, g, f])
                tm = diff[g] * (STEP * fm_ref[d, g, f])
                p = tp if p is None else p + tp
                m = tm if m is None else m + tm
            plus.append(p)
            minus.append(m)
        return plus, minus

    n = pl.num_programs(0) - 1

    @pl.when(i < n)
    def _():
        yr_parts = {}
        yl_parts = {}
        for xl in range(XC):
            x = i * XC + xl
            last = x == nx - 1
            nxt = jnp.minimum(x + 1, nx - 1)
            a = [adj_ref[f, x] for f in range(nf)]
            plus, minus = flux(0, [jnp.where(last, xf_ref[g], adj_ref[g, nxt]) - a[g] for g in range(nf)])
            for f in range(nf):
                sx = offset_terms(plus[f], minus[f], lambda s, k: w_ref[0, s, k, f, xl])
                for o in range(6):
                    acc_ref[f, x + o] = acc_ref[f, x + o] + sx[o]
            a = [adj_ref[f, x] for f in range(nf)]
            plus, minus = flux(1, [
                jnp.where(row == ny - 1, yf_ref[g, pl.ds(x, 1), :], pltpu.roll(a[g], ny - 1, 0)) - a[g]
                for g in range(nf)
            ])
            for f in range(nf):
                sy = offset_terms(plus[f], minus[f], lambda s, k: w_ref[1, s, k, f, xl])
                iy, wyr, wyl = split_rows(sy, row8, ny)
                acc_ref[f, x + 2] = acc_ref[f, x + 2] + iy
                rear = pltpu.roll(wyr, 4 * (xl % 2), 0)
                lead = pltpu.roll(wyl, (2 + 2 * (xl % 4)) % 8, 0)
                kr = (f, xl // 2)
                kl = (f, xl // 4)
                yr_parts[kr] = rear if kr not in yr_parts else yr_parts[kr] + rear
                yl_parts[kl] = lead if kl not in yl_parts else yl_parts[kl] + lead
            a = [adj_ref[f, x] for f in range(nf)]
            zshift = nz - 1 - x
            plus, minus = flux(2, [
                jnp.where(lane == nz - 1, pltpu.roll(zf_ref[g], zshift, 1), pltpu.roll(a[g], nz - 1, 1)) - a[g]
                for g in range(nf)
            ])
            for f in range(nf):
                sz = offset_terms(plus[f], minus[f], lambda s, k: w_ref[2, s, k, f, xl])
                iz, wzr, wzl = split_lanes(sz, lane, nz)
                acc_ref[f, x + 2] = acc_ref[f, x + 2] + iz
                zz_ref[0, f] = zz_ref[0, f] + pltpu.roll(wzl, 2 + 4 * x, 1)
                zz_ref[1, f] = zz_ref[1, f] + pltpu.roll(wzr, 4 * x, 1)
        for (f, t), v in yr_parts.items():
            yr_ref[f, t] = v
        for (f, t), v in yl_parts.items():
            yl_ref[f, t] = v

    @pl.when(i >= 1)
    def _():
        for xl in range(XC):
            x = (i - 1) * XC + xl
            for f in range(nf):
                sec_ref[f, xl] = SECTION * (adj_ref[f, x] + acc_ref[f, x + 2])

    @pl.when(i == n)
    def _():
        for f in range(nf):
            xl_ref[f] = acc_ref[f, 0:2]
            xr_ref[f] = acc_ref[f, nx + 2:nx + 5]


def fix_kernel(row_ref, cnt_ref, sec_ref, axl_ref, axr_ref, ayl_ref, ayr_ref, az_ref,
               coef_ref, own_ref, rank_ref, out_ref, t_ref):
    nf, nx, ny, nz = sec_ref.shape
    row, lane = iotas(ny, nz)
    pad = jnp.zeros((ny - 8, nz), F32)
    for x in range(nx):
        for f in range(nf):
            ty = jnp.concatenate([ayr_ref[f, x // 2], pad], 0)
            add = jnp.where(row < 3, pltpu.roll(ty, (ny - 4 * (x % 2)) % ny, 0), 0.0)
            ty = jnp.concatenate([ayl_ref[f, x // 4], pad], 0)
            add = add + jnp.where(row >= ny - 2, pltpu.roll(ty, (ny - 2 - 2 * (x % 4)) % ny, 0), 0.0)
            add = add + jnp.where(lane < 3, pltpu.roll(az_ref[1, f], (nz - 4 * x) % nz, 1), 0.0)
            add = add + jnp.where(lane >= nz - 2, pltpu.roll(az_ref[0, f], (nz - 2 - 4 * x) % nz, 1), 0.0)
            if x < 3:
                add = add + axr_ref[f, x]
            if x >= nx - 2:
                add = add + axl_ref[f, x - (nx - 2)]
            out_ref[f, x] = sec_ref[f, x] + SECTION * add
    live_n = cnt_ref[0]
    ndev, per = t_ref.shape
    own_ids = lax.broadcasted_iota(jnp.int32, (ndev, nz), 0)
    rank_ids = lax.broadcasted_iota(jnp.int32, (per, nz), 0)
    total = jnp.zeros((ndev, per), F32)
    for r in range(coef_ref.shape[1]):
        idx = row_ref[r]
        lx = idx // ny
        ly = idx % ny
        val = None
        for f in range(nf):
            v = out_ref[f, lx, pl.ds(ly, 1), :] * coef_ref[f, pl.ds(r, 1), :]
            val = v if val is None else val + v
        val = val * jnp.where(r < live_n, 1.0, 0.0).astype(F32)
        a = jnp.where(own_ref[pl.ds(r, 1), :] == own_ids, val, 0.0)
        b = jnp.where(rank_ref[pl.ds(r, 1), :] == rank_ids, 1.0, 0.0)
        total = total + lax.dot_general(a, b, (((1,), (1,)), ((), ())), precision=HI,
                                        preferred_element_type=F32)
    t_ref[...] = total


def on_device(ndev, adjoint, stencil_weights, flux_plus, flux_minus, wall_row, wall_panel, wall_coef,
              wall_count, panel_owner):
    nf, nx, ny, nz = adjoint.shape
    assert nx % XC == 0 and XC % 4 == 0 and ny == 16 and nx * 4 <= nz
    xf, yf, zf = pl.pallas_call(
        fronts_kernel,
        out_shape=(
            jax.ShapeDtypeStruct((nf, ny, nz), F32),
            jax.ShapeDtypeStruct((nf, nx, nz), F32),
            jax.ShapeDtypeStruct((nf, ny, nz), F32),
        ),
        in_specs=[VMEM],
        out_specs=(VMEM, VMEM, VMEM),
    )(adjoint)
    xf = shift_from(xf, "gx", -1)
    yf = shift_from(yf, "gy", -1)
    zf = shift_from(zf, "gz", -1)
    const4 = lambda i: (0, 0, 0, 0)
    last = nx // XC - 1
    const3 = lambda i: (0, 0, 0)
    sec, xl, xr, yl, yr, zz = pl.pallas_call(
        stencil_kernel,
        grid=(nx // XC + 1,),
        out_shape=(
            jax.ShapeDtypeStruct((nf, nx, ny, nz), F32),
            jax.ShapeDtypeStruct((nf, 2, ny, nz), F32),
            jax.ShapeDtypeStruct((nf, 3, ny, nz), F32),
            jax.ShapeDtypeStruct((nf, nx // 4, 8, nz), F32),
            jax.ShapeDtypeStruct((nf, nx // 2, 8, nz), F32),
            jax.ShapeDtypeStruct((2, nf, ny, nz), F32),
        ),
        in_specs=[
            SMEM,
            SMEM,
            pl.BlockSpec((nf, nx, ny, nz), const4),
            pl.BlockSpec((nf, ny, nz), const3),
            pl.BlockSpec((nf, nx, nz), const3),
            pl.BlockSpec((nf, ny, nz), const3),
            pl.BlockSpec((3, 2, 3, nf, XC, ny, nz), lambda i: (0, 0, 0, 0, jnp.minimum(i, last), 0, 0)),
        ],
        out_specs=(
            pl.BlockSpec((nf, XC, ny, nz), lambda i: (0, jnp.maximum(i - 1, 0), 0, 0)),
            pl.BlockSpec((nf, 2, ny, nz), const4),
            pl.BlockSpec((nf, 3, ny, nz), const4),
            pl.BlockSpec((nf, XC // 4, 8, nz), lambda i: (0, jnp.minimum(i, last), 0, 0)),
            pl.BlockSpec((nf, XC // 2, 8, nz), lambda i: (0, jnp.minimum(i, last), 0, 0)),
            pl.BlockSpec((2, nf, ny, nz), const4),
        ),
        scratch_shapes=[pltpu.VMEM((nf, nx + 5, ny, nz), F32)],
        compiler_params=pltpu.CompilerParams(
            dimension_semantics=("arbitrary",), vmem_limit_bytes=48 * 1024 * 1024
        ),
    )(flux_plus, flux_minus, adjoint, xf, yf, zf, stencil_weights)
    axl = shift_from(xl, "gx", -1)
    axr = shift_from(xr, "gx", 1)
    ayl = shift_from(yl, "gy", -1)
    ayr = shift_from(yr, "gy", 1)
    if lax.axis_size("gz") == 2:
        az = shift_from(zz, "gz", 1)
    else:
        az = jnp.stack([shift_from(zz[0], "gz", -1), shift_from(zz[1], "gz", 1)])
    npan = panel_owner.shape[0]
    per = npan // ndev
    nb = 32
    na = npan // nb
    own_oh = (panel_owner[:, None] == jnp.arange(ndev, dtype=jnp.int32)).astype(F32)
    oh3 = own_oh.reshape(na, nb, ndev)
    below_b = (jnp.arange(nb)[None, :] < jnp.arange(nb)[:, None]).astype(F32)
    below_a = (jnp.arange(na)[None, :] < jnp.arange(na)[:, None]).astype(F32)
    inner = jnp.einsum("bc,acd->abd", below_b, oh3, precision=HI)
    before = jnp.einsum("ac,cd->ad", below_a, jnp.sum(oh3, axis=1), precision=HI)
    rank = jnp.sum((inner + before[:, None, :]) * oh3, axis=2)
    oh_a = (wall_panel[..., None] // nb == jnp.arange(na, dtype=jnp.int32)).astype(F32)
    oh_b = (wall_panel[..., None] % nb == jnp.arange(nb, dtype=jnp.int32)).astype(F32)

    def lookup(table):
        picked = jnp.einsum("rza,ab->rzb", oh_a, table, precision=HI) * oh_b
        return jnp.round(jnp.sum(picked, axis=2)).astype(jnp.int32)

    cell_own = lookup(panel_owner.reshape(na, nb).astype(F32))
    cell_rank = lookup(rank)
    nr = wall_row.shape[0]
    section, t = pl.pallas_call(
        fix_kernel,
        out_shape=(
            jax.ShapeDtypeStruct((nf, nx, ny, nz), F32),
            jax.ShapeDtypeStruct((ndev, per), F32),
        ),
        in_specs=[SMEM, SMEM] + [VMEM] * 9,
        out_specs=(VMEM, VMEM),
        input_output_aliases={2: 0},
        compiler_params=pltpu.CompilerParams(vmem_limit_bytes=16 * 1024 * 1024),
    )(wall_row, wall_count, sec, axl, axr, ayl, ayr, az, wall_coef, cell_own, cell_rank)

    got = lax.all_to_all(t, AXES, 0, 0, tiled=True)
    return section, jnp.sum(got, axis=0)


def solution(mesh):
    ndev = mesh.size
    placed = (
        P(None, "gx", "gy", "gz"),
        P(None, None, None, None, "gx", "gy", "gz"),
        P(),
        P(),
        P(AXES),
        P(AXES, None),
        P(None, AXES, None),
        P(AXES),
        P(),
    )
    return jax.shard_map(
        lambda *args: on_device(ndev, *args),
        mesh=mesh,
        in_specs=placed,
        out_specs=(P(None, "gx", "gy", "gz"), P(AXES)),
        check_vma=False,
    )
```
